32 devices in a mesh: sky: 8 (over z, y), los: 4 (over x, core).
Axes of the slice: x: 2, y: 2, z: 4, core: 2. Of those that a mesh axis runs over, the one named last changes fastest.
Arguments:
- features: bfloat16 [32, 16, 32, 128], P(None, 'sky', 'los'), may hold values from -6 to 6
- pre_first: bfloat16 [32, 16, 32, 128], P(None, 'sky', 'los'), may hold values from -8 to 8
- pre_second: bfloat16 [32, 16, 32, 128], P(None, 'sky', 'los'), may hold values from -8 to 8
- w_first: bfloat16 [3, 3, 3, 32, 32], replicated, may hold values from -0.21875 to 0.21875
- w_second: bfloat16 [3, 3, 3, 32, 32], replicated, may hold values from -0.21875 to 0.21875
- w_out: bfloat16 [3, 32], replicated, may hold values from -1 to 1
- b_out: float32 [3], replicated, may hold values from -1 to 1
- y_target: float32 [16, 128], P('sky'), may hold values from -6 to 6
- k_target: float32 [16, 128], P('sky'), may hold values from -6 to 6
Outputs:
- grad_features: bfloat16 [32, 16, 32, 128], P(None, 'sky', 'los')
- grad_first: float32 [3, 3, 3, 32, 32], replicated
- grad_second: float32 [3, 3, 3, 32, 32], replicated
- grad_out: float32 [3, 32], replicated
- grad_bias: float32 [3], replicated
The draws below stay inside these ranges and needn't reach their ends.
All inputs are finite; a program needn't handle non-finite values.
Results may differ from the reference program's by a relative error of at most 0.0067.
Values may be sent and summed in bfloat16 or wider, within the bound.
No kernel may reach another device: no remote copies, remote signals or barrier semaphores. Data moves between devices by JAX's collectives and lax.ppermute only.
A program may use at most 64 MiB of HBM per device.

```python
import math
import jax
import jax.numpy as jnp
from jax import lax

C = 32
NX = 16
NZ = 32
NY = 128


def wave_numbers(key, extent):
    lowest = max(1, extent // 4)
    highest = max(lowest + 1, extent // 3 + 1)
    counts = jax.random.randint(jax.random.fold_in(key, 1), (6,), lowest, highest, dtype=jnp.int32)
    flips = jax.random.randint(jax.random.fold_in(key, 2), (6,), 0, 2, dtype=jnp.int32)
    return jnp.where(flips == 1, extent - counts, counts)


def shared_field(key):
    mode_total = 6
    waves_x = wave_numbers(jax.random.fold_in(key, 11), NX)
    waves_z = wave_numbers(jax.random.fold_in(key, 12), NZ)
    waves_y = wave_numbers(jax.random.fold_in(key, 13), NY)
    coord_x = jnp.arange(NX, dtype=jnp.int32)[:, None, None]
    coord_z = jnp.arange(NZ, dtype=jnp.int32)[None, :, None]
    coord_y = jnp.arange(NY, dtype=jnp.int32)[None, None, :]
    cell_total = NX * NZ * NY
    offsets = jax.random.uniform(jax.random.fold_in(key, 14), (C, mode_total), jnp.float32, 0.0, 2.0 * math.pi)
    mode_scale = math.sqrt(2.0 / mode_total)
    amplitude = jax.random.normal(jax.random.fold_in(key, 15), (C, mode_total), jnp.float32) * mode_scale
    rough_part = 0.8 * jax.random.normal(jax.random.fold_in(key, 16), (C, NX, NZ, NY), jnp.float32)
    smooth_part = jnp.zeros((C, NX, NZ, NY), jnp.float32)
    for mode_index in range(mode_total):
        term_x = waves_x[mode_index] * coord_x % NX * (NZ * NY)
        term_z = waves_z[mode_index] * coord_z % NZ * (NX * NY)
        term_y = waves_y[mode_index] * coord_y % NY * (NX * NZ)
        numer = (term_x + term_z + term_y) % cell_total
        angle = numer.astype(jnp.float32) * (2.0 * math.pi / cell_total)
        smooth_part = smooth_part + amplitude[:, mode_index, None, None, None] * jnp.cos(angle[None] + offsets[:, mode_index, None, None, None])
    return smooth_part + rough_part


def draw_pre_first(key, part):
    return jnp.clip(shared_field(key), -8.0, 8.0).astype(jnp.bfloat16)


def draw_pre_second(key, part):
    base_field = shared_field(key)
    noise_part = 0.8 * jax.random.normal(jax.random.fold_in(key, 21), base_field.shape, jnp.float32)
    return jnp.clip(base_field + noise_part, -8.0, 8.0).astype(jnp.bfloat16)


def shard_levels(rng, dims, pieces, least, largest):
    def one(dim, parts):
        draws = jax.random.uniform(jax.random.fold_in(jax.random.fold_in(rng, 6), dim), (parts,), jnp.float32, least / len(pieces), largest / len(pieces))
        return jnp.repeat(jnp.exp(draws), dims[dim] // parts).reshape((-1,) + (1,) * (len(dims) - dim - 1))

    loudness = one(*pieces[0])
    for cut in pieces[1:]:
        loudness = loudness * one(*cut)
    return loudness


def normal_values(own_key, shape, scale, reach, split=(), held_as=jnp.bfloat16):
    gain = shard_levels(own_key, shape, split, -0.22, 0.18) if split else 1.0
    array = jax.random.normal(own_key, shape, jnp.float32) * scale * gain
    return jnp.minimum(jnp.maximum(array, -reach), reach).astype(held_as)


def setup_inputs(seed: int = 0) -> dict:
    arg_keys = jax.random.split(jax.random.key(seed), 10)
    return {
        "features": normal_values(arg_keys[0], (C, NX, NZ, NY), 1.0, 6.0, ((1, 8), (2, 4))),
        "pre_first": draw_pre_first(jax.random.fold_in(arg_keys[9], 71), 0),
        "pre_second": draw_pre_second(jax.random.fold_in(arg_keys[9], 71), 0),
        "w_first": normal_values(arg_keys[3], (3, 3, 3, C, C), (27 * C) ** -0.5, 0.21875),
        "w_second": normal_values(arg_keys[4], (3, 3, 3, C, C), (27 * C) ** -0.5, 0.21875),
        "w_out": normal_values(arg_keys[5], (3, C), C ** -0.5, 1.0),
        "b_out": jnp.clip(jax.random.uniform(arg_keys[6], (3,), jnp.float32, -1.0, 1.0), -1.0, 1.0),
        "y_target": normal_values(arg_keys[7], (NX, NY), 1.0, 6.0, ((0, 8),), jnp.float32),
        "k_target": normal_values(arg_keys[8], (NX, NY), 1.0, 6.0, ((0, 8),), jnp.float32),
    }


def wrapped(field):
    return jnp.pad(field, ((0, 0), (1, 1), (1, 1), (1, 1)), mode='wrap')

def silu_slope(value):
    sigma = jax.nn.sigmoid(value)
    return sigma * (1.0 + value * (1.0 - sigma))

def spread(weight, grad_field):
    padded = wrapped(grad_field.astype(jnp.float32))
    extent_x, extent_z, extent_y = (grad_field.shape[1], grad_field.shape[2], grad_field.shape[3])
    result = jnp.zeros(grad_field.shape, jnp.float32)
    for tap_x in range(3):
        for tap_z in range(3):
            for tap_y in range(3):
                window = padded[:, 2 - tap_x:2 - tap_x + extent_x, 2 - tap_z:2 - tap_z + extent_z, 2 - tap_y:2 - tap_y + extent_y]
                result = result + jnp.einsum('oi,oxzy->ixzy', weight[tap_x, tap_z, tap_y].astype(jnp.float32), window)
    return result

def weight_grad(grad_field, inputs):
    padded = wrapped(inputs.astype(jnp.float32))
    grad_wide = grad_field.astype(jnp.float32)
    extent_x, extent_z, extent_y = (grad_field.shape[1], grad_field.shape[2], grad_field.shape[3])
    taps_list = []
    for tap_x in range(3):
        for tap_z in range(3):
            for tap_y in range(3):
                window = padded[:, tap_x:tap_x + extent_x, tap_z:tap_z + extent_z, tap_y:tap_y + extent_y]
                taps_list.append(jnp.einsum('oxzy,ixzy->oi', grad_wide, window))
    channels = grad_field.shape[0]
    return jnp.stack(taps_list).reshape(3, 3, 3, channels, inputs.shape[0])

def reference(features, pre_first, pre_second, w_first, w_second, w_out, b_out, y_target, k_target):
    norm_factor = 1.0 / math.sqrt(NX * NY * NZ)
    first_wide = pre_first.astype(jnp.float32)
    second_wide = pre_second.astype(jnp.float32)
    hidden_first = jax.nn.silu(first_wide).astype(jnp.bfloat16)
    hidden_second = jax.nn.silu(second_wide).astype(jnp.bfloat16)
    heads_raw = jnp.einsum('oi,ixzy->oxzy', w_out.astype(jnp.float32), hidden_second.astype(jnp.float32))
    heads_raw = heads_raw + b_out[:, None, None, None]
    pressure = jax.nn.softplus(heads_raw[0])
    density = jax.nn.softplus(heads_raw[1])
    velocity = heads_raw[2]
    y_map = lax.optimization_barrier(jnp.sum(pressure, axis=1)) / NZ
    k_map = -lax.optimization_barrier(jnp.sum(density * velocity, axis=1)) / NZ
    y_resid = (y_map - y_target)[:, None, :]
    k_resid = (k_map - k_target)[:, None, :]
    head_grad = jnp.stack((y_resid * jax.nn.sigmoid(heads_raw[0]), -k_resid * velocity * jax.nn.sigmoid(heads_raw[1]), -k_resid * density)).astype(jnp.bfloat16)
    head_wide = head_grad.astype(jnp.float32)
    grad_out = jnp.einsum('oxzy,ixzy->oi', head_wide, hidden_second.astype(jnp.float32)) * norm_factor
    grad_bias = lax.optimization_barrier(jnp.sum(head_wide, axis=(1, 2, 3))) * norm_factor
    back_second = jnp.einsum('oi,oxzy->ixzy', w_out.astype(jnp.float32), head_wide)
    grad_second_pre = (back_second * silu_slope(second_wide)).astype(jnp.bfloat16)
    back_first = spread(w_second, grad_second_pre)
    grad_first_pre = (back_first * silu_slope(first_wide)).astype(jnp.bfloat16)
    grad_second = weight_grad(grad_second_pre, hidden_first) * norm_factor
    grad_first = weight_grad(grad_first_pre, features) * norm_factor
    grad_features = spread(w_first, grad_first_pre).astype(jnp.bfloat16)
    return (grad_features, grad_first, grad_second, grad_out, grad_bias)
```

```python
import math

import jax
import jax.numpy as jnp
from jax import lax
from jax.sharding import PartitionSpec as P


def extended(block, sides, width):
    for axis, dim in sides:
        count = lax.axis_size(axis)
        forward = [(i, i + 1) for i in range(count - 1)]
        forward.append((count - 1, 0))
        backward = [(target, source) for source, target in forward]
        low = lax.ppermute(
            lax.slice_in_dim(block, block.shape[dim] - width, None, axis=dim), axis, forward
        )
        high = lax.ppermute(lax.slice_in_dim(block, 0, width, axis=dim), axis, backward)
        block = jnp.concatenate([low, block, high], axis=dim)
    return block


def butterfly_sum(value, axes):
    for axis in axes:
        count = lax.axis_size(axis)
        if count & (count - 1):
            value = lax.psum(value, axis)
            continue
        step = 1
        while step < count:
            pairs = [(i, i ^ step) for i in range(count)]
            value = value + lax.ppermute(value, axis, pairs)
            step *= 2
    return value


def pack_rows(parts):
    flat = jnp.concatenate([part.reshape(-1) for part in parts])
    rows = -(-flat.shape[0] // 128)
    flat = jnp.pad(flat, (0, rows * 128 - flat.shape[0]))
    return flat.reshape(rows, 128)


def unpack_rows(packed, shapes):
    flat = packed.reshape(-1)
    parts = []
    start = 0
    for shape in shapes:
        size = math.prod(shape)
        parts.append(flat[start : start + size].reshape(shape))
        start += size
    return parts


def silu_slope(value):
    sigma = jax.nn.sigmoid(value)
    return sigma * (1.0 + value * (1.0 - sigma))


def wrap_columns(field):
    return jnp.concatenate((field[..., -1:], field, field[..., :1]), axis=-1)


def spread_local(weight, padded, shape):
    result = jnp.zeros(shape, jnp.float32)
    for tap_x in range(3):
        for tap_z in range(3):
            for tap_y in range(3):
                window = padded[
                    :,
                    2 - tap_x : 2 - tap_x + shape[1],
                    2 - tap_z : 2 - tap_z + shape[2],
                    2 - tap_y : 2 - tap_y + shape[3],
                ]
                result = result + jnp.einsum(
                    "oi,oxzy->ixzy",
                    weight[tap_x, tap_z, tap_y],
                    window,
                    preferred_element_type=jnp.float32,
                )
    return result


def taps_from_inputs(grad_field, padded_inputs):
    shape = grad_field.shape
    taps_list = []
    for tap_x in range(3):
        for tap_z in range(3):
            for tap_y in range(3):
                window = padded_inputs[
                    :, tap_x : tap_x + shape[1], tap_z : tap_z + shape[2], tap_y : tap_y + shape[3]
                ]
                taps_list.append(
                    jnp.einsum(
                        "oxzy,ixzy->oi", grad_field, window, preferred_element_type=jnp.float32
                    )
                )
    return jnp.stack(taps_list).reshape(3, 3, 3, shape[0], padded_inputs.shape[0])


def per_device(
    features, pre_first, pre_second, w_first, w_second, w_out, b_out, y_target, k_target
):
    count_sky = lax.axis_size("sky")
    count_los = lax.axis_size("los")
    depth_all = pre_first.shape[2] * count_los
    norm_factor = 1.0 / math.sqrt(features.shape[1] * count_sky * features.shape[3] * depth_all)
    shape = features.shape
    first_wide = pre_first.astype(jnp.float32)
    second_wide = pre_second.astype(jnp.float32)
    hidden_second = jax.nn.silu(second_wide).astype(jnp.bfloat16)
    heads_raw = jnp.einsum(
        "oi,ixzy->oxzy", w_out, hidden_second, preferred_element_type=jnp.float32
    )
    heads_raw = heads_raw + b_out[:, None, None, None]
    pressure = jax.nn.softplus(heads_raw[0])
    density = jax.nn.softplus(heads_raw[1])
    velocity = heads_raw[2]
    y_part = jnp.sum(pressure, axis=1) / depth_all
    k_part = -jnp.sum(density * velocity, axis=1) / depth_all
    y_map, k_map = butterfly_sum(jnp.stack((y_part, k_part)), ("los",))
    y_resid = y_map - y_target
    k_resid = k_map - k_target
    y_resid = y_resid[:, None, :]
    k_resid = k_resid[:, None, :]
    head_grad = jnp.stack(
        (
            y_resid * jax.nn.sigmoid(heads_raw[0]),
            -k_resid * velocity * jax.nn.sigmoid(heads_raw[1]),
            -k_resid * density,
        )
    ).astype(jnp.bfloat16)
    grad_out = (
        jnp.einsum("oxzy,ixzy->oi", head_grad, hidden_second, preferred_element_type=jnp.float32)
        * norm_factor
    )
    grad_bias = jnp.sum(head_grad.astype(jnp.float32), axis=(1, 2, 3)) * norm_factor
    back_second = jnp.einsum("oi,oxzy->ixzy", w_out, head_grad, preferred_element_type=jnp.float32)
    grad_second_pre = (back_second * silu_slope(second_wide)).astype(jnp.bfloat16)
    second_padded = wrap_columns(extended(grad_second_pre, (("sky", 1), ("los", 2)), 1))
    back_first = spread_local(w_second, second_padded, shape)
    grad_first_pre = (back_first * silu_slope(first_wide)).astype(jnp.bfloat16)
    first_padded = wrap_columns(extended(grad_first_pre, (("sky", 1), ("los", 2)), 1))
    grad_features = spread_local(w_first, first_padded, shape).astype(jnp.bfloat16)
    saved_padded = wrap_columns(
        extended(jnp.stack((features, pre_first)), (("sky", 2), ("los", 3)), 1)
    )
    hidden_padded = jax.nn.silu(saved_padded[1].astype(jnp.float32)).astype(jnp.bfloat16)
    grad_second = taps_from_inputs(grad_second_pre, hidden_padded)
    grad_first = taps_from_inputs(grad_first_pre, saved_padded[0])
    early = (grad_second * norm_factor, grad_out, grad_bias)
    early_shapes = [part.shape for part in early]
    grad_second, grad_out, grad_bias = unpack_rows(
        butterfly_sum(pack_rows(early), ("los", "sky")), early_shapes
    )
    grad_first = butterfly_sum(grad_first * norm_factor, ("los", "sky"))
    return (grad_features, grad_first, grad_second, grad_out, grad_bias)


def solution(mesh):
    in_specs = (
        P(None, "sky", "los", None),
        P(None, "sky", "los", None),
        P(None, "sky", "los", None),
        P(),
        P(),
        P(),
        P(),
        P("sky", None),
        P("sky", None),
    )
    out_specs = (P(None, "sky", "los", None), P(), P(), P(), P())
    return jax.shard_map(
        per_device, mesh=mesh, in_specs=in_specs, out_specs=out_specs, check_vma=False
    )
```

```python
import math

import jax
import jax.numpy as jnp
from jax import lax
from jax.sharding import PartitionSpec as P


def extended(block, sides, width):
    for axis, dim in sides:
        count = lax.axis_size(axis)
        forward = [(i, i + 1) for i in range(count - 1)]
        forward.append((count - 1, 0))
        backward = [(target, source) for source, target in forward]
        low = lax.ppermute(
            lax.slice_in_dim(block, block.shape[dim] - width, None, axis=dim), axis, forward
        )
        high = lax.ppermute(lax.slice_in_dim(block, 0, width, axis=dim), axis, backward)
        block = jnp.concatenate([low, block, high], axis=dim)
    return block


def butterfly_sum(value, axes):
    for axis in axes:
        count = lax.axis_size(axis)
        if count & (count - 1):
            value = lax.psum(value, axis)
            continue
        step = 1
        while step < count:
            pairs = [(i, i ^ step) for i in range(count)]
            value = value + lax.ppermute(value, axis, pairs)
            step *= 2
    return value


def pack_rows(parts):
    flat = jnp.concatenate([part.reshape(-1) for part in parts])
    rows = -(-flat.shape[0] // 128)
    flat = jnp.pad(flat, (0, rows * 128 - flat.shape[0]))
    return flat.reshape(rows, 128)


def unpack_rows(packed, shapes):
    flat = packed.reshape(-1)
    parts = []
    start = 0
    for shape in shapes:
        size = math.prod(shape)
        parts.append(flat[start : start + size].reshape(shape))
        start += size
    return parts


def silu_slope(value):
    sigma = jax.nn.sigmoid(value)
    return sigma * (1.0 + value * (1.0 - sigma))


def wrap_columns(field):
    return jnp.concatenate((field[..., -1:], field, field[..., :1]), axis=-1)


def spread_local(weight, padded, shape):
    result = jnp.zeros(shape, jnp.float32)
    for tap_x in range(3):
        for tap_z in range(3):
            for tap_y in range(3):
                window = padded[
                    :,
                    2 - tap_x : 2 - tap_x + shape[1],
                    2 - tap_z : 2 - tap_z + shape[2],
                    2 - tap_y : 2 - tap_y + shape[3],
                ]
                result = result + jnp.einsum(
                    "oi,oxzy->ixzy",
                    weight[tap_x, tap_z, tap_y],
                    window,
                    preferred_element_type=jnp.float32,
                )
    return result


def taps_from_inputs(grad_field, padded_inputs):
    shape = grad_field.shape
    taps_list = []
    for tap_x in range(3):
        for tap_z in range(3):
            for tap_y in range(3):
                window = padded_inputs[
                    :, tap_x : tap_x + shape[1], tap_z : tap_z + shape[2], tap_y : tap_y + shape[3]
                ]
                taps_list.append(
                    jnp.einsum(
                        "oxzy,ixzy->oi", grad_field, window, preferred_element_type=jnp.float32
                    )
                )
    return jnp.stack(taps_list).reshape(3, 3, 3, shape[0], padded_inputs.shape[0])


def per_device(
    features, pre_first, pre_second, w_first, w_second, w_out, b_out, y_target, k_target
):
    count_sky = lax.axis_size("sky")
    count_los = lax.axis_size("los")
    depth_all = pre_first.shape[2] * count_los
    norm_factor = 1.0 / math.sqrt(features.shape[1] * count_sky * features.shape[3] * depth_all)
    shape = features.shape
    first_wide = pre_first.astype(jnp.float32)
    second_wide = pre_second.astype(jnp.float32)
    hidden_second = jax.nn.silu(second_wide).astype(jnp.bfloat16)
    heads_raw = jnp.einsum(
        "oi,ixzy->oxzy", w_out, hidden_second, preferred_element_type=jnp.float32
    )
    heads_raw = heads_raw + b_out[:, None, None, None]
    pressure = jax.nn.softplus(heads_raw[0])
    density = jax.nn.softplus(heads_raw[1])
    velocity = heads_raw[2]
    y_part = jnp.sum(pressure, axis=1) / depth_all
    k_part = -jnp.sum(density * velocity, axis=1) / depth_all
    y_map, k_map = butterfly_sum(jnp.stack((y_part, k_part)), ("los",))
    y_resid = y_map - y_target
    k_resid = k_map - k_target
    y_resid = y_resid[:, None, :]
    k_resid = k_resid[:, None, :]
    head_grad = jnp.stack(
        (
            y_resid * jax.nn.sigmoid(heads_raw[0]),
            -k_resid * velocity * jax.nn.sigmoid(heads_raw[1]),
            -k_resid * density,
        )
    ).astype(jnp.bfloat16)
    grad_out = (
        jnp.einsum("oxzy,ixzy->oi", head_grad, hidden_second, preferred_element_type=jnp.float32)
        * norm_factor
    )
    grad_bias = jnp.sum(head_grad.astype(jnp.float32), axis=(1, 2, 3)) * norm_factor
    back_second = jnp.einsum("oi,oxzy->ixzy", w_out, head_grad, preferred_element_type=jnp.float32)
    grad_second_pre = (back_second * silu_slope(second_wide)).astype(jnp.bfloat16)
    second_padded = wrap_columns(extended(grad_second_pre, (("sky", 1), ("los", 2)), 1))
    back_first = spread_local(w_second, second_padded, shape)
    grad_first_pre = (back_first * silu_slope(first_wide)).astype(jnp.bfloat16)
    first_padded = wrap_columns(extended(grad_first_pre, (("sky", 1), ("los", 2)), 1))
    grad_features = spread_local(w_first, first_padded, shape).astype(jnp.bfloat16)
    saved_padded = wrap_columns(
        extended(jnp.stack((features, pre_first)), (("sky", 2), ("los", 3)), 1)
    )
    hidden_padded = jax.nn.silu(saved_padded[1].astype(jnp.float32)).astype(jnp.bfloat16)
    grad_second = taps_from_inputs(grad_second_pre, hidden_padded)
    grad_first = taps_from_inputs(grad_first_pre, saved_padded[0])
    early = (grad_second * norm_factor, grad_out, grad_bias)
    early_shapes = [part.shape for part in early]
    grad_second, grad_out, grad_bias = unpack_rows(
        butterfly_sum(pack_rows(early), ("los", "sky")), early_shapes
    )
    (grad_first,) = unpack_rows(
        butterfly_sum(pack_rows((grad_first * norm_factor,)), ("los", "sky")), [grad_first.shape]
    )
    return (grad_features, grad_first, grad_second, grad_out, grad_bias)


def solution(mesh):
    in_specs = (
        P(None, "sky", "los", None),
        P(None, "sky", "los", None),
        P(None, "sky", "los", None),
        P(),
        P(),
        P(),
        P(),
        P("sky", None),
        P("sky", None),
    )
    out_specs = (P(None, "sky", "los", None), P(), P(), P(), P())
    return jax.shard_map(
        per_device, mesh=mesh, in_specs=in_specs, out_specs=out_specs, check_vma=False
    )
```

```python
import math

import jax
import jax.numpy as jnp
from jax import lax
from jax.sharding import PartitionSpec as P


def extended(block, sides, width):
    for axis, dim in sides:
        count = lax.axis_size(axis)
        forward = [(i, i + 1) for i in range(count - 1)]
        forward.append((count - 1, 0))
        backward = [(target, source) for source, target in forward]
        low = lax.ppermute(
            lax.slice_in_dim(block, block.shape[dim] - width, None, axis=dim), axis, forward
        )
        high = lax.ppermute(lax.slice_in_dim(block, 0, width, axis=dim), axis, backward)
        block = jnp.concatenate([low, block, high], axis=dim)
    return block


def butterfly_sum(value, axes):
    for axis in axes:
        count = lax.axis_size(axis)
        if count & (count - 1):
            value = lax.psum(value, axis)
            continue
        step = 1
        while step < count:
            pairs = [(i, i ^ step) for i in range(count)]
            value = value + lax.ppermute(value, axis, pairs)
            step *= 2
    return value


def pack_rows(parts):
    flat = jnp.concatenate([part.reshape(-1) for part in parts])
    rows = -(-flat.shape[0] // 128)
    flat = jnp.pad(flat, (0, rows * 128 - flat.shape[0]))
    return flat.reshape(rows, 128)


def unpack_rows(packed, shapes):
    flat = packed.reshape(-1)
    parts = []
    start = 0
    for shape in shapes:
        size = math.prod(shape)
        parts.append(flat[start : start + size].reshape(shape))
        start += size
    return parts


def silu_slope(value):
    sigma = jax.nn.sigmoid(value)
    return sigma * (1.0 + value * (1.0 - sigma))


def wrap_columns(field):
    return jnp.concatenate((field[..., -1:], field, field[..., :1]), axis=-1)


def spread_local(weight, padded, shape):
    result = jnp.zeros(shape, jnp.float32)
    for tap_x in range(3):
        for tap_z in range(3):
            for tap_y in range(3):
                window = padded[
                    :,
                    2 - tap_x : 2 - tap_x + shape[1],
                    2 - tap_z : 2 - tap_z + shape[2],
                    2 - tap_y : 2 - tap_y + shape[3],
                ]
                result = result + jnp.einsum(
                    "oi,oxzy->ixzy",
                    weight[tap_x, tap_z, tap_y],
                    window,
                    preferred_element_type=jnp.float32,
                )
    return result


def taps_from_inputs(grad_field, padded_inputs):
    shape = grad_field.shape
    taps_list = []
    for tap_x in range(3):
        for tap_z in range(3):
            for tap_y in range(3):
                window = padded_inputs[
                    :, tap_x : tap_x + shape[1], tap_z : tap_z + shape[2], tap_y : tap_y + shape[3]
                ]
                taps_list.append(
                    jnp.einsum(
                        "oxzy,ixzy->oi", grad_field, window, preferred_element_type=jnp.float32
                    )
                )
    return jnp.stack(taps_list).reshape(3, 3, 3, shape[0], padded_inputs.shape[0])


def per_device(
    features, pre_first, pre_second, w_first, w_second, w_out, b_out, y_target, k_target
):
    count_sky = lax.axis_size("sky")
    count_los = lax.axis_size("los")
    depth_all = pre_first.shape[2] * count_los
    norm_factor = 1.0 / math.sqrt(features.shape[1] * count_sky * features.shape[3] * depth_all)
    shape = features.shape
    saved_padded = wrap_columns(
        extended(jnp.stack((features, pre_first)), (("sky", 2), ("los", 3)), 1)
    )
    hidden_padded = jax.nn.silu(saved_padded[1].astype(jnp.float32)).astype(jnp.bfloat16)
    first_wide = pre_first.astype(jnp.float32)
    second_wide = pre_second.astype(jnp.float32)
    hidden_second = jax.nn.silu(second_wide).astype(jnp.bfloat16)
    heads_raw = jnp.einsum(
        "oi,ixzy->oxzy", w_out, hidden_second, preferred_element_type=jnp.float32
    )
    heads_raw = heads_raw + b_out[:, None, None, None]
    pressure = jax.nn.softplus(heads_raw[0])
    density = jax.nn.softplus(heads_raw[1])
    velocity = heads_raw[2]
    y_part = jnp.sum(pressure, axis=1) / depth_all
    k_part = -jnp.sum(density * velocity, axis=1) / depth_all
    y_map, k_map = butterfly_sum(jnp.stack((y_part, k_part)), ("los",))
    y_resid = y_map - y_target
    k_resid = k_map - k_target
    y_resid = y_resid[:, None, :]
    k_resid = k_resid[:, None, :]
    head_grad = jnp.stack(
        (
            y_resid * jax.nn.sigmoid(heads_raw[0]),
            -k_resid * velocity * jax.nn.sigmoid(heads_raw[1]),
            -k_resid * density,
        )
    ).astype(jnp.bfloat16)
    grad_out = (
        jnp.einsum("oxzy,ixzy->oi", head_grad, hidden_second, preferred_element_type=jnp.float32)
        * norm_factor
    )
    grad_bias = jnp.sum(head_grad.astype(jnp.float32), axis=(1, 2, 3)) * norm_factor
    back_second = jnp.einsum("oi,oxzy->ixzy", w_out, head_grad, preferred_element_type=jnp.float32)
    grad_second_pre = (back_second * silu_slope(second_wide)).astype(jnp.bfloat16)
    grad_second = taps_from_inputs(grad_second_pre, hidden_padded)
    early = (grad_second * norm_factor, grad_out, grad_bias)
    early_shapes = [part.shape for part in early]
    early_packed, grad_second_pre = lax.optimization_barrier((pack_rows(early), grad_second_pre))
    early_packed = butterfly_sum(early_packed, ("los", "sky"))
    second_padded = wrap_columns(extended(grad_second_pre, (("sky", 1), ("los", 2)), 1))
    back_first = spread_local(w_second, second_padded, shape)
    grad_first_pre = (back_first * silu_slope(first_wide)).astype(jnp.bfloat16)
    early_packed, grad_first_pre = lax.optimization_barrier((early_packed, grad_first_pre))
    grad_first = taps_from_inputs(grad_first_pre, saved_padded[0])
    late_packed, grad_first_pre = lax.optimization_barrier(
        (pack_rows((grad_first * norm_factor,)), grad_first_pre)
    )
    late_packed = butterfly_sum(late_packed, ("los", "sky"))
    first_padded = wrap_columns(extended(grad_first_pre, (("sky", 1), ("los", 2)), 1))
    grad_features = spread_local(w_first, first_padded, shape).astype(jnp.bfloat16)
    grad_second, grad_out, grad_bias = unpack_rows(early_packed, early_shapes)
    (grad_first,) = unpack_rows(late_packed, [grad_first.shape])
    return (grad_features, grad_first, grad_second, grad_out, grad_bias)


def solution(mesh):
    in_specs = (
        P(None, "sky", "los", None),
        P(None, "sky", "los", None),
        P(None, "sky", "los", None),
        P(),
        P(),
        P(),
        P(),
        P("sky", None),
        P("sky", None),
    )
    out_specs = (P(None, "sky", "los", None), P(), P(), P(), P())
    return jax.shard_map(
        per_device, mesh=mesh, in_specs=in_specs, out_specs=out_specs, check_vma=False
    )
```

```python
import math

import jax
import jax.numpy as jnp
from jax import lax
from jax.sharding import PartitionSpec as P


def extended(block, sides, width):
    for axis, dim in sides:
        count = lax.axis_size(axis)
        forward = [(i, i + 1) for i in range(count - 1)]
        forward.append((count - 1, 0))
        backward = [(target, source) for source, target in forward]
        low = lax.ppermute(
            lax.slice_in_dim(block, block.shape[dim] - width, None, axis=dim), axis, forward
        )
        high = lax.ppermute(lax.slice_in_dim(block, 0, width, axis=dim), axis, backward)
        block = jnp.concatenate([low, block, high], axis=dim)
    return block


def butterfly_sum(value, axes):
    for axis in axes:
        count = lax.axis_size(axis)
        if count & (count - 1):
            value = lax.psum(value, axis)
            continue
        step = 1
        while step < count:
            pairs = [(i, i ^ step) for i in range(count)]
            value = value + lax.ppermute(value, axis, pairs)
            step *= 2
    return value


def pack_rows(parts):
    flat = jnp.concatenate([part.reshape(-1) for part in parts])
    rows = -(-flat.shape[0] // 128)
    flat = jnp.pad(flat, (0, rows * 128 - flat.shape[0]))
    return flat.reshape(rows, 128)


def unpack_rows(packed, shapes):
    flat = packed.reshape(-1)
    parts = []
    start = 0
    for shape in shapes:
        size = math.prod(shape)
        parts.append(flat[start : start + size].reshape(shape))
        start += size
    return parts


def silu_slope(value):
    sigma = jax.nn.sigmoid(value)
    return sigma * (1.0 + value * (1.0 - sigma))


def wrap_columns(field):
    return jnp.concatenate((field[..., -1:], field, field[..., :1]), axis=-1)


def spread_local(weight, padded, shape):
    kernel = jnp.transpose(weight[::-1, ::-1, ::-1], (4, 3, 0, 1, 2))
    return lax.conv_general_dilated(
        padded[None],
        kernel,
        (1, 1, 1),
        "VALID",
        dimension_numbers=("NCDHW", "OIDHW", "NCDHW"),
        preferred_element_type=jnp.float32,
    )[0]


def taps_from_inputs(grad_field, padded_inputs):
    taps = lax.conv_general_dilated(
        padded_inputs[:, None],
        grad_field[:, None],
        (1, 1, 1),
        "VALID",
        dimension_numbers=("NCDHW", "OIDHW", "NCDHW"),
        preferred_element_type=jnp.float32,
    )
    return jnp.transpose(taps, (2, 3, 4, 1, 0))


def per_device(
    features, pre_first, pre_second, w_first, w_second, w_out, b_out, y_target, k_target
):
    count_sky = lax.axis_size("sky")
    count_los = lax.axis_size("los")
    depth_all = pre_first.shape[2] * count_los
    norm_factor = 1.0 / math.sqrt(features.shape[1] * count_sky * features.shape[3] * depth_all)
    shape = features.shape
    first_wide = pre_first.astype(jnp.float32)
    second_wide = pre_second.astype(jnp.float32)
    hidden_second = jax.nn.silu(second_wide).astype(jnp.bfloat16)
    heads_raw = jnp.einsum(
        "oi,ixzy->oxzy", w_out, hidden_second, preferred_element_type=jnp.float32
    )
    heads_raw = heads_raw + b_out[:, None, None, None]
    pressure = jax.nn.softplus(heads_raw[0])
    density = jax.nn.softplus(heads_raw[1])
    velocity = heads_raw[2]
    y_part = jnp.sum(pressure, axis=1) / depth_all
    k_part = -jnp.sum(density * velocity, axis=1) / depth_all
    y_map, k_map = butterfly_sum(jnp.stack((y_part, k_part)), ("los",))
    y_resid = y_map - y_target
    k_resid = k_map - k_target
    y_resid = y_resid[:, None, :]
    k_resid = k_resid[:, None, :]
    head_grad = jnp.stack(
        (
            y_resid * jax.nn.sigmoid(heads_raw[0]),
            -k_resid * velocity * jax.nn.sigmoid(heads_raw[1]),
            -k_resid * density,
        )
    ).astype(jnp.bfloat16)
    grad_out = (
        jnp.einsum("oxzy,ixzy->oi", head_grad, hidden_second, preferred_element_type=jnp.float32)
        * norm_factor
    )
    grad_bias = jnp.sum(head_grad.astype(jnp.float32), axis=(1, 2, 3)) * norm_factor
    back_second = jnp.einsum("oi,oxzy->ixzy", w_out, head_grad, preferred_element_type=jnp.float32)
    grad_second_pre = (back_second * silu_slope(second_wide)).astype(jnp.bfloat16)
    second_padded = wrap_columns(extended(grad_second_pre, (("sky", 1), ("los", 2)), 1))
    back_first = spread_local(w_second, second_padded, shape)
    grad_first_pre = (back_first * silu_slope(first_wide)).astype(jnp.bfloat16)
    first_padded = wrap_columns(extended(grad_first_pre, (("sky", 1), ("los", 2)), 1))
    grad_features = spread_local(w_first, first_padded, shape).astype(jnp.bfloat16)
    saved_padded = wrap_columns(
        extended(jnp.stack((features, pre_first)), (("sky", 2), ("los", 3)), 1)
    )
    hidden_padded = jax.nn.silu(saved_padded[1].astype(jnp.float32)).astype(jnp.bfloat16)
    grad_second = taps_from_inputs(grad_second_pre, hidden_padded)
    grad_first = taps_from_inputs(grad_first_pre, saved_padded[0])
    early = (grad_second * norm_factor, grad_out, grad_bias)
    early_shapes = [part.shape for part in early]
    grad_second, grad_out, grad_bias = unpack_rows(
        butterfly_sum(pack_rows(early), ("los", "sky")), early_shapes
    )
    (grad_first,) = unpack_rows(
        butterfly_sum(pack_rows((grad_first * norm_factor,)), ("los", "sky")), [grad_first.shape]
    )
    return (grad_features, grad_first, grad_second, grad_out, grad_bias)


def solution(mesh):
    in_specs = (
        P(None, "sky", "los", None),
        P(None, "sky", "los", None),
        P(None, "sky", "los", None),
        P(),
        P(),
        P(),
        P(),
        P("sky", None),
        P("sky", None),
    )
    out_specs = (P(None, "sky", "los", None), P(), P(), P(), P())
    return jax.shard_map(
        per_device, mesh=mesh, in_specs=in_specs, out_specs=out_specs, check_vma=False
    )
```

```python
import math

import jax
import jax.numpy as jnp
from jax import lax
from jax.sharding import PartitionSpec as P


def extended(block, sides, width):
    for axis, dim in sides:
        count = lax.axis_size(axis)
        forward = [(i, i + 1) for i in range(count - 1)]
        forward.append((count - 1, 0))
        backward = [(target, source) for source, target in forward]
        low = lax.ppermute(
            lax.slice_in_dim(block, block.shape[dim] - width, None, axis=dim), axis, forward
        )
        high = lax.ppermute(lax.slice_in_dim(block, 0, width, axis=dim), axis, backward)
        block = jnp.concatenate([low, block, high], axis=dim)
    return block


def butterfly_sum(value, axes):
    for axis in axes:
        count = lax.axis_size(axis)
        if count & (count - 1):
            value = lax.psum(value, axis)
            continue
        step = 1
        while step < count:
            pairs = [(i, i ^ step) for i in range(count)]
            value = value + lax.ppermute(value, axis, pairs)
            step *= 2
    return value


def pack_rows(parts):
    flat = jnp.concatenate([part.reshape(-1) for part in parts])
    rows = -(-flat.shape[0] // 128)
    flat = jnp.pad(flat, (0, rows * 128 - flat.shape[0]))
    return flat.reshape(rows, 128)


def unpack_rows(packed, shapes):
    flat = packed.reshape(-1)
    parts = []
    start = 0
    for shape in shapes:
        size = math.prod(shape)
        parts.append(flat[start : start + size].reshape(shape))
        start += size
    return parts


def silu_slope(value):
    sigma = jax.nn.sigmoid(value)
    return sigma * (1.0 + value * (1.0 - sigma))


def wrap_columns(field):
    return jnp.concatenate((field[..., -1:], field, field[..., :1]), axis=-1)


def spread_local(weight, padded, shape):
    kernel = jnp.transpose(weight[::-1, ::-1, ::-1], (4, 3, 0, 1, 2))
    return lax.conv_general_dilated(
        padded[None],
        kernel,
        (1, 1, 1),
        "VALID",
        dimension_numbers=("NCDHW", "OIDHW", "NCDHW"),
        preferred_element_type=jnp.float32,
    )[0]


def taps_from_inputs(grad_field, padded_inputs):
    shape = grad_field.shape
    taps_list = []
    for tap_x in range(3):
        for tap_z in range(3):
            for tap_y in range(3):
                window = padded_inputs[
                    :, tap_x : tap_x + shape[1], tap_z : tap_z + shape[2], tap_y : tap_y + shape[3]
                ]
                taps_list.append(
                    jnp.einsum(
                        "oxzy,ixzy->oi", grad_field, window, preferred_element_type=jnp.float32
                    )
                )
    return jnp.stack(taps_list).reshape(3, 3, 3, shape[0], padded_inputs.shape[0])


def per_device(
    features, pre_first, pre_second, w_first, w_second, w_out, b_out, y_target, k_target
):
    count_sky = lax.axis_size("sky")
    count_los = lax.axis_size("los")
    depth_all = pre_first.shape[2] * count_los
    norm_factor = 1.0 / math.sqrt(features.shape[1] * count_sky * features.shape[3] * depth_all)
    shape = features.shape
    first_wide = pre_first.astype(jnp.float32)
    second_wide = pre_second.astype(jnp.float32)
    hidden_second = jax.nn.silu(second_wide).astype(jnp.bfloat16)
    heads_raw = jnp.einsum(
        "oi,ixzy->oxzy", w_out, hidden_second, preferred_element_type=jnp.float32
    )
    heads_raw = heads_raw + b_out[:, None, None, None]
    pressure = jax.nn.softplus(heads_raw[0])
    density = jax.nn.softplus(heads_raw[1])
    velocity = heads_raw[2]
    y_part = jnp.sum(pressure, axis=1) / depth_all
    k_part = -jnp.sum(density * velocity, axis=1) / depth_all
    y_map, k_map = butterfly_sum(jnp.stack((y_part, k_part)), ("los",))
    y_resid = y_map - y_target
    k_resid = k_map - k_target
    y_resid = y_resid[:, None, :]
    k_resid = k_resid[:, None, :]
    head_grad = jnp.stack(
        (
            y_resid * jax.nn.sigmoid(heads_raw[0]),
            -k_resid * velocity * jax.nn.sigmoid(heads_raw[1]),
            -k_resid * density,
        )
    ).astype(jnp.bfloat16)
    grad_out = (
        jnp.einsum("oxzy,ixzy->oi", head_grad, hidden_second, preferred_element_type=jnp.float32)
        * norm_factor
    )
    grad_bias = jnp.sum(head_grad.astype(jnp.float32), axis=(1, 2, 3)) * norm_factor
    back_second = jnp.einsum("oi,oxzy->ixzy", w_out, head_grad, preferred_element_type=jnp.float32)
    grad_second_pre = (back_second * silu_slope(second_wide)).astype(jnp.bfloat16)
    second_padded = wrap_columns(extended(grad_second_pre, (("sky", 1), ("los", 2)), 1))
    back_first = spread_local(w_second, second_padded, shape)
    grad_first_pre = (back_first * silu_slope(first_wide)).astype(jnp.bfloat16)
    first_padded = wrap_columns(extended(grad_first_pre, (("sky", 1), ("los", 2)), 1))
    grad_features = spread_local(w_first, first_padded, shape).astype(jnp.bfloat16)
    saved_padded = wrap_columns(
        extended(jnp.stack((features, pre_first)), (("sky", 2), ("los", 3)), 1)
    )
    hidden_padded = jax.nn.silu(saved_padded[1].astype(jnp.float32)).astype(jnp.bfloat16)
    grad_second = taps_from_inputs(grad_second_pre, hidden_padded)
    grad_first = taps_from_inputs(grad_first_pre, saved_padded[0])
    early = (grad_second * norm_factor, grad_out, grad_bias)
    early_shapes = [part.shape for part in early]
    grad_second, grad_out, grad_bias = unpack_rows(
        butterfly_sum(pack_rows(early), ("los", "sky")), early_shapes
    )
    (grad_first,) = unpack_rows(
        butterfly_sum(pack_rows((grad_first * norm_factor,)), ("los", "sky")), [grad_first.shape]
    )
    return (grad_features, grad_first, grad_second, grad_out, grad_bias)


def solution(mesh):
    in_specs = (
        P(None, "sky", "los", None),
        P(None, "sky", "los", None),
        P(None, "sky", "los", None),
        P(),
        P(),
        P(),
        P(),
        P("sky", None),
        P("sky", None),
    )
    out_specs = (P(None, "sky", "los", None), P(), P(), P(), P())
    return jax.shard_map(
        per_device, mesh=mesh, in_specs=in_specs, out_specs=out_specs, check_vma=False
    )
```

```python
import math

import jax
import jax.numpy as jnp
from jax import lax
from jax.sharding import PartitionSpec as P


def extended(block, sides, width):
    for axis, dim in sides:
        count = lax.axis_size(axis)
        forward = [(i, i + 1) for i in range(count - 1)]
        forward.append((count - 1, 0))
        backward = [(target, source) for source, target in forward]
        low = lax.ppermute(
            lax.slice_in_dim(block, block.shape[dim] - width, None, axis=dim), axis, forward
        )
        high = lax.ppermute(lax.slice_in_dim(block, 0, width, axis=dim), axis, backward)
        block = jnp.concatenate([low, block, high], axis=dim)
    return block


def butterfly_sum(value, axes, skip=0):
    for axis in axes:
        count = lax.axis_size(axis)
        if count & (count - 1):
            value = lax.psum(value, axis)
            continue
        step = 2 if skip and axis == axes[0] else 1
        while step < count:
            pairs = [(i, i ^ step) for i in range(count)]
            value = value + lax.ppermute(value, axis, pairs)
            step *= 2
    return value


def split_sum(value, axes):
    first = axes[0]
    if lax.axis_size(first) % 2:
        return butterfly_sum(value, axes)
    half = value.shape[0] // 2
    pairs = [(i, i ^ 1) for i in range(lax.axis_size(first))]
    upper = lax.axis_index(first) % 2 == 1
    keep = jnp.where(upper, value[half:], value[:half])
    send = jnp.where(upper, value[:half], value[half:])
    keep = keep + lax.ppermute(send, first, pairs)
    keep = butterfly_sum(keep, axes, skip=1)
    other = lax.ppermute(keep, first, pairs)
    return jnp.where(
        upper, jnp.concatenate((other, keep)), jnp.concatenate((keep, other))
    )


def pack_rows(parts):
    flat = jnp.concatenate([part.reshape(-1) for part in parts])
    rows = -(-flat.shape[0] // 2048) * 16
    flat = jnp.pad(flat, (0, rows * 128 - flat.shape[0]))
    return flat.reshape(rows, 128)


def unpack_rows(packed, shapes):
    flat = packed.reshape(-1)
    parts = []
    start = 0
    for shape in shapes:
        size = math.prod(shape)
        parts.append(flat[start : start + size].reshape(shape))
        start += size
    return parts


def silu_slope(value):
    sigma = jax.nn.sigmoid(value)
    return sigma * (1.0 + value * (1.0 - sigma))


def wrap_columns(field):
    return jnp.concatenate((field[..., -1:], field, field[..., :1]), axis=-1)


def spread_local(weight, padded, shape):
    kernel = jnp.transpose(weight[::-1, ::-1, ::-1], (4, 3, 0, 1, 2))
    return lax.conv_general_dilated(
        padded[None],
        kernel,
        (1, 1, 1),
        "VALID",
        dimension_numbers=("NCDHW", "OIDHW", "NCDHW"),
        preferred_element_type=jnp.float32,
    )[0]


def taps_from_inputs(grad_field, padded_inputs):
    shape = grad_field.shape
    taps_list = []
    for tap_x in range(3):
        for tap_z in range(3):
            for tap_y in range(3):
                window = padded_inputs[
                    :, tap_x : tap_x + shape[1], tap_z : tap_z + shape[2], tap_y : tap_y + shape[3]
                ]
                taps_list.append(
                    jnp.einsum(
                        "oxzy,ixzy->oi", grad_field, window, preferred_element_type=jnp.float32
                    )
                )
    return jnp.stack(taps_list).reshape(3, 3, 3, shape[0], padded_inputs.shape[0])


def per_device(
    features, pre_first, pre_second, w_first, w_second, w_out, b_out, y_target, k_target
):
    count_sky = lax.axis_size("sky")
    count_los = lax.axis_size("los")
    depth_all = pre_first.shape[2] * count_los
    norm_factor = 1.0 / math.sqrt(features.shape[1] * count_sky * features.shape[3] * depth_all)
    shape = features.shape
    first_wide = pre_first.astype(jnp.float32)
    second_wide = pre_second.astype(jnp.float32)
    hidden_second = jax.nn.silu(second_wide).astype(jnp.bfloat16)
    heads_raw = jnp.einsum(
        "oi,ixzy->oxzy", w_out, hidden_second, preferred_element_type=jnp.float32
    )
    heads_raw = heads_raw + b_out[:, None, None, None]
    pressure = jax.nn.softplus(heads_raw[0])
    density = jax.nn.softplus(heads_raw[1])
    velocity = heads_raw[2]
    y_part = jnp.sum(pressure, axis=1) / depth_all
    k_part = -jnp.sum(density * velocity, axis=1) / depth_all
    y_map, k_map = butterfly_sum(jnp.stack((y_part, k_part)), ("los",))
    y_resid = y_map - y_target
    k_resid = k_map - k_target
    y_resid = y_resid[:, None, :]
    k_resid = k_resid[:, None, :]
    head_grad = jnp.stack(
        (
            y_resid * jax.nn.sigmoid(heads_raw[0]),
            -k_resid * velocity * jax.nn.sigmoid(heads_raw[1]),
            -k_resid * density,
        )
    ).astype(jnp.bfloat16)
    grad_out = (
        jnp.einsum("oxzy,ixzy->oi", head_grad, hidden_second, preferred_element_type=jnp.float32)
        * norm_factor
    )
    grad_bias = jnp.sum(head_grad.astype(jnp.float32), axis=(1, 2, 3)) * norm_factor
    back_second = jnp.einsum("oi,oxzy->ixzy", w_out, head_grad, preferred_element_type=jnp.float32)
    grad_second_pre = (back_second * silu_slope(second_wide)).astype(jnp.bfloat16)
    second_padded = wrap_columns(extended(grad_second_pre, (("sky", 1), ("los", 2)), 1))
    back_first = spread_local(w_second, second_padded, shape)
    grad_first_pre = (back_first * silu_slope(first_wide)).astype(jnp.bfloat16)
    first_padded = wrap_columns(extended(grad_first_pre, (("sky", 1), ("los", 2)), 1))
    grad_features = spread_local(w_first, first_padded, shape).astype(jnp.bfloat16)
    saved_padded = wrap_columns(
        extended(jnp.stack((features, pre_first)), (("sky", 2), ("los", 3)), 1)
    )
    hidden_padded = jax.nn.silu(saved_padded[1].astype(jnp.float32)).astype(jnp.bfloat16)
    grad_second = taps_from_inputs(grad_second_pre, hidden_padded)
    grad_first = taps_from_inputs(grad_first_pre, saved_padded[0])
    early = (grad_second * norm_factor, grad_out, grad_bias)
    early_shapes = [part.shape for part in early]
    grad_second, grad_out, grad_bias = unpack_rows(
        split_sum(pack_rows(early), ("los", "sky")), early_shapes
    )
    (grad_first,) = unpack_rows(
        split_sum(pack_rows((grad_first * norm_factor,)), ("los", "sky")), [grad_first.shape]
    )
    return (grad_features, grad_first, grad_second, grad_out, grad_bias)


def solution(mesh):
    in_specs = (
        P(None, "sky", "los", None),
        P(None, "sky", "los", None),
        P(None, "sky", "los", None),
        P(),
        P(),
        P(),
        P(),
        P("sky", None),
        P("sky", None),
    )
    out_specs = (P(None, "sky", "los", None), P(), P(), P(), P())
    return jax.shard_map(
        per_device, mesh=mesh, in_specs=in_specs, out_specs=out_specs, check_vma=False
    )
```

```python
import math

import jax
import jax.numpy as jnp
from jax import lax
from jax.sharding import PartitionSpec as P


def extended(block, sides, width):
    for axis, dim in sides:
        count = lax.axis_size(axis)
        forward = [(i, i + 1) for i in range(count - 1)]
        forward.append((count - 1, 0))
        backward = [(target, source) for source, target in forward]
        low = lax.ppermute(
            lax.slice_in_dim(block, block.shape[dim] - width, None, axis=dim), axis, forward
        )
        high = lax.ppermute(lax.slice_in_dim(block, 0, width, axis=dim), axis, backward)
        block = jnp.concatenate([low, block, high], axis=dim)
    return block


def butterfly_sum(value, axes, skip=0):
    for axis in axes:
        count = lax.axis_size(axis)
        if count & (count - 1):
            value = lax.psum(value, axis)
            continue
        step = 2 if skip and axis == axes[0] else 1
        while step < count:
            pairs = [(i, i ^ step) for i in range(count)]
            value = value + lax.ppermute(value, axis, pairs)
            step *= 2
    return value


def split_sum(value, axes):
    first = axes[0]
    if lax.axis_size(first) % 2:
        return butterfly_sum(value, axes)
    half = value.shape[0] // 2
    pairs = [(i, i ^ 1) for i in range(lax.axis_size(first))]
    upper = lax.axis_index(first) % 2 == 1
    keep = jnp.where(upper, value[half:], value[:half])
    send = jnp.where(upper, value[:half], value[half:])
    keep = keep + lax.ppermute(send, first, pairs)
    keep = butterfly_sum(keep, axes, skip=1)
    other = lax.ppermute(keep, first, pairs)
    return jnp.where(
        upper, jnp.concatenate((other, keep)), jnp.concatenate((keep, other))
    )


def pack_rows(parts):
    flat = jnp.concatenate([part.reshape(-1) for part in parts])
    rows = -(-flat.shape[0] // 2048) * 16
    flat = jnp.pad(flat, (0, rows * 128 - flat.shape[0]))
    return flat.reshape(rows, 128)


def unpack_rows(packed, shapes):
    flat = packed.reshape(-1)
    parts = []
    start = 0
    for shape in shapes:
        size = math.prod(shape)
        parts.append(flat[start : start + size].reshape(shape))
        start += size
    return parts


def silu_slope(value):
    sigma = jax.nn.sigmoid(value)
    return sigma * (1.0 + value * (1.0 - sigma))


def wrap_columns(field):
    return jnp.concatenate((field[..., -1:], field, field[..., :1]), axis=-1)


def spread_local(weight, padded, shape):
    kernel = jnp.transpose(weight[::-1, ::-1, ::-1], (4, 3, 0, 1, 2))
    return lax.conv_general_dilated(
        padded[None],
        kernel,
        (1, 1, 1),
        "VALID",
        dimension_numbers=("NCDHW", "OIDHW", "NCDHW"),
        preferred_element_type=jnp.float32,
    )[0]


def taps_from_inputs(grad_field, padded_inputs):
    shape = grad_field.shape
    windows = jnp.stack(
        [
            padded_inputs[
                :, tap_x : tap_x + shape[1], tap_z : tap_z + shape[2], tap_y : tap_y + shape[3]
            ]
            for tap_x in range(3)
            for tap_z in range(3)
            for tap_y in range(3)
        ]
    )
    taps = jnp.einsum(
        "oxzy,tixzy->toi", grad_field, windows, preferred_element_type=jnp.float32
    )
    return taps.reshape(3, 3, 3, shape[0], padded_inputs.shape[0])


def per_device(
    features, pre_first, pre_second, w_first, w_second, w_out, b_out, y_target, k_target
):
    count_sky = lax.axis_size("sky")
    count_los = lax.axis_size("los")
    depth_all = pre_first.shape[2] * count_los
    norm_factor = 1.0 / math.sqrt(features.shape[1] * count_sky * features.shape[3] * depth_all)
    shape = features.shape
    first_wide = pre_first.astype(jnp.float32)
    second_wide = pre_second.astype(jnp.float32)
    hidden_second = jax.nn.silu(second_wide).astype(jnp.bfloat16)
    heads_raw = jnp.einsum(
        "oi,ixzy->oxzy", w_out, hidden_second, preferred_element_type=jnp.float32
    )
    heads_raw = heads_raw + b_out[:, None, None, None]
    pressure = jax.nn.softplus(heads_raw[0])
    density = jax.nn.softplus(heads_raw[1])
    velocity = heads_raw[2]
    y_part = jnp.sum(pressure, axis=1) / depth_all
    k_part = -jnp.sum(density * velocity, axis=1) / depth_all
    y_map, k_map = butterfly_sum(jnp.stack((y_part, k_part)), ("los",))
    y_resid = y_map - y_target
    k_resid = k_map - k_target
    y_resid = y_resid[:, None, :]
    k_resid = k_resid[:, None, :]
    head_grad = jnp.stack(
        (
            y_resid * jax.nn.sigmoid(heads_raw[0]),
            -k_resid * velocity * jax.nn.sigmoid(heads_raw[1]),
            -k_resid * density,
        )
    ).astype(jnp.bfloat16)
    grad_out = (
        jnp.einsum("oxzy,ixzy->oi", head_grad, hidden_second, preferred_element_type=jnp.float32)
        * norm_factor
    )
    grad_bias = jnp.sum(head_grad.astype(jnp.float32), axis=(1, 2, 3)) * norm_factor
    back_second = jnp.einsum("oi,oxzy->ixzy", w_out, head_grad, preferred_element_type=jnp.float32)
    grad_second_pre = (back_second * silu_slope(second_wide)).astype(jnp.bfloat16)
    second_padded = wrap_columns(extended(grad_second_pre, (("sky", 1), ("los", 2)), 1))
    back_first = spread_local(w_second, second_padded, shape)
    grad_first_pre = (back_first * silu_slope(first_wide)).astype(jnp.bfloat16)
    first_padded = wrap_columns(extended(grad_first_pre, (("sky", 1), ("los", 2)), 1))
    grad_features = spread_local(w_first, first_padded, shape).astype(jnp.bfloat16)
    saved_padded = wrap_columns(
        extended(jnp.stack((features, pre_first)), (("sky", 2), ("los", 3)), 1)
    )
    hidden_padded = jax.nn.silu(saved_padded[1].astype(jnp.float32)).astype(jnp.bfloat16)
    grad_second = taps_from_inputs(grad_second_pre, hidden_padded)
    grad_first = taps_from_inputs(grad_first_pre, saved_padded[0])
    early = (grad_second * norm_factor, grad_out, grad_bias)
    early_shapes = [part.shape for part in early]
    grad_second, grad_out, grad_bias = unpack_rows(
        split_sum(pack_rows(early), ("los", "sky")), early_shapes
    )
    (grad_first,) = unpack_rows(
        split_sum(pack_rows((grad_first * norm_factor,)), ("los", "sky")), [grad_first.shape]
    )
    return (grad_features, grad_first, grad_second, grad_out, grad_bias)


def solution(mesh):
    in_specs = (
        P(None, "sky", "los", None),
        P(None, "sky", "los", None),
        P(None, "sky", "los", None),
        P(),
        P(),
        P(),
        P(),
        P("sky", None),
        P("sky", None),
    )
    out_specs = (P(None, "sky", "los", None), P(), P(), P(), P())
    return jax.shard_map(
        per_device, mesh=mesh, in_specs=in_specs, out_specs=out_specs, check_vma=False
    )
```

```python
import math

import jax
import jax.numpy as jnp
from jax import lax
from jax.sharding import PartitionSpec as P


def extended(block, sides, width):
    for axis, dim in sides:
        count = lax.axis_size(axis)
        forward = [(i, i + 1) for i in range(count - 1)]
        forward.append((count - 1, 0))
        backward = [(target, source) for source, target in forward]
        low = lax.ppermute(
            lax.slice_in_dim(block, block.shape[dim] - width, None, axis=dim), axis, forward
        )
        high = lax.ppermute(lax.slice_in_dim(block, 0, width, axis=dim), axis, backward)
        block = jnp.concatenate([low, block, high], axis=dim)
    return block


def haloed(block, dim_sky, dim_los):
    count_sky = lax.axis_size("sky")
    count_los = lax.axis_size("los")
    extent_sky = block.shape[dim_sky]
    extent_los = block.shape[dim_los]

    def part(sky_range, los_range):
        piece = lax.slice_in_dim(block, sky_range[0], sky_range[1], axis=dim_sky)
        return lax.slice_in_dim(piece, los_range[0], los_range[1], axis=dim_los)

    def shift(piece, step_sky, step_los):
        pairs = [
            (
                sky * count_los + los,
                (sky + step_sky) % count_sky * count_los + (los + step_los) % count_los,
            )
            for sky in range(count_sky)
            for los in range(count_los)
        ]
        return lax.ppermute(piece, ("sky", "los"), pairs)

    last_sky = (extent_sky - 1, extent_sky)
    first_sky = (0, 1)
    all_sky = (0, extent_sky)
    last_los = (extent_los - 1, extent_los)
    first_los = (0, 1)
    all_los = (0, extent_los)
    low_row = jnp.concatenate(
        (
            shift(part(last_sky, last_los), 1, 1),
            shift(part(last_sky, all_los), 1, 0),
            shift(part(last_sky, first_los), 1, -1),
        ),
        axis=dim_los,
    )
    middle = jnp.concatenate(
        (shift(part(all_sky, last_los), 0, 1), block, shift(part(all_sky, first_los), 0, -1)),
        axis=dim_los,
    )
    high_row = jnp.concatenate(
        (
            shift(part(first_sky, last_los), -1, 1),
            shift(part(first_sky, all_los), -1, 0),
            shift(part(first_sky, first_los), -1, -1),
        ),
        axis=dim_los,
    )
    return jnp.concatenate((low_row, middle, high_row), axis=dim_sky)


def butterfly_sum(value, axes, skip=0):
    for axis in axes:
        count = lax.axis_size(axis)
        if count & (count - 1):
            value = lax.psum(value, axis)
            continue
        step = 2 if skip and axis == axes[0] else 1
        while step < count:
            pairs = [(i, i ^ step) for i in range(count)]
            value = value + lax.ppermute(value, axis, pairs)
            step *= 2
    return value


def split_sum(value, axes):
    first = axes[0]
    if lax.axis_size(first) % 2:
        return butterfly_sum(value, axes)
    half = value.shape[0] // 2
    pairs = [(i, i ^ 1) for i in range(lax.axis_size(first))]
    upper = lax.axis_index(first) % 2 == 1
    keep = jnp.where(upper, value[half:], value[:half])
    send = jnp.where(upper, value[:half], value[half:])
    keep = keep + lax.ppermute(send, first, pairs)
    keep = butterfly_sum(keep, axes, skip=1)
    other = lax.ppermute(keep, first, pairs)
    return jnp.where(
        upper, jnp.concatenate((other, keep)), jnp.concatenate((keep, other))
    )


def pack_rows(parts):
    flat = jnp.concatenate([part.reshape(-1) for part in parts])
    rows = -(-flat.shape[0] // 2048) * 16
    flat = jnp.pad(flat, (0, rows * 128 - flat.shape[0]))
    return flat.reshape(rows, 128)


def unpack_rows(packed, shapes):
    flat = packed.reshape(-1)
    parts = []
    start = 0
    for shape in shapes:
        size = math.prod(shape)
        parts.append(flat[start : start + size].reshape(shape))
        start += size
    return parts


def silu_slope(value):
    sigma = jax.nn.sigmoid(value)
    return sigma * (1.0 + value * (1.0 - sigma))


def wrap_columns(field):
    return jnp.concatenate((field[..., -1:], field, field[..., :1]), axis=-1)


def spread_local(weight, padded, shape):
    kernel = jnp.transpose(weight[::-1, ::-1, ::-1], (4, 3, 0, 1, 2))
    return lax.conv_general_dilated(
        padded[None],
        kernel,
        (1, 1, 1),
        "VALID",
        dimension_numbers=("NCDHW", "OIDHW", "NCDHW"),
        preferred_element_type=jnp.float32,
    )[0]


def taps_from_inputs(grad_field, padded_inputs):
    shape = grad_field.shape
    windows = jnp.stack(
        [
            padded_inputs[
                :, tap_x : tap_x + shape[1], tap_z : tap_z + shape[2], tap_y : tap_y + shape[3]
            ]
            for tap_x in range(3)
            for tap_z in range(3)
            for tap_y in range(3)
        ]
    )
    taps = jnp.einsum(
        "oxzy,tixzy->toi", grad_field, windows, preferred_element_type=jnp.float32
    )
    return taps.reshape(3, 3, 3, shape[0], padded_inputs.shape[0])


def per_device(
    features, pre_first, pre_second, w_first, w_second, w_out, b_out, y_target, k_target
):
    count_sky = lax.axis_size("sky")
    count_los = lax.axis_size("los")
    depth_all = pre_first.shape[2] * count_los
    norm_factor = 1.0 / math.sqrt(features.shape[1] * count_sky * features.shape[3] * depth_all)
    shape = features.shape
    first_wide = pre_first.astype(jnp.float32)
    second_wide = pre_second.astype(jnp.float32)
    hidden_second = jax.nn.silu(second_wide).astype(jnp.bfloat16)
    heads_raw = jnp.einsum(
        "oi,ixzy->oxzy", w_out, hidden_second, preferred_element_type=jnp.float32
    )
    heads_raw = heads_raw + b_out[:, None, None, None]
    pressure = jax.nn.softplus(heads_raw[0])
    density = jax.nn.softplus(heads_raw[1])
    velocity = heads_raw[2]
    y_part = jnp.sum(pressure, axis=1) / depth_all
    k_part = -jnp.sum(density * velocity, axis=1) / depth_all
    y_map, k_map = butterfly_sum(jnp.stack((y_part, k_part)), ("los",))
    y_resid = y_map - y_target
    k_resid = k_map - k_target
    y_resid = y_resid[:, None, :]
    k_resid = k_resid[:, None, :]
    head_grad = jnp.stack(
        (
            y_resid * jax.nn.sigmoid(heads_raw[0]),
            -k_resid * velocity * jax.nn.sigmoid(heads_raw[1]),
            -k_resid * density,
        )
    ).astype(jnp.bfloat16)
    grad_out = (
        jnp.einsum("oxzy,ixzy->oi", head_grad, hidden_second, preferred_element_type=jnp.float32)
        * norm_factor
    )
    grad_bias = jnp.sum(head_grad.astype(jnp.float32), axis=(1, 2, 3)) * norm_factor
    back_second = jnp.einsum("oi,oxzy->ixzy", w_out, head_grad, preferred_element_type=jnp.float32)
    grad_second_pre = (back_second * silu_slope(second_wide)).astype(jnp.bfloat16)
    second_padded = wrap_columns(haloed(grad_second_pre, 1, 2))
    back_first = spread_local(w_second, second_padded, shape)
    grad_first_pre = (back_first * silu_slope(first_wide)).astype(jnp.bfloat16)
    first_padded = wrap_columns(haloed(grad_first_pre, 1, 2))
    grad_features = spread_local(w_first, first_padded, shape).astype(jnp.bfloat16)
    saved_padded = wrap_columns(
        haloed(jnp.stack((features, pre_first)), 2, 3)
    )
    hidden_padded = jax.nn.silu(saved_padded[1].astype(jnp.float32)).astype(jnp.bfloat16)
    grad_second = taps_from_inputs(grad_second_pre, hidden_padded)
    grad_first = taps_from_inputs(grad_first_pre, saved_padded[0])
    early = (grad_second * norm_factor, grad_out, grad_bias)
    early_shapes = [part.shape for part in early]
    grad_second, grad_out, grad_bias = unpack_rows(
        split_sum(pack_rows(early), ("los", "sky")), early_shapes
    )
    (grad_first,) = unpack_rows(
        split_sum(pack_rows((grad_first * norm_factor,)), ("los", "sky")), [grad_first.shape]
    )
    return (grad_features, grad_first, grad_second, grad_out, grad_bias)


def solution(mesh):
    in_specs = (
        P(None, "sky", "los", None),
        P(None, "sky", "los", None),
        P(None, "sky", "los", None),
        P(),
        P(),
        P(),
        P(),
        P("sky", None),
        P("sky", None),
    )
    out_specs = (P(None, "sky", "los", None), P(), P(), P(), P())
    return jax.shard_map(
        per_device, mesh=mesh, in_specs=in_specs, out_specs=out_specs, check_vma=False
    )
```

```python
import math

import jax
import jax.numpy as jnp
from jax import lax
from jax.sharding import PartitionSpec as P


def extended(block, sides, width):
    for axis, dim in sides:
        count = lax.axis_size(axis)
        forward = [(i, i + 1) for i in range(count - 1)]
        forward.append((count - 1, 0))
        backward = [(target, source) for source, target in forward]
        low = lax.ppermute(
            lax.slice_in_dim(block, block.shape[dim] - width, None, axis=dim), axis, forward
        )
        high = lax.ppermute(lax.slice_in_dim(block, 0, width, axis=dim), axis, backward)
        block = jnp.concatenate([low, block, high], axis=dim)
    return block


def butterfly_sum(value, axes, skip=0):
    for axis in axes:
        count = lax.axis_size(axis)
        if count & (count - 1):
            value = lax.psum(value, axis)
            continue
        step = 2 if skip and axis == axes[0] else 1
        while step < count:
            pairs = [(i, i ^ step) for i in range(count)]
            value = value + lax.ppermute(value, axis, pairs)
            step *= 2
    return value


def split_sum(value, axes):
    first = axes[0]
    if lax.axis_size(first) % 2:
        return butterfly_sum(value, axes)
    half = value.shape[0] // 2
    pairs = [(i, i ^ 1) for i in range(lax.axis_size(first))]
    upper = lax.axis_index(first) % 2 == 1
    keep = jnp.where(upper, value[half:], value[:half])
    send = jnp.where(upper, value[:half], value[half:])
    keep = keep + lax.ppermute(send, first, pairs)
    keep = butterfly_sum(keep, axes, skip=1)
    other = lax.ppermute(keep, first, pairs)
    return jnp.where(
        upper, jnp.concatenate((other, keep)), jnp.concatenate((keep, other))
    )


def pack_rows(parts):
    flat = jnp.concatenate([part.reshape(-1) for part in parts])
    rows = -(-flat.shape[0] // 2048) * 16
    flat = jnp.pad(flat, (0, rows * 128 - flat.shape[0]))
    return flat.reshape(rows, 128)


def unpack_rows(packed, shapes):
    flat = packed.reshape(-1)
    parts = []
    start = 0
    for shape in shapes:
        size = math.prod(shape)
        parts.append(flat[start : start + size].reshape(shape))
        start += size
    return parts


def silu_slope(value):
    sigma = jax.nn.sigmoid(value)
    return sigma * (1.0 + value * (1.0 - sigma))


def wrap_columns(field):
    return jnp.concatenate((field[..., -1:], field, field[..., :1]), axis=-1)


def spread_local(weight, padded, shape):
    kernel = jnp.transpose(weight[::-1, ::-1, ::-1], (4, 3, 0, 1, 2))
    return lax.conv_general_dilated(
        padded[None],
        kernel,
        (1, 1, 1),
        "VALID",
        dimension_numbers=("NCDHW", "OIDHW", "NCDHW"),
        preferred_element_type=jnp.float32,
    )[0]


def taps_from_inputs(grad_field, padded_inputs):
    shape = grad_field.shape
    windows = jnp.stack(
        [
            padded_inputs[
                :, tap_x : tap_x + shape[1], tap_z : tap_z + shape[2], tap_y : tap_y + shape[3]
            ]
            for tap_x in range(3)
            for tap_z in range(3)
            for tap_y in range(3)
        ]
    )
    taps = jnp.einsum(
        "oxzy,tixzy->toi", grad_field, windows, preferred_element_type=jnp.float32
    )
    return taps.reshape(3, 3, 3, shape[0], padded_inputs.shape[0])


def per_device(
    features, pre_first, pre_second, w_first, w_second, w_out, b_out, y_target, k_target
):
    count_sky = lax.axis_size("sky")
    count_los = lax.axis_size("los")
    depth_all = pre_first.shape[2] * count_los
    norm_factor = 1.0 / math.sqrt(features.shape[1] * count_sky * features.shape[3] * depth_all)
    shape = features.shape
    first_wide = pre_first.astype(jnp.float32)
    second_wide = pre_second.astype(jnp.float32)
    hidden_second = jax.nn.silu(second_wide).astype(jnp.bfloat16)
    heads_raw = jnp.einsum(
        "oi,ixzy->oxzy", w_out, hidden_second, preferred_element_type=jnp.float32
    )
    heads_raw = heads_raw + b_out[:, None, None, None]
    pressure = jax.nn.softplus(heads_raw[0])
    density = jax.nn.softplus(heads_raw[1])
    velocity = heads_raw[2]
    y_part = jnp.sum(pressure, axis=1) / depth_all
    k_part = -jnp.sum(density * velocity, axis=1) / depth_all
    y_map, k_map = butterfly_sum(jnp.stack((y_part, k_part)), ("los",))
    y_resid = y_map - y_target
    k_resid = k_map - k_target
    y_resid = y_resid[:, None, :]
    k_resid = k_resid[:, None, :]
    head_grad = jnp.stack(
        (
            y_resid * jax.nn.sigmoid(heads_raw[0]),
            -k_resid * velocity * jax.nn.sigmoid(heads_raw[1]),
            -k_resid * density,
        )
    ).astype(jnp.bfloat16)
    grad_out = (
        jnp.einsum("oxzy,ixzy->oi", head_grad, hidden_second, preferred_element_type=jnp.float32)
        * norm_factor
    )
    grad_bias = jnp.sum(head_grad.astype(jnp.float32), axis=(1, 2, 3)) * norm_factor
    back_second = jnp.einsum("oi,oxzy->ixzy", w_out, head_grad, preferred_element_type=jnp.float32)
    grad_second_pre = (back_second * silu_slope(second_wide)).astype(jnp.bfloat16)
    second_padded = wrap_columns(extended(grad_second_pre, (("sky", 1), ("los", 2)), 1))
    back_first = spread_local(w_second, second_padded, shape)
    grad_first_pre = (back_first * silu_slope(first_wide)).astype(jnp.bfloat16)
    first_padded = wrap_columns(extended(grad_first_pre, (("sky", 1), ("los", 2)), 1))
    grad_features = spread_local(w_first, first_padded, shape).astype(jnp.bfloat16)
    saved_padded = wrap_columns(
        extended(jnp.stack((features, pre_first)), (("sky", 2), ("los", 3)), 1)
    )
    hidden_padded = jax.nn.silu(saved_padded[1].astype(jnp.float32)).astype(jnp.bfloat16)
    grad_second = taps_from_inputs(grad_second_pre, hidden_padded)
    grad_first = taps_from_inputs(grad_first_pre, saved_padded[0])
    reduced = (grad_first * norm_factor, grad_second * norm_factor, grad_out, grad_bias)
    reduced_shapes = [part.shape for part in reduced]
    grad_first, grad_second, grad_out, grad_bias = unpack_rows(
        split_sum(pack_rows(reduced), ("los", "sky")), reduced_shapes
    )
    return (grad_features, grad_first, grad_second, grad_out, grad_bias)


def solution(mesh):
    in_specs = (
        P(None, "sky", "los", None),
        P(None, "sky", "los", None),
        P(None, "sky", "los", None),
        P(),
        P(),
        P(),
        P(),
        P("sky", None),
        P("sky", None),
    )
    out_specs = (P(None, "sky", "los", None), P(), P(), P(), P())
    return jax.shard_map(
        per_device, mesh=mesh, in_specs=in_specs, out_specs=out_specs, check_vma=False
    )
```

```python
import math

import jax
import jax.numpy as jnp
from jax import lax
from jax.sharding import PartitionSpec as P


def extended(block, sides, width):
    for axis, dim in sides:
        count = lax.axis_size(axis)
        forward = [(i, i + 1) for i in range(count - 1)]
        forward.append((count - 1, 0))
        backward = [(target, source) for source, target in forward]
        low = lax.ppermute(
            lax.slice_in_dim(block, block.shape[dim] - width, None, axis=dim), axis, forward
        )
        high = lax.ppermute(lax.slice_in_dim(block, 0, width, axis=dim), axis, backward)
        block = jnp.concatenate([low, block, high], axis=dim)
    return block


def butterfly_sum(value, axes, skip=0):
    for axis in axes:
        count = lax.axis_size(axis)
        if count & (count - 1):
            value = lax.psum(value, axis)
            continue
        step = 2 if skip and axis == axes[0] else 1
        while step < count:
            pairs = [(i, i ^ step) for i in range(count)]
            value = value + lax.ppermute(value, axis, pairs)
            step *= 2
    return value


def split_sum(value, axes):
    first = axes[0]
    if lax.axis_size(first) % 2:
        return butterfly_sum(value, axes)
    half = value.shape[0] // 2
    pairs = [(i, i ^ 1) for i in range(lax.axis_size(first))]
    upper = lax.axis_index(first) % 2 == 1
    keep = jnp.where(upper, value[half:], value[:half])
    send = jnp.where(upper, value[:half], value[half:])
    keep = keep + lax.ppermute(send, first, pairs)
    keep = butterfly_sum(keep, axes, skip=1)
    other = lax.ppermute(keep, first, pairs)
    return jnp.where(
        upper, jnp.concatenate((other, keep)), jnp.concatenate((keep, other))
    )


def pack_rows(parts):
    flat = jnp.concatenate([part.reshape(-1) for part in parts])
    rows = -(-flat.shape[0] // 2048) * 16
    flat = jnp.pad(flat, (0, rows * 128 - flat.shape[0]))
    return flat.reshape(rows, 128)


def unpack_rows(packed, shapes):
    flat = packed.reshape(-1)
    parts = []
    start = 0
    for shape in shapes:
        size = math.prod(shape)
        parts.append(flat[start : start + size].reshape(shape))
        start += size
    return parts


def silu_slope(value):
    sigma = jax.nn.sigmoid(value)
    return sigma * (1.0 + value * (1.0 - sigma))


def wrap_columns(field):
    return jnp.concatenate((field[..., -1:], field, field[..., :1]), axis=-1)


def spread_local(weight, padded, shape):
    kernel = jnp.transpose(weight[::-1, ::-1, ::-1], (4, 3, 0, 1, 2))
    return lax.conv_general_dilated(
        padded[None],
        kernel,
        (1, 1, 1),
        "VALID",
        dimension_numbers=("NCDHW", "OIDHW", "NCDHW"),
        preferred_element_type=jnp.float32,
    )[0]


def taps_from_inputs(grad_field, padded_inputs):
    shape = grad_field.shape
    windows = jnp.stack(
        [
            padded_inputs[
                :, tap_x : tap_x + shape[1], tap_z : tap_z + shape[2], tap_y : tap_y + shape[3]
            ]
            for tap_x in range(3)
            for tap_z in range(3)
            for tap_y in range(3)
        ]
    )
    taps = jnp.einsum(
        "oxzy,tixzy->toi", grad_field, windows, preferred_element_type=jnp.float32
    )
    return taps.reshape(3, 3, 3, shape[0], padded_inputs.shape[0])


def per_device(
    features, pre_first, pre_second, w_first, w_second, w_out, b_out, y_target, k_target
):
    count_sky = lax.axis_size("sky")
    count_los = lax.axis_size("los")
    depth_all = pre_first.shape[2] * count_los
    norm_factor = 1.0 / math.sqrt(features.shape[1] * count_sky * features.shape[3] * depth_all)
    shape = features.shape
    first_wide = pre_first.astype(jnp.float32)
    second_wide = pre_second.astype(jnp.float32)
    hidden_second = jax.nn.silu(second_wide).astype(jnp.bfloat16)
    heads_raw = jnp.einsum(
        "oi,ixzy->oxzy", w_out, hidden_second, preferred_element_type=jnp.float32
    )
    heads_raw = heads_raw + b_out[:, None, None, None]
    pressure = jax.nn.softplus(heads_raw[0])
    density = jax.nn.softplus(heads_raw[1])
    velocity = heads_raw[2]
    y_part = jnp.sum(pressure, axis=1) / depth_all
    k_part = -jnp.sum(density * velocity, axis=1) / depth_all
    y_map, k_map = butterfly_sum(jnp.stack((y_part, k_part)), ("los",))
    y_resid = y_map - y_target
    k_resid = k_map - k_target
    y_resid = y_resid[:, None, :]
    k_resid = k_resid[:, None, :]
    head_grad = jnp.stack(
        (
            y_resid * jax.nn.sigmoid(heads_raw[0]),
            -k_resid * velocity * jax.nn.sigmoid(heads_raw[1]),
            -k_resid * density,
        )
    ).astype(jnp.bfloat16)
    grad_out = (
        jnp.einsum("oxzy,ixzy->oi", head_grad, hidden_second, preferred_element_type=jnp.float32)
        * norm_factor
    )
    grad_bias = jnp.sum(head_grad.astype(jnp.float32), axis=(1, 2, 3)) * norm_factor
    back_second = jnp.einsum("oi,oxzy->ixzy", w_out, head_grad, preferred_element_type=jnp.float32)
    grad_second_pre = (back_second * silu_slope(second_wide)).astype(jnp.bfloat16)
    all_padded = wrap_columns(
        extended(jnp.stack((grad_second_pre, features, pre_first)), (("sky", 2), ("los", 3)), 1)
    )
    second_padded = all_padded[0]
    back_first = spread_local(w_second, second_padded, shape)
    grad_first_pre = (back_first * silu_slope(first_wide)).astype(jnp.bfloat16)
    first_padded = wrap_columns(extended(grad_first_pre, (("sky", 1), ("los", 2)), 1))
    grad_features = spread_local(w_first, first_padded, shape).astype(jnp.bfloat16)
    saved_padded = all_padded[1:]
    hidden_padded = jax.nn.silu(saved_padded[1].astype(jnp.float32)).astype(jnp.bfloat16)
    grad_second = taps_from_inputs(grad_second_pre, hidden_padded)
    grad_first = taps_from_inputs(grad_first_pre, saved_padded[0])
    reduced = (grad_first * norm_factor, grad_second * norm_factor, grad_out, grad_bias)
    reduced_shapes = [part.shape for part in reduced]
    grad_first, grad_second, grad_out, grad_bias = unpack_rows(
        split_sum(pack_rows(reduced), ("los", "sky")), reduced_shapes
    )
    return (grad_features, grad_first, grad_second, grad_out, grad_bias)


def solution(mesh):
    in_specs = (
        P(None, "sky", "los", None),
        P(None, "sky", "los", None),
        P(None, "sky", "los", None),
        P(),
        P(),
        P(),
        P(),
        P("sky", None),
        P("sky", None),
    )
    out_specs = (P(None, "sky", "los", None), P(), P(), P(), P())
    return jax.shard_map(
        per_device, mesh=mesh, in_specs=in_specs, out_specs=out_specs, check_vma=False
    )
```

```python
import math

import jax
import jax.numpy as jnp
from jax import lax
from jax.sharding import PartitionSpec as P


def extended(block, sides, width):
    for axis, dim in sides:
        count = lax.axis_size(axis)
        forward = [(i, i + 1) for i in range(count - 1)]
        forward.append((count - 1, 0))
        backward = [(target, source) for source, target in forward]
        low = lax.ppermute(
            lax.slice_in_dim(block, block.shape[dim] - width, None, axis=dim), axis, forward
        )
        high = lax.ppermute(lax.slice_in_dim(block, 0, width, axis=dim), axis, backward)
        block = jnp.concatenate([low, block, high], axis=dim)
    return block


def butterfly_sum(value, axes, skip=0):
    for axis in axes:
        count = lax.axis_size(axis)
        if count & (count - 1):
            value = lax.psum(value, axis)
            continue
        step = 2 if skip and axis == axes[0] else 1
        while step < count:
            pairs = [(i, i ^ step) for i in range(count)]
            value = value + lax.ppermute(value, axis, pairs)
            step *= 2
    return value


def split_sum(value, axes):
    first = axes[0]
    if lax.axis_size(first) % 2:
        return butterfly_sum(value, axes)
    half = value.shape[0] // 2
    pairs = [(i, i ^ 1) for i in range(lax.axis_size(first))]
    upper = lax.axis_index(first) % 2 == 1
    keep = jnp.where(upper, value[half:], value[:half])
    send = jnp.where(upper, value[:half], value[half:])
    keep = keep + lax.ppermute(send, first, pairs)
    keep = butterfly_sum(keep, axes, skip=1)
    other = lax.ppermute(keep, first, pairs)
    return jnp.where(
        upper, jnp.concatenate((other, keep)), jnp.concatenate((keep, other))
    )


def pack_rows(parts):
    flat = jnp.concatenate([part.reshape(-1) for part in parts])
    rows = -(-flat.shape[0] // 2048) * 16
    flat = jnp.pad(flat, (0, rows * 128 - flat.shape[0]))
    return flat.reshape(rows, 128)


def unpack_rows(packed, shapes):
    flat = packed.reshape(-1)
    parts = []
    start = 0
    for shape in shapes:
        size = math.prod(shape)
        parts.append(flat[start : start + size].reshape(shape))
        start += size
    return parts


def silu_slope(value):
    sigma = jax.nn.sigmoid(value)
    return sigma * (1.0 + value * (1.0 - sigma))


def wrap_columns(field):
    return jnp.concatenate((field[..., -1:], field, field[..., :1]), axis=-1)


def spread_local(weight, padded, shape):
    kernel = jnp.transpose(weight[::-1, ::-1, ::-1], (4, 3, 0, 1, 2))
    return lax.conv_general_dilated(
        padded[None],
        kernel,
        (1, 1, 1),
        "VALID",
        dimension_numbers=("NCDHW", "OIDHW", "NCDHW"),
        preferred_element_type=jnp.float32,
    )[0]


def taps_from_inputs(grad_field, extended_inputs):
    shape = grad_field.shape
    rolled = jnp.stack([jnp.roll(grad_field, tap_y - 1, axis=3) for tap_y in range(3)])
    windows = jnp.stack(
        [
            extended_inputs[:, tap_x : tap_x + shape[1], tap_z : tap_z + shape[2]]
            for tap_x in range(3)
            for tap_z in range(3)
        ]
    )
    taps = jnp.einsum(
        "soxzy,tixzy->tsoi", rolled, windows, preferred_element_type=jnp.float32
    )
    return taps.reshape(3, 3, 3, shape[0], extended_inputs.shape[0])


def per_device(
    features, pre_first, pre_second, w_first, w_second, w_out, b_out, y_target, k_target
):
    count_sky = lax.axis_size("sky")
    count_los = lax.axis_size("los")
    depth_all = pre_first.shape[2] * count_los
    norm_factor = 1.0 / math.sqrt(features.shape[1] * count_sky * features.shape[3] * depth_all)
    shape = features.shape
    first_wide = pre_first.astype(jnp.float32)
    second_wide = pre_second.astype(jnp.float32)
    hidden_second = jax.nn.silu(second_wide).astype(jnp.bfloat16)
    heads_raw = jnp.einsum(
        "oi,ixzy->oxzy", w_out, hidden_second, preferred_element_type=jnp.float32
    )
    heads_raw = heads_raw + b_out[:, None, None, None]
    pressure = jax.nn.softplus(heads_raw[0])
    density = jax.nn.softplus(heads_raw[1])
    velocity = heads_raw[2]
    y_part = jnp.sum(pressure, axis=1) / depth_all
    k_part = -jnp.sum(density * velocity, axis=1) / depth_all
    y_map, k_map = butterfly_sum(jnp.stack((y_part, k_part)), ("los",))
    y_resid = y_map - y_target
    k_resid = k_map - k_target
    y_resid = y_resid[:, None, :]
    k_resid = k_resid[:, None, :]
    head_grad = jnp.stack(
        (
            y_resid * jax.nn.sigmoid(heads_raw[0]),
            -k_resid * velocity * jax.nn.sigmoid(heads_raw[1]),
            -k_resid * density,
        )
    ).astype(jnp.bfloat16)
    grad_out = (
        jnp.einsum("oxzy,ixzy->oi", head_grad, hidden_second, preferred_element_type=jnp.float32)
        * norm_factor
    )
    grad_bias = jnp.sum(head_grad.astype(jnp.float32), axis=(1, 2, 3)) * norm_factor
    back_second = jnp.einsum("oi,oxzy->ixzy", w_out, head_grad, preferred_element_type=jnp.float32)
    grad_second_pre = (back_second * silu_slope(second_wide)).astype(jnp.bfloat16)
    second_padded = wrap_columns(extended(grad_second_pre, (("sky", 1), ("los", 2)), 1))
    back_first = spread_local(w_second, second_padded, shape)
    grad_first_pre = (back_first * silu_slope(first_wide)).astype(jnp.bfloat16)
    first_padded = wrap_columns(extended(grad_first_pre, (("sky", 1), ("los", 2)), 1))
    grad_features = spread_local(w_first, first_padded, shape).astype(jnp.bfloat16)
    saved_padded = extended(jnp.stack((features, pre_first)), (("sky", 2), ("los", 3)), 1)
    hidden_padded = jax.nn.silu(saved_padded[1].astype(jnp.float32)).astype(jnp.bfloat16)
    grad_second = taps_from_inputs(grad_second_pre, hidden_padded)
    grad_first = taps_from_inputs(grad_first_pre, saved_padded[0])
    reduced = (grad_first * norm_factor, grad_second * norm_factor, grad_out, grad_bias)
    reduced_shapes = [part.shape for part in reduced]
    grad_first, grad_second, grad_out, grad_bias = unpack_rows(
        split_sum(pack_rows(reduced), ("los", "sky")), reduced_shapes
    )
    return (grad_features, grad_first, grad_second, grad_out, grad_bias)


def solution(mesh):
    in_specs = (
        P(None, "sky", "los", None),
        P(None, "sky", "los", None),
        P(None, "sky", "los", None),
        P(),
        P(),
        P(),
        P(),
        P("sky", None),
        P("sky", None),
    )
    out_specs = (P(None, "sky", "los", None), P(), P(), P(), P())
    return jax.shard_map(
        per_device, mesh=mesh, in_specs=in_specs, out_specs=out_specs, check_vma=False
    )
```

```python
import math

import jax
import jax.numpy as jnp
from jax import lax
from jax.sharding import PartitionSpec as P


def extended(block, sides, width):
    for axis, dim in sides:
        count = lax.axis_size(axis)
        forward = [(i, i + 1) for i in range(count - 1)]
        forward.append((count - 1, 0))
        backward = [(target, source) for source, target in forward]
        low = lax.ppermute(
            lax.slice_in_dim(block, block.shape[dim] - width, None, axis=dim), axis, forward
        )
        high = lax.ppermute(lax.slice_in_dim(block, 0, width, axis=dim), axis, backward)
        block = jnp.concatenate([low, block, high], axis=dim)
    return block


def butterfly_sum(value, axes, skip=0):
    for axis in axes:
        count = lax.axis_size(axis)
        if count & (count - 1):
            value = lax.psum(value, axis)
            continue
        step = 2 if skip and axis == axes[0] else 1
        while step < count:
            pairs = [(i, i ^ step) for i in range(count)]
            value = value + lax.ppermute(value, axis, pairs)
            step *= 2
    return value


def split_sum(value, axes):
    first = axes[0]
    if lax.axis_size(first) % 2:
        return butterfly_sum(value, axes)
    half = value.shape[0] // 2
    pairs = [(i, i ^ 1) for i in range(lax.axis_size(first))]
    upper = lax.axis_index(first) % 2 == 1
    keep = jnp.where(upper, value[half:], value[:half])
    send = jnp.where(upper, value[:half], value[half:])
    keep = keep + lax.ppermute(send, first, pairs)
    keep = butterfly_sum(keep, axes, skip=1)
    other = lax.ppermute(keep, first, pairs)
    return jnp.where(
        upper, jnp.concatenate((other, keep)), jnp.concatenate((keep, other))
    )


def pack_rows(parts):
    flat = jnp.concatenate([part.reshape(-1) for part in parts])
    rows = -(-flat.shape[0] // 2048) * 16
    flat = jnp.pad(flat, (0, rows * 128 - flat.shape[0]))
    return flat.reshape(rows, 128)


def unpack_rows(packed, shapes):
    flat = packed.reshape(-1)
    parts = []
    start = 0
    for shape in shapes:
        size = math.prod(shape)
        parts.append(flat[start : start + size].reshape(shape))
        start += size
    return parts


def silu_slope(value):
    sigma = jax.nn.sigmoid(value)
    return sigma * (1.0 + value * (1.0 - sigma))


def wrap_columns(field):
    return jnp.concatenate((field[..., -1:], field, field[..., :1]), axis=-1)


def spread_local(weight, extended_field, shape):
    windows = jnp.stack(
        [
            extended_field[:, 2 - tap_x : 2 - tap_x + shape[1], 2 - tap_z : 2 - tap_z + shape[2]]
            for tap_x in range(3)
            for tap_z in range(3)
        ]
    )
    per_shift = jnp.einsum(
        "toxzy,tsoi->sixzy",
        windows,
        weight.reshape(9, 3, shape[0], shape[0]),
        preferred_element_type=jnp.float32,
    )
    return sum(jnp.roll(per_shift[tap_y], tap_y - 1, axis=3) for tap_y in range(3))


def taps_from_inputs(grad_field, extended_inputs):
    shape = grad_field.shape
    rolled = jnp.stack([jnp.roll(grad_field, tap_y - 1, axis=3) for tap_y in range(3)])
    windows = jnp.stack(
        [
            extended_inputs[:, tap_x : tap_x + shape[1], tap_z : tap_z + shape[2]]
            for tap_x in range(3)
            for tap_z in range(3)
        ]
    )
    taps = jnp.einsum(
        "soxzy,tixzy->tsoi", rolled, windows, preferred_element_type=jnp.float32
    )
    return taps.reshape(3, 3, 3, shape[0], extended_inputs.shape[0])


def per_device(
    features, pre_first, pre_second, w_first, w_second, w_out, b_out, y_target, k_target
):
    count_sky = lax.axis_size("sky")
    count_los = lax.axis_size("los")
    depth_all = pre_first.shape[2] * count_los
    norm_factor = 1.0 / math.sqrt(features.shape[1] * count_sky * features.shape[3] * depth_all)
    shape = features.shape
    first_wide = pre_first.astype(jnp.float32)
    second_wide = pre_second.astype(jnp.float32)
    hidden_second = jax.nn.silu(second_wide).astype(jnp.bfloat16)
    heads_raw = jnp.einsum(
        "oi,ixzy->oxzy", w_out, hidden_second, preferred_element_type=jnp.float32
    )
    heads_raw = heads_raw + b_out[:, None, None, None]
    pressure = jax.nn.softplus(heads_raw[0])
    density = jax.nn.softplus(heads_raw[1])
    velocity = heads_raw[2]
    y_part = jnp.sum(pressure, axis=1) / depth_all
    k_part = -jnp.sum(density * velocity, axis=1) / depth_all
    y_map, k_map = butterfly_sum(jnp.stack((y_part, k_part)), ("los",))
    y_resid = y_map - y_target
    k_resid = k_map - k_target
    y_resid = y_resid[:, None, :]
    k_resid = k_resid[:, None, :]
    head_grad = jnp.stack(
        (
            y_resid * jax.nn.sigmoid(heads_raw[0]),
            -k_resid * velocity * jax.nn.sigmoid(heads_raw[1]),
            -k_resid * density,
        )
    ).astype(jnp.bfloat16)
    grad_out = (
        jnp.einsum("oxzy,ixzy->oi", head_grad, hidden_second, preferred_element_type=jnp.float32)
        * norm_factor
    )
    grad_bias = jnp.sum(head_grad.astype(jnp.float32), axis=(1, 2, 3)) * norm_factor
    back_second = jnp.einsum("oi,oxzy->ixzy", w_out, head_grad, preferred_element_type=jnp.float32)
    grad_second_pre = (back_second * silu_slope(second_wide)).astype(jnp.bfloat16)
    second_padded = extended(grad_second_pre, (("sky", 1), ("los", 2)), 1)
    back_first = spread_local(w_second, second_padded, shape)
    grad_first_pre = (back_first * silu_slope(first_wide)).astype(jnp.bfloat16)
    first_padded = extended(grad_first_pre, (("sky", 1), ("los", 2)), 1)
    grad_features = spread_local(w_first, first_padded, shape).astype(jnp.bfloat16)
    saved_padded = extended(jnp.stack((features, pre_first)), (("sky", 2), ("los", 3)), 1)
    hidden_padded = jax.nn.silu(saved_padded[1].astype(jnp.float32)).astype(jnp.bfloat16)
    grad_second = taps_from_inputs(grad_second_pre, hidden_padded)
    grad_first = taps_from_inputs(grad_first_pre, saved_padded[0])
    reduced = (grad_first * norm_factor, grad_second * norm_factor, grad_out, grad_bias)
    reduced_shapes = [part.shape for part in reduced]
    grad_first, grad_second, grad_out, grad_bias = unpack_rows(
        split_sum(pack_rows(reduced), ("los", "sky")), reduced_shapes
    )
    return (grad_features, grad_first, grad_second, grad_out, grad_bias)


def solution(mesh):
    in_specs = (
        P(None, "sky", "los", None),
        P(None, "sky", "los", None),
        P(None, "sky", "los", None),
        P(),
        P(),
        P(),
        P(),
        P("sky", None),
        P("sky", None),
    )
    out_specs = (P(None, "sky", "los", None), P(), P(), P(), P())
    return jax.shard_map(
        per_device, mesh=mesh, in_specs=in_specs, out_specs=out_specs, check_vma=False
    )
```

```python
import math

import jax
import jax.numpy as jnp
from jax import lax
from jax.sharding import PartitionSpec as P


def extended(block, sides, width):
    for axis, dim in sides:
        count = lax.axis_size(axis)
        forward = [(i, i + 1) for i in range(count - 1)]
        forward.append((count - 1, 0))
        backward = [(target, source) for source, target in forward]
        low = lax.ppermute(
            lax.slice_in_dim(block, block.shape[dim] - width, None, axis=dim), axis, forward
        )
        high = lax.ppermute(lax.slice_in_dim(block, 0, width, axis=dim), axis, backward)
        block = jnp.concatenate([low, block, high], axis=dim)
    return block


def butterfly_sum(value, axes, skip=0):
    for axis in axes:
        count = lax.axis_size(axis)
        if count & (count - 1):
            value = lax.psum(value, axis)
            continue
        step = 2 if skip and axis == axes[0] else 1
        while step < count:
            pairs = [(i, i ^ step) for i in range(count)]
            value = value + lax.ppermute(value, axis, pairs)
            step *= 2
    return value


def split_sum(value, axes):
    sizes = [lax.axis_size(axis) for axis in axes]
    total = math.prod(sizes)
    if total & (total - 1) or sizes[0] % 2:
        return lax.psum(value, axes)
    half = value.shape[0] // 2
    upper = lax.axis_index(axes[0]) % 2 == 1
    keep = jnp.where(upper, value[half:], value[:half])
    send = jnp.where(upper, value[:half], value[half:])
    index_axes = tuple(reversed(axes))
    partner = [(i, i ^ 1) for i in range(total)]
    keep = keep + lax.ppermute(send, index_axes, partner)
    bits = [1 << b for b in range(1, total.bit_length() - 1)]
    turned = bits[len(bits) // 2 :] + bits[: len(bits) // 2]
    for lower_bit, upper_bit in zip(bits, turned):
        pairs = [(i, i ^ (upper_bit if i & 1 else lower_bit)) for i in range(total)]
        keep = keep + lax.ppermute(keep, index_axes, pairs)
    other = lax.ppermute(keep, index_axes, partner)
    return jnp.where(
        upper, jnp.concatenate((other, keep)), jnp.concatenate((keep, other))
    )


def pack_rows(parts):
    flat = jnp.concatenate([part.reshape(-1) for part in parts])
    rows = -(-flat.shape[0] // 2048) * 16
    flat = jnp.pad(flat, (0, rows * 128 - flat.shape[0]))
    return flat.reshape(rows, 128)


def unpack_rows(packed, shapes):
    flat = packed.reshape(-1)
    parts = []
    start = 0
    for shape in shapes:
        size = math.prod(shape)
        parts.append(flat[start : start + size].reshape(shape))
        start += size
    return parts


def silu_slope(value):
    sigma = jax.nn.sigmoid(value)
    return sigma * (1.0 + value * (1.0 - sigma))


def wrap_columns(field):
    return jnp.concatenate((field[..., -1:], field, field[..., :1]), axis=-1)


def spread_local(weight, extended_field, shape):
    windows = jnp.stack(
        [
            extended_field[:, 2 - tap_x : 2 - tap_x + shape[1], 2 - tap_z : 2 - tap_z + shape[2]]
            for tap_x in range(3)
            for tap_z in range(3)
        ]
    )
    per_shift = jnp.einsum(
        "toxzy,tsoi->sixzy",
        windows,
        weight.reshape(9, 3, shape[0], shape[0]),
        preferred_element_type=jnp.float32,
    )
    return sum(jnp.roll(per_shift[tap_y], tap_y - 1, axis=3) for tap_y in range(3))


def taps_from_inputs(grad_field, extended_inputs):
    shape = grad_field.shape
    rolled = jnp.stack([jnp.roll(grad_field, tap_y - 1, axis=3) for tap_y in range(3)])
    windows = jnp.stack(
        [
            extended_inputs[:, tap_x : tap_x + shape[1], tap_z : tap_z + shape[2]]
            for tap_x in range(3)
            for tap_z in range(3)
        ]
    )
    taps = jnp.einsum(
        "soxzy,tixzy->tsoi", rolled, windows, preferred_element_type=jnp.float32
    )
    return taps.reshape(3, 3, 3, shape[0], extended_inputs.shape[0])


def per_device(
    features, pre_first, pre_second, w_first, w_second, w_out, b_out, y_target, k_target
):
    count_sky = lax.axis_size("sky")
    count_los = lax.axis_size("los")
    depth_all = pre_first.shape[2] * count_los
    norm_factor = 1.0 / math.sqrt(features.shape[1] * count_sky * features.shape[3] * depth_all)
    shape = features.shape
    first_wide = pre_first.astype(jnp.float32)
    second_wide = pre_second.astype(jnp.float32)
    hidden_second = jax.nn.silu(second_wide).astype(jnp.bfloat16)
    heads_raw = jnp.einsum(
        "oi,ixzy->oxzy", w_out, hidden_second, preferred_element_type=jnp.float32
    )
    heads_raw = heads_raw + b_out[:, None, None, None]
    pressure = jax.nn.softplus(heads_raw[0])
    density = jax.nn.softplus(heads_raw[1])
    velocity = heads_raw[2]
    y_part = jnp.sum(pressure, axis=1) / depth_all
    k_part = -jnp.sum(density * velocity, axis=1) / depth_all
    y_map, k_map = butterfly_sum(jnp.stack((y_part, k_part)), ("los",))
    y_resid = y_map - y_target
    k_resid = k_map - k_target
    y_resid = y_resid[:, None, :]
    k_resid = k_resid[:, None, :]
    head_grad = jnp.stack(
        (
            y_resid * jax.nn.sigmoid(heads_raw[0]),
            -k_resid * velocity * jax.nn.sigmoid(heads_raw[1]),
            -k_resid * density,
        )
    ).astype(jnp.bfloat16)
    grad_out = (
        jnp.einsum("oxzy,ixzy->oi", head_grad, hidden_second, preferred_element_type=jnp.float32)
        * norm_factor
    )
    grad_bias = jnp.sum(head_grad.astype(jnp.float32), axis=(1, 2, 3)) * norm_factor
    back_second = jnp.einsum("oi,oxzy->ixzy", w_out, head_grad, preferred_element_type=jnp.float32)
    grad_second_pre = (back_second * silu_slope(second_wide)).astype(jnp.bfloat16)
    second_padded = extended(grad_second_pre, (("sky", 1), ("los", 2)), 1)
    back_first = spread_local(w_second, second_padded, shape)
    grad_first_pre = (back_first * silu_slope(first_wide)).astype(jnp.bfloat16)
    first_padded = extended(grad_first_pre, (("sky", 1), ("los", 2)), 1)
    grad_features = spread_local(w_first, first_padded, shape).astype(jnp.bfloat16)
    saved_padded = extended(jnp.stack((features, pre_first)), (("sky", 2), ("los", 3)), 1)
    hidden_padded = jax.nn.silu(saved_padded[1].astype(jnp.float32)).astype(jnp.bfloat16)
    grad_second = taps_from_inputs(grad_second_pre, hidden_padded)
    grad_first = taps_from_inputs(grad_first_pre, saved_padded[0])
    reduced = (grad_first * norm_factor, grad_second * norm_factor, grad_out, grad_bias)
    reduced_shapes = [part.shape for part in reduced]
    grad_first, grad_second, grad_out, grad_bias = unpack_rows(
        split_sum(pack_rows(reduced), ("los", "sky")), reduced_shapes
    )
    return (grad_features, grad_first, grad_second, grad_out, grad_bias)


def solution(mesh):
    in_specs = (
        P(None, "sky", "los", None),
        P(None, "sky", "los", None),
        P(None, "sky", "los", None),
        P(),
        P(),
        P(),
        P(),
        P("sky", None),
        P("sky", None),
    )
    out_specs = (P(None, "sky", "los", None), P(), P(), P(), P())
    return jax.shard_map(
        per_device, mesh=mesh, in_specs=in_specs, out_specs=out_specs, check_vma=False
    )
```

```python
import math

import jax
import jax.numpy as jnp
from jax import lax
from jax.sharding import PartitionSpec as P


def extended(block, sides, width):
    for axis, dim in sides:
        count = lax.axis_size(axis)
        forward = [(i, i + 1) for i in range(count - 1)]
        forward.append((count - 1, 0))
        backward = [(target, source) for source, target in forward]
        low = lax.ppermute(
            lax.slice_in_dim(block, block.shape[dim] - width, None, axis=dim), axis, forward
        )
        high = lax.ppermute(lax.slice_in_dim(block, 0, width, axis=dim), axis, backward)
        block = jnp.concatenate([low, block, high], axis=dim)
    return block


def butterfly_sum(value, axes, skip=0):
    for axis in axes:
        count = lax.axis_size(axis)
        if count & (count - 1):
            value = lax.psum(value, axis)
            continue
        step = 2 if skip and axis == axes[0] else 1
        while step < count:
            pairs = [(i, i ^ step) for i in range(count)]
            value = value + lax.ppermute(value, axis, pairs)
            step *= 2
    return value


def split_sum(value, axes):
    sizes = [lax.axis_size(axis) for axis in axes]
    total = math.prod(sizes)
    if total & (total - 1) or sizes[0] % 2:
        return lax.psum(value, axes)
    half = value.shape[0] // 2
    upper = lax.axis_index(axes[0]) % 2 == 1
    keep = jnp.where(upper, value[half:], value[:half])
    send = jnp.where(upper, value[:half], value[half:])
    index_axes = tuple(reversed(axes))
    partner = [(i, i ^ 1) for i in range(total)]
    keep = keep + lax.ppermute(send, index_axes, partner)
    bits = [1 << b for b in range(1, total.bit_length() - 1)]
    turned = bits[len(bits) // 2 :] + bits[: len(bits) // 2]
    for lower_bit, upper_bit in zip(bits, turned):
        pairs = [(i, i ^ (upper_bit if i & 1 else lower_bit)) for i in range(total)]
        keep = keep + lax.ppermute(keep, index_axes, pairs)
    other = lax.ppermute(keep, index_axes, partner)
    return jnp.where(
        upper, jnp.concatenate((other, keep)), jnp.concatenate((keep, other))
    )


def pack_rows(parts):
    flat = jnp.concatenate([part.reshape(-1) for part in parts])
    rows = -(-flat.shape[0] // 2048) * 16
    flat = jnp.pad(flat, (0, rows * 128 - flat.shape[0]))
    return flat.reshape(rows, 128)


def unpack_rows(packed, shapes):
    flat = packed.reshape(-1)
    parts = []
    start = 0
    for shape in shapes:
        size = math.prod(shape)
        parts.append(flat[start : start + size].reshape(shape))
        start += size
    return parts


def silu_slope(value):
    sigma = jax.nn.sigmoid(value)
    return sigma * (1.0 + value * (1.0 - sigma))


def wrap_columns(field):
    return jnp.concatenate((field[..., -1:], field, field[..., :1]), axis=-1)


def spread_local(weight, extended_field, shape):
    windows = jnp.stack(
        [
            extended_field[:, 2 - tap_x : 2 - tap_x + shape[1], 2 - tap_z : 2 - tap_z + shape[2]]
            for tap_x in range(3)
            for tap_z in range(3)
        ]
    )
    per_shift = jnp.einsum(
        "toxzy,tsoi->sixzy",
        windows,
        weight.reshape(9, 3, shape[0], shape[0]),
        preferred_element_type=jnp.float32,
    )
    return sum(jnp.roll(per_shift[tap_y], tap_y - 1, axis=3) for tap_y in range(3))


def taps_from_halo(extended_grad, inputs):
    shape = inputs.shape
    windows = jnp.stack(
        [
            extended_grad[:, 2 - tap_x : 2 - tap_x + shape[1], 2 - tap_z : 2 - tap_z + shape[2]]
            for tap_x in range(3)
            for tap_z in range(3)
        ]
    )
    rolled = jnp.stack([jnp.roll(inputs, 1 - tap_y, axis=3) for tap_y in range(3)])
    taps = jnp.einsum(
        "toxzy,sixzy->tsoi", windows, rolled, preferred_element_type=jnp.float32
    )
    return taps.reshape(3, 3, 3, extended_grad.shape[0], shape[0])


def per_device(
    features, pre_first, pre_second, w_first, w_second, w_out, b_out, y_target, k_target
):
    count_sky = lax.axis_size("sky")
    count_los = lax.axis_size("los")
    depth_all = pre_first.shape[2] * count_los
    norm_factor = 1.0 / math.sqrt(features.shape[1] * count_sky * features.shape[3] * depth_all)
    shape = features.shape
    first_wide = pre_first.astype(jnp.float32)
    second_wide = pre_second.astype(jnp.float32)
    hidden_second = jax.nn.silu(second_wide).astype(jnp.bfloat16)
    heads_raw = jnp.einsum(
        "oi,ixzy->oxzy", w_out, hidden_second, preferred_element_type=jnp.float32
    )
    heads_raw = heads_raw + b_out[:, None, None, None]
    pressure = jax.nn.softplus(heads_raw[0])
    density = jax.nn.softplus(heads_raw[1])
    velocity = heads_raw[2]
    y_part = jnp.sum(pressure, axis=1) / depth_all
    k_part = -jnp.sum(density * velocity, axis=1) / depth_all
    y_map, k_map = butterfly_sum(jnp.stack((y_part, k_part)), ("los",))
    y_resid = y_map - y_target
    k_resid = k_map - k_target
    y_resid = y_resid[:, None, :]
    k_resid = k_resid[:, None, :]
    head_grad = jnp.stack(
        (
            y_resid * jax.nn.sigmoid(heads_raw[0]),
            -k_resid * velocity * jax.nn.sigmoid(heads_raw[1]),
            -k_resid * density,
        )
    ).astype(jnp.bfloat16)
    grad_out = (
        jnp.einsum("oxzy,ixzy->oi", head_grad, hidden_second, preferred_element_type=jnp.float32)
        * norm_factor
    )
    grad_bias = jnp.sum(head_grad.astype(jnp.float32), axis=(1, 2, 3)) * norm_factor
    back_second = jnp.einsum("oi,oxzy->ixzy", w_out, head_grad, preferred_element_type=jnp.float32)
    grad_second_pre = (back_second * silu_slope(second_wide)).astype(jnp.bfloat16)
    second_padded = extended(grad_second_pre, (("sky", 1), ("los", 2)), 1)
    back_first = spread_local(w_second, second_padded, shape)
    grad_first_pre = (back_first * silu_slope(first_wide)).astype(jnp.bfloat16)
    first_padded = extended(grad_first_pre, (("sky", 1), ("los", 2)), 1)
    grad_features = spread_local(w_first, first_padded, shape).astype(jnp.bfloat16)
    hidden_first = jax.nn.silu(first_wide).astype(jnp.bfloat16)
    grad_second = taps_from_halo(second_padded, hidden_first)
    grad_first = taps_from_halo(first_padded, features)
    reduced = (grad_first * norm_factor, grad_second * norm_factor, grad_out, grad_bias)
    reduced_shapes = [part.shape for part in reduced]
    grad_first, grad_second, grad_out, grad_bias = unpack_rows(
        split_sum(pack_rows(reduced), ("los", "sky")), reduced_shapes
    )
    return (grad_features, grad_first, grad_second, grad_out, grad_bias)


def solution(mesh):
    in_specs = (
        P(None, "sky", "los", None),
        P(None, "sky", "los", None),
        P(None, "sky", "los", None),
        P(),
        P(),
        P(),
        P(),
        P("sky", None),
        P("sky", None),
    )
    out_specs = (P(None, "sky", "los", None), P(), P(), P(), P())
    return jax.shard_map(
        per_device, mesh=mesh, in_specs=in_specs, out_specs=out_specs, check_vma=False
    )
```

```python
import math

import jax
import jax.numpy as jnp
from jax import lax
from jax.sharding import PartitionSpec as P


def extended(block, sides, width):
    for axis, dim in sides:
        count = lax.axis_size(axis)
        forward = [(i, i + 1) for i in range(count - 1)]
        forward.append((count - 1, 0))
        backward = [(target, source) for source, target in forward]
        low = lax.ppermute(
            lax.slice_in_dim(block, block.shape[dim] - width, None, axis=dim), axis, forward
        )
        high = lax.ppermute(lax.slice_in_dim(block, 0, width, axis=dim), axis, backward)
        block = jnp.concatenate([low, block, high], axis=dim)
    return block


def butterfly_sum(value, axes, skip=0):
    for axis in axes:
        count = lax.axis_size(axis)
        if count & (count - 1):
            value = lax.psum(value, axis)
            continue
        step = 2 if skip and axis == axes[0] else 1
        while step < count:
            pairs = [(i, i ^ step) for i in range(count)]
            value = value + lax.ppermute(value, axis, pairs)
            step *= 2
    return value


def split_sum(value, axes):
    sizes = [lax.axis_size(axis) for axis in axes]
    total = math.prod(sizes)
    if total & (total - 1) or sizes[0] % 2:
        return lax.psum(value, axes)
    half = value.shape[0] // 2
    upper = lax.axis_index(axes[0]) % 2 == 1
    keep = jnp.where(upper, value[half:], value[:half])
    send = jnp.where(upper, value[:half], value[half:])
    index_axes = tuple(reversed(axes))
    partner = [(i, i ^ 1) for i in range(total)]
    keep = keep + lax.ppermute(send, index_axes, partner)
    bits = [1 << b for b in range(1, total.bit_length() - 1)]
    turned = bits[len(bits) // 2 :] + bits[: len(bits) // 2]
    for lower_bit, upper_bit in zip(bits, turned):
        pairs = [(i, i ^ (upper_bit if i & 1 else lower_bit)) for i in range(total)]
        keep = keep + lax.ppermute(keep, index_axes, pairs)
    other = lax.ppermute(keep, index_axes, partner)
    return jnp.where(
        upper, jnp.concatenate((other, keep)), jnp.concatenate((keep, other))
    )


def pack_rows(parts):
    flat = jnp.concatenate([part.reshape(-1) for part in parts])
    rows = -(-flat.shape[0] // 2048) * 16
    flat = jnp.pad(flat, (0, rows * 128 - flat.shape[0]))
    return flat.reshape(rows, 128)


def unpack_rows(packed, shapes):
    flat = packed.reshape(-1)
    parts = []
    start = 0
    for shape in shapes:
        size = math.prod(shape)
        parts.append(flat[start : start + size].reshape(shape))
        start += size
    return parts


def silu_slope(value):
    sigma = jax.nn.sigmoid(value)
    return sigma * (1.0 + value * (1.0 - sigma))


def wrap_columns(field):
    return jnp.concatenate((field[..., -1:], field, field[..., :1]), axis=-1)


def spread_local(weight, extended_field, shape):
    windows = jnp.stack(
        [
            extended_field[:, 2 - tap_x : 2 - tap_x + shape[1], 2 - tap_z : 2 - tap_z + shape[2]]
            for tap_x in range(3)
            for tap_z in range(3)
        ]
    )
    per_shift = jnp.einsum(
        "toxzy,tsoi->sixzy",
        windows,
        weight.reshape(9, 3, shape[0], shape[0]),
        preferred_element_type=jnp.float32,
    )
    return sum(jnp.roll(per_shift[tap_y], tap_y - 1, axis=3) for tap_y in range(3))


def taps_from_halo(extended_grad, inputs):
    shape = inputs.shape
    windows = jnp.stack(
        [
            extended_grad[:, 2 - tap_x : 2 - tap_x + shape[1], 2 - tap_z : 2 - tap_z + shape[2]]
            for tap_x in range(3)
            for tap_z in range(3)
        ]
    )
    rolled = jnp.stack([jnp.roll(inputs, 1 - tap_y, axis=3) for tap_y in range(3)])
    taps = jnp.einsum(
        "toxzy,sixzy->tsoi", windows, rolled, preferred_element_type=jnp.float32
    )
    return taps.reshape(3, 3, 3, extended_grad.shape[0], shape[0])


def per_device(
    features, pre_first, pre_second, w_first, w_second, w_out, b_out, y_target, k_target
):
    count_sky = lax.axis_size("sky")
    count_los = lax.axis_size("los")
    depth_all = pre_first.shape[2] * count_los
    norm_factor = 1.0 / math.sqrt(features.shape[1] * count_sky * features.shape[3] * depth_all)
    shape = features.shape
    first_wide = pre_first.astype(jnp.float32)
    second_wide = pre_second.astype(jnp.float32)
    hidden_second = jax.nn.silu(second_wide).astype(jnp.bfloat16)
    heads_raw = jnp.einsum(
        "oi,ixzy->oxzy", w_out, hidden_second, preferred_element_type=jnp.float32
    )
    heads_raw = heads_raw + b_out[:, None, None, None]
    pressure = jax.nn.softplus(heads_raw[0])
    density = jax.nn.softplus(heads_raw[1])
    velocity = heads_raw[2]
    y_part = jnp.sum(pressure, axis=1) / depth_all
    k_part = -jnp.sum(density * velocity, axis=1) / depth_all
    y_map, k_map = butterfly_sum(jnp.stack((y_part, k_part)), ("los",))
    y_resid = y_map - y_target
    k_resid = k_map - k_target
    y_resid = y_resid[:, None, :]
    k_resid = k_resid[:, None, :]
    head_grad = jnp.stack(
        (
            y_resid * jax.nn.sigmoid(heads_raw[0]),
            -k_resid * velocity * jax.nn.sigmoid(heads_raw[1]),
            -k_resid * density,
        )
    ).astype(jnp.bfloat16)
    grad_out = (
        jnp.einsum("oxzy,ixzy->oi", head_grad, hidden_second, preferred_element_type=jnp.float32)
        * norm_factor
    )
    grad_bias = jnp.sum(head_grad.astype(jnp.float32), axis=(1, 2, 3)) * norm_factor
    back_second = jnp.einsum("oi,oxzy->ixzy", w_out, head_grad, preferred_element_type=jnp.float32)
    grad_second_pre = (back_second * silu_slope(second_wide)).astype(jnp.bfloat16)
    both_wide = extended(jnp.stack((grad_second_pre, pre_first)), (("sky", 2), ("los", 3)), 2)
    second_padded = both_wide[0, :, 1:-1, 1:-1]
    first_around = both_wide[1, :, 1:-1, 1:-1].astype(jnp.float32)
    around_shape = first_around.shape
    back_first = spread_local(w_second, both_wide[0], around_shape)
    first_padded = (back_first * silu_slope(first_around)).astype(jnp.bfloat16)
    grad_features = spread_local(w_first, first_padded, shape).astype(jnp.bfloat16)
    hidden_first = jax.nn.silu(first_wide).astype(jnp.bfloat16)
    grad_second = taps_from_halo(second_padded, hidden_first)
    grad_first = taps_from_halo(first_padded, features)
    reduced = (grad_first * norm_factor, grad_second * norm_factor, grad_out, grad_bias)
    reduced_shapes = [part.shape for part in reduced]
    grad_first, grad_second, grad_out, grad_bias = unpack_rows(
        split_sum(pack_rows(reduced), ("los", "sky")), reduced_shapes
    )
    return (grad_features, grad_first, grad_second, grad_out, grad_bias)


def solution(mesh):
    in_specs = (
        P(None, "sky", "los", None),
        P(None, "sky", "los", None),
        P(None, "sky", "los", None),
        P(),
        P(),
        P(),
        P(),
        P("sky", None),
        P("sky", None),
    )
    out_specs = (P(None, "sky", "los", None), P(), P(), P(), P())
    return jax.shard_map(
        per_device, mesh=mesh, in_specs=in_specs, out_specs=out_specs, check_vma=False
    )
```

```python
import math

import jax
import jax.numpy as jnp
from jax import lax
from jax.sharding import PartitionSpec as P


def extended(block, sides, width):
    for axis, dim in sides:
        count = lax.axis_size(axis)
        forward = [(i, i + 1) for i in range(count - 1)]
        forward.append((count - 1, 0))
        backward = [(target, source) for source, target in forward]
        low = lax.ppermute(
            lax.slice_in_dim(block, block.shape[dim] - width, None, axis=dim), axis, forward
        )
        high = lax.ppermute(lax.slice_in_dim(block, 0, width, axis=dim), axis, backward)
        block = jnp.concatenate([low, block, high], axis=dim)
    return block


def butterfly_sum(value, axes, skip=0):
    for axis in axes:
        count = lax.axis_size(axis)
        if count & (count - 1):
            value = lax.psum(value, axis)
            continue
        step = 2 if skip and axis == axes[0] else 1
        while step < count:
            pairs = [(i, i ^ step) for i in range(count)]
            value = value + lax.ppermute(value, axis, pairs)
            step *= 2
    return value


def quad_sum(value, axis):
    count = lax.axis_size(axis)
    if count & (count - 1):
        return lax.psum(value, axis)
    step = 1
    while step < count:
        if step * 2 >= count:
            value = value + lax.ppermute(value, axis, [(i, i ^ step) for i in range(count)])
            break
        near, far, both = (
            lax.ppermute(value, axis, [(i, i ^ mask) for i in range(count)])
            for mask in (step, step * 2, step * 3)
        )
        value = (value + near) + (far + both)
        step *= 4
    return value


def split_sum(value, axes):
    sizes = [lax.axis_size(axis) for axis in axes]
    total = math.prod(sizes)
    if total & (total - 1) or sizes[0] % 2:
        return lax.psum(value, axes)
    half = value.shape[0] // 2
    upper = lax.axis_index(axes[0]) % 2 == 1
    keep = jnp.where(upper, value[half:], value[:half])
    send = jnp.where(upper, value[:half], value[half:])
    index_axes = tuple(reversed(axes))
    partner = [(i, i ^ 1) for i in range(total)]
    keep = keep + lax.ppermute(send, index_axes, partner)
    bits = [1 << b for b in range(1, total.bit_length() - 1)]
    turned = bits[len(bits) // 2 :] + bits[: len(bits) // 2]
    for lower_bit, upper_bit in zip(bits, turned):
        pairs = [(i, i ^ (upper_bit if i & 1 else lower_bit)) for i in range(total)]
        keep = keep + lax.ppermute(keep, index_axes, pairs)
    other = lax.ppermute(keep, index_axes, partner)
    return jnp.where(
        upper, jnp.concatenate((other, keep)), jnp.concatenate((keep, other))
    )


def pack_rows(parts):
    flat = jnp.concatenate([part.reshape(-1) for part in parts])
    rows = -(-flat.shape[0] // 2048) * 16
    flat = jnp.pad(flat, (0, rows * 128 - flat.shape[0]))
    return flat.reshape(rows, 128)


def unpack_rows(packed, shapes):
    flat = packed.reshape(-1)
    parts = []
    start = 0
    for shape in shapes:
        size = math.prod(shape)
        parts.append(flat[start : start + size].reshape(shape))
        start += size
    return parts


def silu_slope(value):
    sigma = jax.nn.sigmoid(value)
    return sigma * (1.0 + value * (1.0 - sigma))


def wrap_columns(field):
    return jnp.concatenate((field[..., -1:], field, field[..., :1]), axis=-1)


def spread_local(weight, extended_field, shape):
    windows = jnp.stack(
        [
            extended_field[:, 2 - tap_x : 2 - tap_x + shape[1], 2 - tap_z : 2 - tap_z + shape[2]]
            for tap_x in range(3)
            for tap_z in range(3)
        ]
    )
    per_shift = jnp.einsum(
        "toxzy,tsoi->sixzy",
        windows,
        weight.reshape(9, 3, shape[0], shape[0]),
        preferred_element_type=jnp.float32,
    )
    return sum(jnp.roll(per_shift[tap_y], tap_y - 1, axis=3) for tap_y in range(3))


def taps_from_halo(extended_grad, inputs):
    shape = inputs.shape
    windows = jnp.stack(
        [
            extended_grad[:, 2 - tap_x : 2 - tap_x + shape[1], 2 - tap_z : 2 - tap_z + shape[2]]
            for tap_x in range(3)
            for tap_z in range(3)
        ]
    )
    rolled = jnp.stack([jnp.roll(inputs, 1 - tap_y, axis=3) for tap_y in range(3)])
    taps = jnp.einsum(
        "toxzy,sixzy->tsoi", windows, rolled, preferred_element_type=jnp.float32
    )
    return taps.reshape(3, 3, 3, extended_grad.shape[0], shape[0])


def per_device(
    features, pre_first, pre_second, w_first, w_second, w_out, b_out, y_target, k_target
):
    count_sky = lax.axis_size("sky")
    count_los = lax.axis_size("los")
    depth_all = pre_first.shape[2] * count_los
    norm_factor = 1.0 / math.sqrt(features.shape[1] * count_sky * features.shape[3] * depth_all)
    shape = features.shape
    first_wide = pre_first.astype(jnp.float32)
    second_wide = pre_second.astype(jnp.float32)
    hidden_second = jax.nn.silu(second_wide).astype(jnp.bfloat16)
    heads_raw = jnp.einsum(
        "oi,ixzy->oxzy", w_out, hidden_second, preferred_element_type=jnp.float32
    )
    heads_raw = heads_raw + b_out[:, None, None, None]
    pressure = jax.nn.softplus(heads_raw[0])
    density = jax.nn.softplus(heads_raw[1])
    velocity = heads_raw[2]
    y_part = jnp.sum(pressure, axis=1) / depth_all
    k_part = -jnp.sum(density * velocity, axis=1) / depth_all
    y_map, k_map = quad_sum(jnp.stack((y_part, k_part)), "los")
    y_resid = y_map - y_target
    k_resid = k_map - k_target
    y_resid = y_resid[:, None, :]
    k_resid = k_resid[:, None, :]
    head_grad = jnp.stack(
        (
            y_resid * jax.nn.sigmoid(heads_raw[0]),
            -k_resid * velocity * jax.nn.sigmoid(heads_raw[1]),
            -k_resid * density,
        )
    ).astype(jnp.bfloat16)
    grad_out = (
        jnp.einsum("oxzy,ixzy->oi", head_grad, hidden_second, preferred_element_type=jnp.float32)
        * norm_factor
    )
    grad_bias = jnp.sum(head_grad.astype(jnp.float32), axis=(1, 2, 3)) * norm_factor
    back_second = jnp.einsum("oi,oxzy->ixzy", w_out, head_grad, preferred_element_type=jnp.float32)
    grad_second_pre = (back_second * silu_slope(second_wide)).astype(jnp.bfloat16)
    second_padded = extended(grad_second_pre, (("sky", 1), ("los", 2)), 1)
    back_first = spread_local(w_second, second_padded, shape)
    grad_first_pre = (back_first * silu_slope(first_wide)).astype(jnp.bfloat16)
    first_padded = extended(grad_first_pre, (("sky", 1), ("los", 2)), 1)
    grad_features = spread_local(w_first, first_padded, shape).astype(jnp.bfloat16)
    hidden_first = jax.nn.silu(first_wide).astype(jnp.bfloat16)
    grad_second = taps_from_halo(second_padded, hidden_first)
    grad_first = taps_from_halo(first_padded, features)
    reduced = (grad_first * norm_factor, grad_second * norm_factor, grad_out, grad_bias)
    reduced_shapes = [part.shape for part in reduced]
    grad_first, grad_second, grad_out, grad_bias = unpack_rows(
        split_sum(pack_rows(reduced), ("los", "sky")), reduced_shapes
    )
    return (grad_features, grad_first, grad_second, grad_out, grad_bias)


def solution(mesh):
    in_specs = (
        P(None, "sky", "los", None),
        P(None, "sky", "los", None),
        P(None, "sky", "los", None),
        P(),
        P(),
        P(),
        P(),
        P("sky", None),
        P("sky", None),
    )
    out_specs = (P(None, "sky", "los", None), P(), P(), P(), P())
    return jax.shard_map(
        per_device, mesh=mesh, in_specs=in_specs, out_specs=out_specs, check_vma=False
    )
```

```python
import math

import jax
import jax.numpy as jnp
from jax import lax
from jax.sharding import PartitionSpec as P


def extended(block, sides, width):
    for axis, dim in sides:
        count = lax.axis_size(axis)
        forward = [(i, i + 1) for i in range(count - 1)]
        forward.append((count - 1, 0))
        backward = [(target, source) for source, target in forward]
        low = lax.ppermute(
            lax.slice_in_dim(block, block.shape[dim] - width, None, axis=dim), axis, forward
        )
        high = lax.ppermute(lax.slice_in_dim(block, 0, width, axis=dim), axis, backward)
        block = jnp.concatenate([low, block, high], axis=dim)
    return block


def butterfly_sum(value, axes, skip=0):
    for axis in axes:
        count = lax.axis_size(axis)
        if count & (count - 1):
            value = lax.psum(value, axis)
            continue
        step = 2 if skip and axis == axes[0] else 1
        while step < count:
            pairs = [(i, i ^ step) for i in range(count)]
            value = value + lax.ppermute(value, axis, pairs)
            step *= 2
    return value


def quad_sum(value, axis):
    count = lax.axis_size(axis)
    if count & (count - 1):
        return lax.psum(value, axis)
    step = 1
    while step < count:
        if step * 2 >= count:
            value = value + lax.ppermute(value, axis, [(i, i ^ step) for i in range(count)])
            break
        near, far, both = (
            lax.ppermute(value, axis, [(i, i ^ mask) for i in range(count)])
            for mask in (step, step * 2, step * 3)
        )
        value = (value + near) + (far + both)
        step *= 4
    return value


def split_sum(value, axes):
    sizes = [lax.axis_size(axis) for axis in axes]
    total = math.prod(sizes)
    if total & (total - 1) or sizes[0] % 2:
        return lax.psum(value, axes)
    half = value.shape[0] // 2
    upper = lax.axis_index(axes[0]) % 2 == 1
    keep = jnp.where(upper, value[half:], value[:half])
    send = jnp.where(upper, value[:half], value[half:])
    index_axes = tuple(reversed(axes))
    partner = [(i, i ^ 1) for i in range(total)]
    keep = keep + lax.ppermute(send, index_axes, partner)
    bits = [1 << b for b in range(1, total.bit_length() - 1)]
    turned = bits[len(bits) // 2 :] + bits[: len(bits) // 2]
    for lower_bit, upper_bit in zip(bits, turned):
        pairs = [(i, i ^ (upper_bit if i & 1 else lower_bit)) for i in range(total)]
        keep = keep + lax.ppermute(keep, index_axes, pairs)
    other = lax.ppermute(keep, index_axes, partner)
    return jnp.where(
        upper, jnp.concatenate((other, keep)), jnp.concatenate((keep, other))
    )


def row_count(shape):
    return -(-math.prod(shape) // 128)


def pack_rows(parts):
    blocks = []
    for part in parts:
        size = math.prod(part.shape)
        rows = row_count(part.shape)
        flat = part.reshape(-1)
        if rows * 128 != size:
            flat = jnp.pad(flat, (0, rows * 128 - size))
        blocks.append(flat.reshape(rows, 128))
    total = sum(block.shape[0] for block in blocks)
    blocks.append(jnp.zeros((-(-total // 16) * 16 - total, 128), jnp.float32))
    return jnp.concatenate(blocks)


def unpack_rows(packed, shapes):
    parts = []
    start = 0
    for shape in shapes:
        size = math.prod(shape)
        rows = row_count(shape)
        block = packed[start : start + rows]
        if rows * 128 != size:
            block = block.reshape(-1)[:size]
        parts.append(block.reshape(shape))
        start += rows
    return parts


def silu_slope(value):
    sigma = jax.nn.sigmoid(value)
    return sigma * (1.0 + value * (1.0 - sigma))


def wrap_columns(field):
    return jnp.concatenate((field[..., -1:], field, field[..., :1]), axis=-1)


def spread_local(weight, extended_field, shape):
    windows = jnp.stack(
        [
            extended_field[:, 2 - tap_x : 2 - tap_x + shape[1], 2 - tap_z : 2 - tap_z + shape[2]]
            for tap_x in range(3)
            for tap_z in range(3)
        ]
    )
    per_shift = jnp.einsum(
        "toxzy,tsoi->sixzy",
        windows,
        weight.reshape(9, 3, shape[0], shape[0]),
        preferred_element_type=jnp.float32,
    )
    return sum(jnp.roll(per_shift[tap_y], tap_y - 1, axis=3) for tap_y in range(3))


def taps_from_halo(extended_grad, inputs):
    shape = inputs.shape
    windows = jnp.stack(
        [
            extended_grad[:, 2 - tap_x : 2 - tap_x + shape[1], 2 - tap_z : 2 - tap_z + shape[2]]
            for tap_x in range(3)
            for tap_z in range(3)
        ]
    )
    rolled = jnp.stack([jnp.roll(inputs, 1 - tap_y, axis=3) for tap_y in range(3)])
    taps = jnp.einsum(
        "toxzy,sixzy->tsoi", windows, rolled, preferred_element_type=jnp.float32
    )
    return taps.reshape(3, 3, 3, extended_grad.shape[0], shape[0])


def per_device(
    features, pre_first, pre_second, w_first, w_second, w_out, b_out, y_target, k_target
):
    count_sky = lax.axis_size("sky")
    count_los = lax.axis_size("los")
    depth_all = pre_first.shape[2] * count_los
    norm_factor = 1.0 / math.sqrt(features.shape[1] * count_sky * features.shape[3] * depth_all)
    shape = features.shape
    first_wide = pre_first.astype(jnp.float32)
    second_wide = pre_second.astype(jnp.float32)
    hidden_second = jax.nn.silu(second_wide).astype(jnp.bfloat16)
    heads_raw = jnp.einsum(
        "oi,ixzy->oxzy", w_out, hidden_second, preferred_element_type=jnp.float32
    )
    heads_raw = heads_raw + b_out[:, None, None, None]
    pressure = jax.nn.softplus(heads_raw[0])
    density = jax.nn.softplus(heads_raw[1])
    velocity = heads_raw[2]
    y_part = jnp.sum(pressure, axis=1) / depth_all
    k_part = -jnp.sum(density * velocity, axis=1) / depth_all
    y_map, k_map = quad_sum(jnp.stack((y_part, k_part)), "los")
    y_resid = y_map - y_target
    k_resid = k_map - k_target
    y_resid = y_resid[:, None, :]
    k_resid = k_resid[:, None, :]
    head_grad = jnp.stack(
        (
            y_resid * jax.nn.sigmoid(heads_raw[0]),
            -k_resid * velocity * jax.nn.sigmoid(heads_raw[1]),
            -k_resid * density,
        )
    ).astype(jnp.bfloat16)
    grad_out = (
        jnp.einsum("oxzy,ixzy->oi", head_grad, hidden_second, preferred_element_type=jnp.float32)
        * norm_factor
    )
    grad_bias = jnp.sum(head_grad.astype(jnp.float32), axis=(1, 2, 3)) * norm_factor
    back_second = jnp.einsum("oi,oxzy->ixzy", w_out, head_grad, preferred_element_type=jnp.float32)
    grad_second_pre = (back_second * silu_slope(second_wide)).astype(jnp.bfloat16)
    second_padded = extended(grad_second_pre, (("sky", 1), ("los", 2)), 1)
    back_first = spread_local(w_second, second_padded, shape)
    grad_first_pre = (back_first * silu_slope(first_wide)).astype(jnp.bfloat16)
    first_padded = extended(grad_first_pre, (("sky", 1), ("los", 2)), 1)
    grad_features = spread_local(w_first, first_padded, shape).astype(jnp.bfloat16)
    hidden_first = jax.nn.silu(first_wide).astype(jnp.bfloat16)
    grad_second = taps_from_halo(second_padded, hidden_first)
    grad_first = taps_from_halo(first_padded, features)
    reduced = (grad_first * norm_factor, grad_second * norm_factor, grad_out, grad_bias)
    reduced_shapes = [part.shape for part in reduced]
    grad_first, grad_second, grad_out, grad_bias = unpack_rows(
        split_sum(pack_rows(reduced), ("los", "sky")), reduced_shapes
    )
    return (grad_features, grad_first, grad_second, grad_out, grad_bias)


def solution(mesh):
    in_specs = (
        P(None, "sky", "los", None),
        P(None, "sky", "los", None),
        P(None, "sky", "los", None),
        P(),
        P(),
        P(),
        P(),
        P("sky", None),
        P("sky", None),
    )
    out_specs = (P(None, "sky", "los", None), P(), P(), P(), P())
    return jax.shard_map(
        per_device, mesh=mesh, in_specs=in_specs, out_specs=out_specs, check_vma=False
    )
```

```python
import math

import jax
import jax.numpy as jnp
from jax import lax
from jax.sharding import PartitionSpec as P


def extended(block, sides, width):
    for axis, dim in sides:
        count = lax.axis_size(axis)
        forward = [(i, i + 1) for i in range(count - 1)]
        forward.append((count - 1, 0))
        backward = [(target, source) for source, target in forward]
        low = lax.ppermute(
            lax.slice_in_dim(block, block.shape[dim] - width, None, axis=dim), axis, forward
        )
        high = lax.ppermute(lax.slice_in_dim(block, 0, width, axis=dim), axis, backward)
        block = jnp.concatenate([low, block, high], axis=dim)
    return block


def butterfly_sum(value, axes, skip=0):
    for axis in axes:
        count = lax.axis_size(axis)
        if count & (count - 1):
            value = lax.psum(value, axis)
            continue
        step = 2 if skip and axis == axes[0] else 1
        while step < count:
            pairs = [(i, i ^ step) for i in range(count)]
            value = value + lax.ppermute(value, axis, pairs)
            step *= 2
    return value


def quad_sum(value, axis):
    count = lax.axis_size(axis)
    if count & (count - 1):
        return lax.psum(value, axis)
    step = 1
    while step < count:
        if step * 2 >= count:
            value = value + lax.ppermute(value, axis, [(i, i ^ step) for i in range(count)])
            break
        near, far, both = (
            lax.ppermute(value, axis, [(i, i ^ mask) for i in range(count)])
            for mask in (step, step * 2, step * 3)
        )
        value = (value + near) + (far + both)
        step *= 4
    return value


def split_sum(value, axes):
    sizes = [lax.axis_size(axis) for axis in axes]
    total = math.prod(sizes)
    if total & (total - 1) or sizes[0] % 2:
        return lax.psum(value, axes)
    half = value.shape[0] // 2
    upper = lax.axis_index(axes[0]) % 2 == 1
    keep = jnp.where(upper, value[half:], value[:half])
    send = jnp.where(upper, value[:half], value[half:])
    index_axes = tuple(reversed(axes))
    partner = [(i, i ^ 1) for i in range(total)]
    keep = keep + lax.ppermute(send, index_axes, partner)
    bits = [1 << b for b in range(1, total.bit_length() - 1)]
    turned = bits[len(bits) // 2 :] + bits[: len(bits) // 2]
    for lower_bit, upper_bit in zip(bits, turned):
        pairs = [(i, i ^ (upper_bit if i & 1 else lower_bit)) for i in range(total)]
        keep = keep + lax.ppermute(keep, index_axes, pairs)
    other = lax.ppermute(keep, index_axes, partner)
    return jnp.where(
        upper, jnp.concatenate((other, keep)), jnp.concatenate((keep, other))
    )


def row_count(shape):
    return -(-math.prod(shape) // 128)


def pack_rows(parts):
    blocks = []
    for part in parts:
        size = math.prod(part.shape)
        rows = row_count(part.shape)
        flat = part.reshape(-1)
        if rows * 128 != size:
            flat = jnp.pad(flat, (0, rows * 128 - size))
        blocks.append(flat.reshape(rows, 128))
    total = sum(block.shape[0] for block in blocks)
    blocks.append(jnp.zeros((-(-total // 16) * 16 - total, 128), jnp.float32))
    return jnp.concatenate(blocks)


def unpack_rows(packed, shapes):
    parts = []
    start = 0
    for shape in shapes:
        size = math.prod(shape)
        rows = row_count(shape)
        block = packed[start : start + rows]
        if rows * 128 != size:
            block = block.reshape(-1)[:size]
        parts.append(block.reshape(shape))
        start += rows
    return parts


def silu_slope(value):
    sigma = jax.nn.sigmoid(value)
    return sigma * (1.0 + value * (1.0 - sigma))


def wrap_columns(field):
    return jnp.concatenate((field[..., -1:], field, field[..., :1]), axis=-1)


def spread_local(weight, extended_field, shape):
    windows = jnp.stack(
        [
            extended_field[:, 2 - tap_x : 2 - tap_x + shape[1], 2 - tap_z : 2 - tap_z + shape[2]]
            for tap_x in range(3)
            for tap_z in range(3)
        ]
    )
    per_shift = jnp.einsum(
        "toxzy,tsoi->sixzy",
        windows,
        weight.reshape(9, 3, shape[0], shape[0]),
        preferred_element_type=jnp.float32,
    )
    return sum(jnp.roll(per_shift[tap_y], tap_y - 1, axis=3) for tap_y in range(3))


def taps_from_halo(extended_grad, inputs):
    shape = inputs.shape
    windows = jnp.stack(
        [
            extended_grad[:, 2 - tap_x : 2 - tap_x + shape[1], 2 - tap_z : 2 - tap_z + shape[2]]
            for tap_x in range(3)
            for tap_z in range(3)
        ]
    )
    rolled = jnp.stack([jnp.roll(inputs, 1 - tap_y, axis=3) for tap_y in range(3)])
    taps = jnp.einsum(
        "toxzy,sixzy->tsoi", windows, rolled, preferred_element_type=jnp.float32
    )
    return taps.reshape(3, 3, 3, extended_grad.shape[0], shape[0])


def per_device(
    features, pre_first, pre_second, w_first, w_second, w_out, b_out, y_target, k_target
):
    count_sky = lax.axis_size("sky")
    count_los = lax.axis_size("los")
    depth_all = pre_first.shape[2] * count_los
    norm_factor = 1.0 / math.sqrt(features.shape[1] * count_sky * features.shape[3] * depth_all)
    shape = features.shape
    first_wide = pre_first.astype(jnp.float32)
    second_wide = pre_second.astype(jnp.float32)
    hidden_second = jax.nn.silu(second_wide).astype(jnp.bfloat16)
    heads_raw = jnp.einsum(
        "oi,ixzy->oxzy", w_out, hidden_second, preferred_element_type=jnp.float32
    )
    heads_raw = heads_raw + b_out[:, None, None, None]
    pressure = jax.nn.softplus(heads_raw[0])
    density = jax.nn.softplus(heads_raw[1])
    velocity = heads_raw[2]
    y_part = jnp.sum(pressure, axis=1) / depth_all
    k_part = -jnp.sum(density * velocity, axis=1) / depth_all
    y_map, k_map = quad_sum(jnp.stack((y_part, k_part)), "los")
    y_resid = y_map - y_target
    k_resid = k_map - k_target
    y_resid = y_resid[:, None, :]
    k_resid = k_resid[:, None, :]
    head_grad = jnp.stack(
        (
            y_resid * jax.nn.sigmoid(heads_raw[0]),
            -k_resid * velocity * jax.nn.sigmoid(heads_raw[1]),
            -k_resid * density,
        )
    ).astype(jnp.bfloat16)
    grad_out = (
        jnp.einsum("oxzy,ixzy->oi", head_grad, hidden_second, preferred_element_type=jnp.float32)
        * norm_factor
    )
    grad_bias = jnp.sum(head_grad.astype(jnp.float32), axis=(1, 2, 3)) * norm_factor
    back_second = jnp.einsum("oi,oxzy->ixzy", w_out, head_grad, preferred_element_type=jnp.float32)
    grad_second_pre = (back_second * silu_slope(second_wide)).astype(jnp.bfloat16)
    second_padded = extended(grad_second_pre, (("los", 2), ("sky", 1)), 1)
    back_first = spread_local(w_second, second_padded, shape)
    grad_first_pre = (back_first * silu_slope(first_wide)).astype(jnp.bfloat16)
    first_padded = extended(grad_first_pre, (("los", 2), ("sky", 1)), 1)
    grad_features = spread_local(w_first, first_padded, shape).astype(jnp.bfloat16)
    hidden_first = jax.nn.silu(first_wide).astype(jnp.bfloat16)
    grad_second = taps_from_halo(second_padded, hidden_first)
    grad_first = taps_from_halo(first_padded, features)
    reduced = (grad_first * norm_factor, grad_second * norm_factor, grad_out, grad_bias)
    reduced_shapes = [part.shape for part in reduced]
    grad_first, grad_second, grad_out, grad_bias = unpack_rows(
        split_sum(pack_rows(reduced), ("los", "sky")), reduced_shapes
    )
    return (grad_features, grad_first, grad_second, grad_out, grad_bias)


def solution(mesh):
    in_specs = (
        P(None, "sky", "los", None),
        P(None, "sky", "los", None),
        P(None, "sky", "los", None),
        P(),
        P(),
        P(),
        P(),
        P("sky", None),
        P("sky", None),
    )
    out_specs = (P(None, "sky", "los", None), P(), P(), P(), P())
    return jax.shard_map(
        per_device, mesh=mesh, in_specs=in_specs, out_specs=out_specs, check_vma=False
    )
```

```python
import math

import jax
import jax.numpy as jnp
from jax import lax
from jax.sharding import PartitionSpec as P


def extended(block, sides, width):
    for axis, dim in sides:
        count = lax.axis_size(axis)
        forward = [(i, i + 1) for i in range(count - 1)]
        forward.append((count - 1, 0))
        backward = [(target, source) for source, target in forward]
        low = lax.ppermute(
            lax.slice_in_dim(block, block.shape[dim] - width, None, axis=dim), axis, forward
        )
        high = lax.ppermute(lax.slice_in_dim(block, 0, width, axis=dim), axis, backward)
        block = jnp.concatenate([low, block, high], axis=dim)
    return block


def butterfly_sum(value, axes, skip=0):
    for axis in axes:
        count = lax.axis_size(axis)
        if count & (count - 1):
            value = lax.psum(value, axis)
            continue
        step = 2 if skip and axis == axes[0] else 1
        while step < count:
            pairs = [(i, i ^ step) for i in range(count)]
            value = value + lax.ppermute(value, axis, pairs)
            step *= 2
    return value


def quad_sum(value, axis):
    count = lax.axis_size(axis)
    if count & (count - 1):
        return lax.psum(value, axis)
    step = 1
    while step < count:
        if step * 2 >= count:
            value = value + lax.ppermute(value, axis, [(i, i ^ step) for i in range(count)])
            break
        near, far, both = (
            lax.ppermute(value, axis, [(i, i ^ mask) for i in range(count)])
            for mask in (step, step * 2, step * 3)
        )
        value = (value + near) + (far + both)
        step *= 4
    return value


def split_sum(value, axes):
    sizes = [lax.axis_size(axis) for axis in axes]
    total = math.prod(sizes)
    if total & (total - 1) or sizes[0] % 2:
        return lax.psum(value, axes)
    half = value.shape[0] // 2
    upper = lax.axis_index(axes[0]) % 2 == 1
    keep = jnp.where(upper, value[half:], value[:half])
    send = jnp.where(upper, value[:half], value[half:])
    index_axes = tuple(reversed(axes))
    partner = [(i, i ^ 1) for i in range(total)]
    keep = keep + lax.ppermute(send, index_axes, partner)
    bits = [1 << b for b in range(1, total.bit_length() - 1)]
    if len(bits) >= 2:
        near, far, both = (
            lax.ppermute(keep, index_axes, [(i, i ^ mask) for i in range(total)])
            for mask in (bits[0], bits[1], bits[0] | bits[1])
        )
        keep = (keep + near) + (far + both)
        bits = bits[2:]
    for bit in bits:
        keep = keep + lax.ppermute(keep, index_axes, [(i, i ^ bit) for i in range(total)])
    other = lax.ppermute(keep, index_axes, partner)
    return jnp.where(
        upper, jnp.concatenate((other, keep)), jnp.concatenate((keep, other))
    )


def row_count(shape):
    return -(-math.prod(shape) // 128)


def pack_rows(parts):
    blocks = []
    for part in parts:
        size = math.prod(part.shape)
        rows = row_count(part.shape)
        flat = part.reshape(-1)
        if rows * 128 != size:
            flat = jnp.pad(flat, (0, rows * 128 - size))
        blocks.append(flat.reshape(rows, 128))
    total = sum(block.shape[0] for block in blocks)
    blocks.append(jnp.zeros((-(-total // 16) * 16 - total, 128), jnp.float32))
    return jnp.concatenate(blocks)


def unpack_rows(packed, shapes):
    parts = []
    start = 0
    for shape in shapes:
        size = math.prod(shape)
        rows = row_count(shape)
        block = packed[start : start + rows]
        if rows * 128 != size:
            block = block.reshape(-1)[:size]
        parts.append(block.reshape(shape))
        start += rows
    return parts


def silu_slope(value):
    sigma = jax.nn.sigmoid(value)
    return sigma * (1.0 + value * (1.0 - sigma))


def wrap_columns(field):
    return jnp.concatenate((field[..., -1:], field, field[..., :1]), axis=-1)


def spread_local(weight, extended_field, shape):
    windows = jnp.stack(
        [
            extended_field[:, 2 - tap_x : 2 - tap_x + shape[1], 2 - tap_z : 2 - tap_z + shape[2]]
            for tap_x in range(3)
            for tap_z in range(3)
        ]
    )
    per_shift = jnp.einsum(
        "toxzy,tsoi->sixzy",
        windows,
        weight.reshape(9, 3, shape[0], shape[0]),
        preferred_element_type=jnp.float32,
    )
    return sum(jnp.roll(per_shift[tap_y], tap_y - 1, axis=3) for tap_y in range(3))


def taps_from_halo(extended_grad, inputs):
    shape = inputs.shape
    windows = jnp.stack(
        [
            extended_grad[:, 2 - tap_x : 2 - tap_x + shape[1], 2 - tap_z : 2 - tap_z + shape[2]]
            for tap_x in range(3)
            for tap_z in range(3)
        ]
    )
    rolled = jnp.stack([jnp.roll(inputs, 1 - tap_y, axis=3) for tap_y in range(3)])
    taps = jnp.einsum(
        "toxzy,sixzy->tsoi", windows, rolled, preferred_element_type=jnp.float32
    )
    return taps.reshape(3, 3, 3, extended_grad.shape[0], shape[0])


def per_device(
    features, pre_first, pre_second, w_first, w_second, w_out, b_out, y_target, k_target
):
    count_sky = lax.axis_size("sky")
    count_los = lax.axis_size("los")
    depth_all = pre_first.shape[2] * count_los
    norm_factor = 1.0 / math.sqrt(features.shape[1] * count_sky * features.shape[3] * depth_all)
    shape = features.shape
    first_wide = pre_first.astype(jnp.float32)
    second_wide = pre_second.astype(jnp.float32)
    hidden_second = jax.nn.silu(second_wide).astype(jnp.bfloat16)
    heads_raw = jnp.einsum(
        "oi,ixzy->oxzy", w_out, hidden_second, preferred_element_type=jnp.float32
    )
    heads_raw = heads_raw + b_out[:, None, None, None]
    pressure = jax.nn.softplus(heads_raw[0])
    density = jax.nn.softplus(heads_raw[1])
    velocity = heads_raw[2]
    y_part = jnp.sum(pressure, axis=1) / depth_all
    k_part = -jnp.sum(density * velocity, axis=1) / depth_all
    y_map, k_map = quad_sum(jnp.stack((y_part, k_part)), "los")
    y_resid = y_map - y_target
    k_resid = k_map - k_target
    y_resid = y_resid[:, None, :]
    k_resid = k_resid[:, None, :]
    head_grad = jnp.stack(
        (
            y_resid * jax.nn.sigmoid(heads_raw[0]),
            -k_resid * velocity * jax.nn.sigmoid(heads_raw[1]),
            -k_resid * density,
        )
    ).astype(jnp.bfloat16)
    grad_out = (
        jnp.einsum("oxzy,ixzy->oi", head_grad, hidden_second, preferred_element_type=jnp.float32)
        * norm_factor
    )
    grad_bias = jnp.sum(head_grad.astype(jnp.float32), axis=(1, 2, 3)) * norm_factor
    back_second = jnp.einsum("oi,oxzy->ixzy", w_out, head_grad, preferred_element_type=jnp.float32)
    grad_second_pre = (back_second * silu_slope(second_wide)).astype(jnp.bfloat16)
    second_padded = extended(grad_second_pre, (("sky", 1), ("los", 2)), 1)
    back_first = spread_local(w_second, second_padded, shape)
    grad_first_pre = (back_first * silu_slope(first_wide)).astype(jnp.bfloat16)
    first_padded = extended(grad_first_pre, (("sky", 1), ("los", 2)), 1)
    grad_features = spread_local(w_first, first_padded, shape).astype(jnp.bfloat16)
    hidden_first = jax.nn.silu(first_wide).astype(jnp.bfloat16)
    grad_second = taps_from_halo(second_padded, hidden_first)
    grad_first = taps_from_halo(first_padded, features)
    reduced = (grad_first * norm_factor, grad_second * norm_factor, grad_out, grad_bias)
    reduced_shapes = [part.shape for part in reduced]
    grad_first, grad_second, grad_out, grad_bias = unpack_rows(
        split_sum(pack_rows(reduced), ("los", "sky")), reduced_shapes
    )
    return (grad_features, grad_first, grad_second, grad_out, grad_bias)


def solution(mesh):
    in_specs = (
        P(None, "sky", "los", None),
        P(None, "sky", "los", None),
        P(None, "sky", "los", None),
        P(),
        P(),
        P(),
        P(),
        P("sky", None),
        P("sky", None),
    )
    out_specs = (P(None, "sky", "los", None), P(), P(), P(), P())
    return jax.shard_map(
        per_device, mesh=mesh, in_specs=in_specs, out_specs=out_specs, check_vma=False
    )
```

```python
import math

import jax
import jax.numpy as jnp
from jax import lax
from jax.sharding import PartitionSpec as P


def extended(block, sides, width):
    for axis, dim in sides:
        count = lax.axis_size(axis)
        forward = [(i, i + 1) for i in range(count - 1)]
        forward.append((count - 1, 0))
        backward = [(target, source) for source, target in forward]
        low = lax.ppermute(
            lax.slice_in_dim(block, block.shape[dim] - width, None, axis=dim), axis, forward
        )
        high = lax.ppermute(lax.slice_in_dim(block, 0, width, axis=dim), axis, backward)
        block = jnp.concatenate([low, block, high], axis=dim)
    return block


def butterfly_sum(value, axes, skip=0):
    for axis in axes:
        count = lax.axis_size(axis)
        if count & (count - 1):
            value = lax.psum(value, axis)
            continue
        step = 2 if skip and axis == axes[0] else 1
        while step < count:
            pairs = [(i, i ^ step) for i in range(count)]
            value = value + lax.ppermute(value, axis, pairs)
            step *= 2
    return value


def quad_sum(value, axis):
    count = lax.axis_size(axis)
    if count & (count - 1):
        return lax.psum(value, axis)
    step = 1
    while step < count:
        if step * 2 >= count:
            value = value + lax.ppermute(value, axis, [(i, i ^ step) for i in range(count)])
            break
        near, far, both = (
            lax.ppermute(value, axis, [(i, i ^ mask) for i in range(count)])
            for mask in (step, step * 2, step * 3)
        )
        value = (value + near) + (far + both)
        step *= 4
    return value


def split_sum(value, axes):
    sizes = [lax.axis_size(axis) for axis in axes]
    total = math.prod(sizes)
    if total & (total - 1) or sizes[0] % 2:
        return lax.psum(value, axes)
    half = value.shape[0] // 2
    upper = lax.axis_index(axes[0]) % 2 == 1
    keep = jnp.where(upper, value[half:], value[:half])
    send = jnp.where(upper, value[:half], value[half:])
    index_axes = tuple(reversed(axes))
    partner = [(i, i ^ 1) for i in range(total)]
    keep = keep + lax.ppermute(send, index_axes, partner)
    bits = [1 << b for b in range(1, total.bit_length() - 1)]
    while len(bits) >= 2:
        near, far, both = (
            lax.ppermute(keep, index_axes, [(i, i ^ mask) for i in range(total)])
            for mask in (bits[0], bits[1], bits[0] | bits[1])
        )
        keep = (keep + near) + (far + both)
        bits = bits[2:]
    for bit in bits:
        keep = keep + lax.ppermute(keep, index_axes, [(i, i ^ bit) for i in range(total)])
    other = lax.ppermute(keep, index_axes, partner)
    return jnp.where(
        upper, jnp.concatenate((other, keep)), jnp.concatenate((keep, other))
    )


def row_count(shape):
    return -(-math.prod(shape) // 128)


def pack_rows(parts):
    blocks = []
    for part in parts:
        size = math.prod(part.shape)
        rows = row_count(part.shape)
        flat = part.reshape(-1)
        if rows * 128 != size:
            flat = jnp.pad(flat, (0, rows * 128 - size))
        blocks.append(flat.reshape(rows, 128))
    total = sum(block.shape[0] for block in blocks)
    blocks.append(jnp.zeros((-(-total // 16) * 16 - total, 128), jnp.float32))
    return jnp.concatenate(blocks)


def unpack_rows(packed, shapes):
    parts = []
    start = 0
    for shape in shapes:
        size = math.prod(shape)
        rows = row_count(shape)
        block = packed[start : start + rows]
        if rows * 128 != size:
            block = block.reshape(-1)[:size]
        parts.append(block.reshape(shape))
        start += rows
    return parts


def silu_slope(value):
    sigma = jax.nn.sigmoid(value)
    return sigma * (1.0 + value * (1.0 - sigma))


def wrap_columns(field):
    return jnp.concatenate((field[..., -1:], field, field[..., :1]), axis=-1)


def spread_local(weight, extended_field, shape):
    windows = jnp.stack(
        [
            extended_field[:, 2 - tap_x : 2 - tap_x + shape[1], 2 - tap_z : 2 - tap_z + shape[2]]
            for tap_x in range(3)
            for tap_z in range(3)
        ]
    )
    per_shift = jnp.einsum(
        "toxzy,tsoi->sixzy",
        windows,
        weight.reshape(9, 3, shape[0], shape[0]),
        preferred_element_type=jnp.float32,
    )
    return sum(jnp.roll(per_shift[tap_y], tap_y - 1, axis=3) for tap_y in range(3))


def taps_from_halo(extended_grad, inputs):
    shape = inputs.shape
    windows = jnp.stack(
        [
            extended_grad[:, 2 - tap_x : 2 - tap_x + shape[1], 2 - tap_z : 2 - tap_z + shape[2]]
            for tap_x in range(3)
            for tap_z in range(3)
        ]
    )
    rolled = jnp.stack([jnp.roll(inputs, 1 - tap_y, axis=3) for tap_y in range(3)])
    taps = jnp.einsum(
        "toxzy,sixzy->tsoi", windows, rolled, preferred_element_type=jnp.float32
    )
    return taps.reshape(3, 3, 3, extended_grad.shape[0], shape[0])


def per_device(
    features, pre_first, pre_second, w_first, w_second, w_out, b_out, y_target, k_target
):
    count_sky = lax.axis_size("sky")
    count_los = lax.axis_size("los")
    depth_all = pre_first.shape[2] * count_los
    norm_factor = 1.0 / math.sqrt(features.shape[1] * count_sky * features.shape[3] * depth_all)
    shape = features.shape
    first_wide = pre_first.astype(jnp.float32)
    second_wide = pre_second.astype(jnp.float32)
    hidden_second = jax.nn.silu(second_wide).astype(jnp.bfloat16)
    heads_raw = jnp.einsum(
        "oi,ixzy->oxzy", w_out, hidden_second, preferred_element_type=jnp.float32
    )
    heads_raw = heads_raw + b_out[:, None, None, None]
    pressure = jax.nn.softplus(heads_raw[0])
    density = jax.nn.softplus(heads_raw[1])
    velocity = heads_raw[2]
    y_part = jnp.sum(pressure, axis=1) / depth_all
    k_part = -jnp.sum(density * velocity, axis=1) / depth_all
    y_map, k_map = quad_sum(jnp.stack((y_part, k_part)), "los")
    y_resid = y_map - y_target
    k_resid = k_map - k_target
    y_resid = y_resid[:, None, :]
    k_resid = k_resid[:, None, :]
    head_grad = jnp.stack(
        (
            y_resid * jax.nn.sigmoid(heads_raw[0]),
            -k_resid * velocity * jax.nn.sigmoid(heads_raw[1]),
            -k_resid * density,
        )
    ).astype(jnp.bfloat16)
    grad_out = (
        jnp.einsum("oxzy,ixzy->oi", head_grad, hidden_second, preferred_element_type=jnp.float32)
        * norm_factor
    )
    grad_bias = jnp.sum(head_grad.astype(jnp.float32), axis=(1, 2, 3)) * norm_factor
    back_second = jnp.einsum("oi,oxzy->ixzy", w_out, head_grad, preferred_element_type=jnp.float32)
    grad_second_pre = (back_second * silu_slope(second_wide)).astype(jnp.bfloat16)
    second_padded = extended(grad_second_pre, (("sky", 1), ("los", 2)), 1)
    back_first = spread_local(w_second, second_padded, shape)
    grad_first_pre = (back_first * silu_slope(first_wide)).astype(jnp.bfloat16)
    first_padded = extended(grad_first_pre, (("sky", 1), ("los", 2)), 1)
    grad_features = spread_local(w_first, first_padded, shape).astype(jnp.bfloat16)
    hidden_first = jax.nn.silu(first_wide).astype(jnp.bfloat16)
    grad_second = taps_from_halo(second_padded, hidden_first)
    grad_first = taps_from_halo(first_padded, features)
    reduced = (grad_first * norm_factor, grad_second * norm_factor, grad_out, grad_bias)
    reduced_shapes = [part.shape for part in reduced]
    grad_first, grad_second, grad_out, grad_bias = unpack_rows(
        split_sum(pack_rows(reduced), ("los", "sky")), reduced_shapes
    )
    return (grad_features, grad_first, grad_second, grad_out, grad_bias)


def solution(mesh):
    in_specs = (
        P(None, "sky", "los", None),
        P(None, "sky", "los", None),
        P(None, "sky", "los", None),
        P(),
        P(),
        P(),
        P(),
        P("sky", None),
        P("sky", None),
    )
    out_specs = (P(None, "sky", "los", None), P(), P(), P(), P())
    return jax.shard_map(
        per_device, mesh=mesh, in_specs=in_specs, out_specs=out_specs, check_vma=False
    )
```

```python
import math

import jax
import jax.numpy as jnp
from jax import lax
from jax.sharding import PartitionSpec as P


def extended(block, sides, width):
    for axis, dim in sides:
        count = lax.axis_size(axis)
        forward = [(i, i + 1) for i in range(count - 1)]
        forward.append((count - 1, 0))
        backward = [(target, source) for source, target in forward]
        low = lax.ppermute(
            lax.slice_in_dim(block, block.shape[dim] - width, None, axis=dim), axis, forward
        )
        high = lax.ppermute(lax.slice_in_dim(block, 0, width, axis=dim), axis, backward)
        block = jnp.concatenate([low, block, high], axis=dim)
    return block


def butterfly_sum(value, axes, skip=0):
    for axis in axes:
        count = lax.axis_size(axis)
        if count & (count - 1):
            value = lax.psum(value, axis)
            continue
        step = 2 if skip and axis == axes[0] else 1
        while step < count:
            pairs = [(i, i ^ step) for i in range(count)]
            value = value + lax.ppermute(value, axis, pairs)
            step *= 2
    return value


def quad_sum(value, axis):
    count = lax.axis_size(axis)
    if count & (count - 1):
        return lax.psum(value, axis)
    step = 1
    while step < count:
        if step * 2 >= count:
            value = value + lax.ppermute(value, axis, [(i, i ^ step) for i in range(count)])
            break
        near, far, both = (
            lax.ppermute(value, axis, [(i, i ^ mask) for i in range(count)])
            for mask in (step, step * 2, step * 3)
        )
        value = (value + near) + (far + both)
        step *= 4
    return value


def split_sum(value, axes):
    sizes = [lax.axis_size(axis) for axis in axes]
    total = math.prod(sizes)
    if total & (total - 1) or sizes[0] % 2:
        return lax.psum(value, axes)
    half = value.shape[0] // 2
    side = lax.axis_index(axes[0]) % 2
    keep = lax.dynamic_slice_in_dim(value, side * half, half)
    send = lax.dynamic_slice_in_dim(value, (1 - side) * half, half)
    index_axes = tuple(reversed(axes))
    partner = [(i, i ^ 1) for i in range(total)]
    keep = keep + lax.ppermute(send, index_axes, partner)
    bits = [1 << b for b in range(1, total.bit_length() - 1)]
    if len(bits) >= 2:
        near, far, both = (
            lax.ppermute(keep, index_axes, [(i, i ^ mask) for i in range(total)])
            for mask in (bits[0], bits[1], bits[0] | bits[1])
        )
        keep = (keep + near) + (far + both)
        bits = bits[2:]
    for bit in bits:
        keep = keep + lax.ppermute(keep, index_axes, [(i, i ^ bit) for i in range(total)])
    other = lax.ppermute(keep, index_axes, partner)
    return lax.dynamic_update_slice_in_dim(
        jnp.concatenate((other, other)), keep, side * half, axis=0
    )


def row_count(shape):
    return -(-math.prod(shape) // 128)


def pack_rows(parts):
    blocks = []
    for part in parts:
        size = math.prod(part.shape)
        rows = row_count(part.shape)
        flat = part.reshape(-1)
        if rows * 128 != size:
            flat = jnp.pad(flat, (0, rows * 128 - size))
        blocks.append(flat.reshape(rows, 128))
    total = sum(block.shape[0] for block in blocks)
    blocks.append(jnp.zeros((-(-total // 16) * 16 - total, 128), jnp.float32))
    return jnp.concatenate(blocks)


def unpack_rows(packed, shapes):
    parts = []
    start = 0
    for shape in shapes:
        size = math.prod(shape)
        rows = row_count(shape)
        block = packed[start : start + rows]
        if rows * 128 != size:
            block = block.reshape(-1)[:size]
        parts.append(block.reshape(shape))
        start += rows
    return parts


def silu_slope(value):
    sigma = jax.nn.sigmoid(value)
    return sigma * (1.0 + value * (1.0 - sigma))


def wrap_columns(field):
    return jnp.concatenate((field[..., -1:], field, field[..., :1]), axis=-1)


def spread_local(weight, extended_field, shape):
    windows = jnp.stack(
        [
            extended_field[:, 2 - tap_x : 2 - tap_x + shape[1], 2 - tap_z : 2 - tap_z + shape[2]]
            for tap_x in range(3)
            for tap_z in range(3)
        ]
    )
    per_shift = jnp.einsum(
        "toxzy,tsoi->sixzy",
        windows,
        weight.reshape(9, 3, shape[0], shape[0]),
        preferred_element_type=jnp.float32,
    )
    return sum(jnp.roll(per_shift[tap_y], tap_y - 1, axis=3) for tap_y in range(3))


def taps_from_halo(extended_grad, inputs):
    shape = inputs.shape
    windows = jnp.stack(
        [
            extended_grad[:, 2 - tap_x : 2 - tap_x + shape[1], 2 - tap_z : 2 - tap_z + shape[2]]
            for tap_x in range(3)
            for tap_z in range(3)
        ]
    )
    rolled = jnp.stack([jnp.roll(inputs, 1 - tap_y, axis=3) for tap_y in range(3)])
    taps = jnp.einsum(
        "toxzy,sixzy->tsoi", windows, rolled, preferred_element_type=jnp.float32
    )
    return taps.reshape(3, 3, 3, extended_grad.shape[0], shape[0])


def per_device(
    features, pre_first, pre_second, w_first, w_second, w_out, b_out, y_target, k_target
):
    count_sky = lax.axis_size("sky")
    count_los = lax.axis_size("los")
    depth_all = pre_first.shape[2] * count_los
    norm_factor = 1.0 / math.sqrt(features.shape[1] * count_sky * features.shape[3] * depth_all)
    shape = features.shape
    first_wide = pre_first.astype(jnp.float32)
    second_wide = pre_second.astype(jnp.float32)
    hidden_second = jax.nn.silu(second_wide).astype(jnp.bfloat16)
    heads_raw = jnp.einsum(
        "oi,ixzy->oxzy", w_out, hidden_second, preferred_element_type=jnp.float32
    )
    heads_raw = heads_raw + b_out[:, None, None, None]
    pressure = jax.nn.softplus(heads_raw[0])
    density = jax.nn.softplus(heads_raw[1])
    velocity = heads_raw[2]
    y_part = jnp.sum(pressure, axis=1) / depth_all
    k_part = -jnp.sum(density * velocity, axis=1) / depth_all
    y_map, k_map = quad_sum(jnp.stack((y_part, k_part)), "los")
    y_resid = y_map - y_target
    k_resid = k_map - k_target
    y_resid = y_resid[:, None, :]
    k_resid = k_resid[:, None, :]
    head_grad = jnp.stack(
        (
            y_resid * jax.nn.sigmoid(heads_raw[0]),
            -k_resid * velocity * jax.nn.sigmoid(heads_raw[1]),
            -k_resid * density,
        )
    ).astype(jnp.bfloat16)
    grad_out = (
        jnp.einsum("oxzy,ixzy->oi", head_grad, hidden_second, preferred_element_type=jnp.float32)
        * norm_factor
    )
    grad_bias = jnp.sum(head_grad.astype(jnp.float32), axis=(1, 2, 3)) * norm_factor
    back_second = jnp.einsum("oi,oxzy->ixzy", w_out, head_grad, preferred_element_type=jnp.float32)
    grad_second_pre = (back_second * silu_slope(second_wide)).astype(jnp.bfloat16)
    second_padded = extended(grad_second_pre, (("sky", 1), ("los", 2)), 1)
    back_first = spread_local(w_second, second_padded, shape)
    grad_first_pre = (back_first * silu_slope(first_wide)).astype(jnp.bfloat16)
    first_padded = extended(grad_first_pre, (("sky", 1), ("los", 2)), 1)
    grad_features = spread_local(w_first, first_padded, shape).astype(jnp.bfloat16)
    hidden_first = jax.nn.silu(first_wide).astype(jnp.bfloat16)
    grad_second = taps_from_halo(second_padded, hidden_first)
    grad_first = taps_from_halo(first_padded, features)
    reduced = (grad_first * norm_factor, grad_second * norm_factor, grad_out, grad_bias)
    reduced_shapes = [part.shape for part in reduced]
    grad_first, grad_second, grad_out, grad_bias = unpack_rows(
        split_sum(pack_rows(reduced), ("los", "sky")), reduced_shapes
    )
    return (grad_features, grad_first, grad_second, grad_out, grad_bias)


def solution(mesh):
    in_specs = (
        P(None, "sky", "los", None),
        P(None, "sky", "los", None),
        P(None, "sky", "los", None),
        P(),
        P(),
        P(),
        P(),
        P("sky", None),
        P("sky", None),
    )
    out_specs = (P(None, "sky", "los", None), P(), P(), P(), P())
    return jax.shard_map(
        per_device, mesh=mesh, in_specs=in_specs, out_specs=out_specs, check_vma=False
    )
```

```python
import math

import jax
import jax.numpy as jnp
from jax import lax
from jax.sharding import PartitionSpec as P


def extended(block, sides, width):
    for axis, dim in sides:
        count = lax.axis_size(axis)
        forward = [(i, i + 1) for i in range(count - 1)]
        forward.append((count - 1, 0))
        backward = [(target, source) for source, target in forward]
        low = lax.ppermute(
            lax.slice_in_dim(block, block.shape[dim] - width, None, axis=dim), axis, forward
        )
        high = lax.ppermute(lax.slice_in_dim(block, 0, width, axis=dim), axis, backward)
        block = jnp.concatenate([low, block, high], axis=dim)
    return block


def butterfly_sum(value, axes, skip=0):
    for axis in axes:
        count = lax.axis_size(axis)
        if count & (count - 1):
            value = lax.psum(value, axis)
            continue
        step = 2 if skip and axis == axes[0] else 1
        while step < count:
            pairs = [(i, i ^ step) for i in range(count)]
            value = value + lax.ppermute(value, axis, pairs)
            step *= 2
    return value


def quad_sum(value, axis):
    count = lax.axis_size(axis)
    if count & (count - 1):
        return lax.psum(value, axis)
    step = 1
    while step < count:
        if step * 2 >= count:
            value = value + lax.ppermute(value, axis, [(i, i ^ step) for i in range(count)])
            break
        near, far, both = (
            lax.ppermute(value, axis, [(i, i ^ mask) for i in range(count)])
            for mask in (step, step * 2, step * 3)
        )
        value = (value + near) + (far + both)
        step *= 4
    return value


def split_sum(value, axes):
    sizes = [lax.axis_size(axis) for axis in axes]
    total = math.prod(sizes)
    half = value.shape[0] // 2
    if total & (total - 1) or sizes[0] % 2:
        value = lax.psum(value, axes)
        return value[:half], value[half:], 0
    side = lax.axis_index(axes[0]) % 2
    keep = lax.dynamic_slice_in_dim(value, side * half, half)
    send = lax.dynamic_slice_in_dim(value, (1 - side) * half, half)
    index_axes = tuple(reversed(axes))
    partner = [(i, i ^ 1) for i in range(total)]
    keep = keep + lax.ppermute(send, index_axes, partner)
    bits = [1 << b for b in range(1, total.bit_length() - 1)]
    if len(bits) >= 2:
        near, far, both = (
            lax.ppermute(keep, index_axes, [(i, i ^ mask) for i in range(total)])
            for mask in (bits[0], bits[1], bits[0] | bits[1])
        )
        keep = (keep + near) + (far + both)
        bits = bits[2:]
    for bit in bits:
        keep = keep + lax.ppermute(keep, index_axes, [(i, i ^ bit) for i in range(total)])
    return keep, lax.ppermute(keep, index_axes, partner), side


def row_count(shape):
    return -(-math.prod(shape) // 128)


def pack_rows(parts):
    blocks = []
    for part in parts:
        size = math.prod(part.shape)
        rows = row_count(part.shape)
        flat = part.reshape(-1)
        if rows * 128 != size:
            flat = jnp.pad(flat, (0, rows * 128 - size))
        blocks.append(flat.reshape(rows, 128))
    total = sum(block.shape[0] for block in blocks)
    blocks.append(jnp.zeros((-(-total // 16) * 16 - total, 128), jnp.float32))
    return jnp.concatenate(blocks)


def unpack_rows(packed, shapes):
    parts = []
    start = 0
    for shape in shapes:
        size = math.prod(shape)
        rows = row_count(shape)
        block = packed[start : start + rows]
        if rows * 128 != size:
            block = block.reshape(-1)[:size]
        parts.append(block.reshape(shape))
        start += rows
    return parts


def silu_slope(value):
    sigma = jax.nn.sigmoid(value)
    return sigma * (1.0 + value * (1.0 - sigma))


def wrap_columns(field):
    return jnp.concatenate((field[..., -1:], field, field[..., :1]), axis=-1)


def spread_local(weight, extended_field, shape):
    windows = jnp.stack(
        [
            extended_field[:, 2 - tap_x : 2 - tap_x + shape[1], 2 - tap_z : 2 - tap_z + shape[2]]
            for tap_x in range(3)
            for tap_z in range(3)
        ]
    )
    per_shift = jnp.einsum(
        "toxzy,tsoi->sixzy",
        windows,
        weight.reshape(9, 3, shape[0], shape[0]),
        preferred_element_type=jnp.float32,
    )
    return sum(jnp.roll(per_shift[tap_y], tap_y - 1, axis=3) for tap_y in range(3))


def taps_from_halo(extended_grad, inputs):
    shape = inputs.shape
    windows = jnp.stack(
        [
            extended_grad[:, 2 - tap_x : 2 - tap_x + shape[1], 2 - tap_z : 2 - tap_z + shape[2]]
            for tap_x in range(3)
            for tap_z in range(3)
        ]
    )
    rolled = jnp.stack([jnp.roll(inputs, 1 - tap_y, axis=3) for tap_y in range(3)])
    taps = jnp.einsum(
        "toxzy,sixzy->tsoi", windows, rolled, preferred_element_type=jnp.float32
    )
    return taps.reshape(3, 3, 3, extended_grad.shape[0], shape[0])


def per_device(
    features, pre_first, pre_second, w_first, w_second, w_out, b_out, y_target, k_target
):
    count_sky = lax.axis_size("sky")
    count_los = lax.axis_size("los")
    depth_all = pre_first.shape[2] * count_los
    norm_factor = 1.0 / math.sqrt(features.shape[1] * count_sky * features.shape[3] * depth_all)
    shape = features.shape
    first_wide = pre_first.astype(jnp.float32)
    second_wide = pre_second.astype(jnp.float32)
    hidden_second = jax.nn.silu(second_wide).astype(jnp.bfloat16)
    heads_raw = jnp.einsum(
        "oi,ixzy->oxzy", w_out, hidden_second, preferred_element_type=jnp.float32
    )
    heads_raw = heads_raw + b_out[:, None, None, None]
    pressure = jax.nn.softplus(heads_raw[0])
    density = jax.nn.softplus(heads_raw[1])
    velocity = heads_raw[2]
    y_part = jnp.sum(pressure, axis=1) / depth_all
    k_part = -jnp.sum(density * velocity, axis=1) / depth_all
    y_map, k_map = quad_sum(jnp.stack((y_part, k_part)), "los")
    y_resid = y_map - y_target
    k_resid = k_map - k_target
    y_resid = y_resid[:, None, :]
    k_resid = k_resid[:, None, :]
    head_grad = jnp.stack(
        (
            y_resid * jax.nn.sigmoid(heads_raw[0]),
            -k_resid * velocity * jax.nn.sigmoid(heads_raw[1]),
            -k_resid * density,
        )
    ).astype(jnp.bfloat16)
    grad_out = (
        jnp.einsum("oxzy,ixzy->oi", head_grad, hidden_second, preferred_element_type=jnp.float32)
        * norm_factor
    )
    grad_bias = jnp.sum(head_grad.astype(jnp.float32), axis=(1, 2, 3)) * norm_factor
    back_second = jnp.einsum("oi,oxzy->ixzy", w_out, head_grad, preferred_element_type=jnp.float32)
    grad_second_pre = (back_second * silu_slope(second_wide)).astype(jnp.bfloat16)
    second_padded = extended(grad_second_pre, (("sky", 1), ("los", 2)), 1)
    back_first = spread_local(w_second, second_padded, shape)
    grad_first_pre = (back_first * silu_slope(first_wide)).astype(jnp.bfloat16)
    first_padded = extended(grad_first_pre, (("sky", 1), ("los", 2)), 1)
    grad_features = spread_local(w_first, first_padded, shape).astype(jnp.bfloat16)
    hidden_first = jax.nn.silu(first_wide).astype(jnp.bfloat16)
    grad_second = taps_from_halo(second_padded, hidden_first)
    grad_first = taps_from_halo(first_padded, features)
    first_half = pack_rows((grad_first * norm_factor, grad_out, grad_bias))
    second_half = pack_rows((grad_second * norm_factor,))
    rows = max(first_half.shape[0], second_half.shape[0])
    first_half, second_half = (
        jnp.pad(part, ((0, rows - part.shape[0]), (0, 0))) for part in (first_half, second_half)
    )
    keep, other, side = split_sum(jnp.concatenate((first_half, second_half)), ("los", "sky"))
    main_rows = row_count(grad_first.shape)
    keep_grad = keep[:main_rows].reshape(grad_first.shape)
    other_grad = other[:main_rows].reshape(grad_first.shape)
    keep_first = side == 0
    grad_first = jnp.where(keep_first, keep_grad, other_grad)
    grad_second = jnp.where(keep_first, other_grad, keep_grad)
    small = jnp.where(keep_first, keep[main_rows:], other[main_rows:])
    grad_out, grad_bias = unpack_rows(small, [grad_out.shape, grad_bias.shape])
    return (grad_features, grad_first, grad_second, grad_out, grad_bias)


def solution(mesh):
    in_specs = (
        P(None, "sky", "los", None),
        P(None, "sky", "los", None),
        P(None, "sky", "los", None),
        P(),
        P(),
        P(),
        P(),
        P("sky", None),
        P("sky", None),
    )
    out_specs = (P(None, "sky", "los", None), P(), P(), P(), P())
    return jax.shard_map(
        per_device, mesh=mesh, in_specs=in_specs, out_specs=out_specs, check_vma=False
    )
```

```python
import math

import jax
import jax.numpy as jnp
from jax import lax
from jax.sharding import PartitionSpec as P


def extended(block, sides, width):
    for axis, dim in sides:
        count = lax.axis_size(axis)
        forward = [(i, i + 1) for i in range(count - 1)]
        forward.append((count - 1, 0))
        backward = [(target, source) for source, target in forward]
        low = lax.ppermute(
            lax.slice_in_dim(block, block.shape[dim] - width, None, axis=dim), axis, forward
        )
        high = lax.ppermute(lax.slice_in_dim(block, 0, width, axis=dim), axis, backward)
        block = jnp.concatenate([low, block, high], axis=dim)
    return block


def butterfly_sum(value, axes, skip=0):
    for axis in axes:
        count = lax.axis_size(axis)
        if count & (count - 1):
            value = lax.psum(value, axis)
            continue
        step = 2 if skip and axis == axes[0] else 1
        while step < count:
            pairs = [(i, i ^ step) for i in range(count)]
            value = value + lax.ppermute(value, axis, pairs)
            step *= 2
    return value


def quad_sum(value, axis):
    count = lax.axis_size(axis)
    if count & (count - 1):
        return lax.psum(value, axis)
    step = 1
    while step < count:
        if step * 2 >= count:
            value = value + lax.ppermute(value, axis, [(i, i ^ step) for i in range(count)])
            break
        near, far, both = (
            lax.ppermute(value, axis, [(i, i ^ mask) for i in range(count)])
            for mask in (step, step * 2, step * 3)
        )
        value = (value + near) + (far + both)
        step *= 4
    return value


def split_sum(value, axes):
    sizes = [lax.axis_size(axis) for axis in axes]
    total = math.prod(sizes)
    if total & (total - 1) or sizes[0] % 2:
        return lax.psum(value, axes)
    half = value.shape[0] // 2
    side = lax.axis_index(axes[0]) % 2
    keep = lax.dynamic_slice_in_dim(value, side * half, half)
    send = lax.dynamic_slice_in_dim(value, (1 - side) * half, half)
    index_axes = tuple(reversed(axes))
    partner = [(i, i ^ 1) for i in range(total)]
    keep = keep + lax.ppermute(send, index_axes, partner)
    bits = [1 << b for b in range(1, total.bit_length() - 1)]
    if len(bits) >= 2:
        near, far, both = (
            lax.ppermute(keep, index_axes, [(i, i ^ mask) for i in range(total)])
            for mask in (bits[0], bits[1], bits[0] | bits[1])
        )
        keep = (keep + near) + (far + both)
        bits = bits[2:]
    for bit in reversed(bits):
        keep = keep + lax.ppermute(keep, index_axes, [(i, i ^ bit) for i in range(total)])
    other = lax.ppermute(keep, index_axes, partner)
    return lax.dynamic_update_slice_in_dim(
        jnp.concatenate((other, other)), keep, side * half, axis=0
    )


def row_count(shape):
    return -(-math.prod(shape) // 128)


def pack_rows(parts):
    blocks = []
    for part in parts:
        size = math.prod(part.shape)
        rows = row_count(part.shape)
        flat = part.reshape(-1)
        if rows * 128 != size:
            flat = jnp.pad(flat, (0, rows * 128 - size))
        blocks.append(flat.reshape(rows, 128))
    total = sum(block.shape[0] for block in blocks)
    blocks.append(jnp.zeros((-(-total // 16) * 16 - total, 128), jnp.float32))
    return jnp.concatenate(blocks)


def unpack_rows(packed, shapes):
    parts = []
    start = 0
    for shape in shapes:
        size = math.prod(shape)
        rows = row_count(shape)
        block = packed[start : start + rows]
        if rows * 128 != size:
            block = block.reshape(-1)[:size]
        parts.append(block.reshape(shape))
        start += rows
    return parts


def silu_slope(value):
    sigma = jax.nn.sigmoid(value)
    return sigma * (1.0 + value * (1.0 - sigma))


def wrap_columns(field):
    return jnp.concatenate((field[..., -1:], field, field[..., :1]), axis=-1)


def spread_local(weight, extended_field, shape):
    windows = jnp.stack(
        [
            extended_field[:, 2 - tap_x : 2 - tap_x + shape[1], 2 - tap_z : 2 - tap_z + shape[2]]
            for tap_x in range(3)
            for tap_z in range(3)
        ]
    )
    per_shift = jnp.einsum(
        "toxzy,tsoi->sixzy",
        windows,
        weight.reshape(9, 3, shape[0], shape[0]),
        preferred_element_type=jnp.float32,
    )
    return sum(jnp.roll(per_shift[tap_y], tap_y - 1, axis=3) for tap_y in range(3))


def taps_from_halo(extended_grad, inputs):
    shape = inputs.shape
    windows = jnp.stack(
        [
            extended_grad[:, 2 - tap_x : 2 - tap_x + shape[1], 2 - tap_z : 2 - tap_z + shape[2]]
            for tap_x in range(3)
            for tap_z in range(3)
        ]
    )
    rolled = jnp.stack([jnp.roll(inputs, 1 - tap_y, axis=3) for tap_y in range(3)])
    taps = jnp.einsum(
        "toxzy,sixzy->tsoi", windows, rolled, preferred_element_type=jnp.float32
    )
    return taps.reshape(3, 3, 3, extended_grad.shape[0], shape[0])


def per_device(
    features, pre_first, pre_second, w_first, w_second, w_out, b_out, y_target, k_target
):
    count_sky = lax.axis_size("sky")
    count_los = lax.axis_size("los")
    depth_all = pre_first.shape[2] * count_los
    norm_factor = 1.0 / math.sqrt(features.shape[1] * count_sky * features.shape[3] * depth_all)
    shape = features.shape
    first_wide = pre_first.astype(jnp.float32)
    second_wide = pre_second.astype(jnp.float32)
    hidden_second = jax.nn.silu(second_wide).astype(jnp.bfloat16)
    heads_raw = jnp.einsum(
        "oi,ixzy->oxzy", w_out, hidden_second, preferred_element_type=jnp.float32
    )
    heads_raw = heads_raw + b_out[:, None, None, None]
    pressure = jax.nn.softplus(heads_raw[0])
    density = jax.nn.softplus(heads_raw[1])
    velocity = heads_raw[2]
    y_part = jnp.sum(pressure, axis=1) / depth_all
    k_part = -jnp.sum(density * velocity, axis=1) / depth_all
    y_map, k_map = quad_sum(jnp.stack((y_part, k_part)), "los")
    y_resid = y_map - y_target
    k_resid = k_map - k_target
    y_resid = y_resid[:, None, :]
    k_resid = k_resid[:, None, :]
    head_grad = jnp.stack(
        (
            y_resid * jax.nn.sigmoid(heads_raw[0]),
            -k_resid * velocity * jax.nn.sigmoid(heads_raw[1]),
            -k_resid * density,
        )
    ).astype(jnp.bfloat16)
    grad_out = (
        jnp.einsum("oxzy,ixzy->oi", head_grad, hidden_second, preferred_element_type=jnp.float32)
        * norm_factor
    )
    grad_bias = jnp.sum(head_grad.astype(jnp.float32), axis=(1, 2, 3)) * norm_factor
    back_second = jnp.einsum("oi,oxzy->ixzy", w_out, head_grad, preferred_element_type=jnp.float32)
    grad_second_pre = (back_second * silu_slope(second_wide)).astype(jnp.bfloat16)
    second_padded = extended(grad_second_pre, (("sky", 1), ("los", 2)), 1)
    back_first = spread_local(w_second, second_padded, shape)
    grad_first_pre = (back_first * silu_slope(first_wide)).astype(jnp.bfloat16)
    first_padded = extended(grad_first_pre, (("sky", 1), ("los", 2)), 1)
    grad_features = spread_local(w_first, first_padded, shape).astype(jnp.bfloat16)
    hidden_first = jax.nn.silu(first_wide).astype(jnp.bfloat16)
    grad_second = taps_from_halo(second_padded, hidden_first)
    grad_first = taps_from_halo(first_padded, features)
    reduced = (grad_first * norm_factor, grad_second * norm_factor, grad_out, grad_bias)
    reduced_shapes = [part.shape for part in reduced]
    grad_first, grad_second, grad_out, grad_bias = unpack_rows(
        split_sum(pack_rows(reduced), ("los", "sky")), reduced_shapes
    )
    return (grad_features, grad_first, grad_second, grad_out, grad_bias)


def solution(mesh):
    in_specs = (
        P(None, "sky", "los", None),
        P(None, "sky", "los", None),
        P(None, "sky", "los", None),
        P(),
        P(),
        P(),
        P(),
        P("sky", None),
        P("sky", None),
    )
    out_specs = (P(None, "sky", "los", None), P(), P(), P(), P())
    return jax.shard_map(
        per_device, mesh=mesh, in_specs=in_specs, out_specs=out_specs, check_vma=False
    )
```

```python
import math

import jax
import jax.numpy as jnp
from jax import lax
from jax.sharding import PartitionSpec as P


def extended(block, sides, width):
    for axis, dim in sides:
        count = lax.axis_size(axis)
        forward = [(i, i + 1) for i in range(count - 1)]
        forward.append((count - 1, 0))
        backward = [(target, source) for source, target in forward]
        low = lax.ppermute(
            lax.slice_in_dim(block, block.shape[dim] - width, None, axis=dim), axis, forward
        )
        high = lax.ppermute(lax.slice_in_dim(block, 0, width, axis=dim), axis, backward)
        block = jnp.concatenate([low, block, high], axis=dim)
    return block


def butterfly_sum(value, axes, skip=0):
    for axis in axes:
        count = lax.axis_size(axis)
        if count & (count - 1):
            value = lax.psum(value, axis)
            continue
        step = 2 if skip and axis == axes[0] else 1
        while step < count:
            pairs = [(i, i ^ step) for i in range(count)]
            value = value + lax.ppermute(value, axis, pairs)
            step *= 2
    return value


def quad_sum(value, axis):
    count = lax.axis_size(axis)
    if count & (count - 1):
        return lax.psum(value, axis)
    step = 1
    while step < count:
        if step * 2 >= count:
            value = value + lax.ppermute(value, axis, [(i, i ^ step) for i in range(count)])
            break
        near, far, both = (
            lax.ppermute(value, axis, [(i, i ^ mask) for i in range(count)])
            for mask in (step, step * 2, step * 3)
        )
        value = (value + near) + (far + both)
        step *= 4
    return value


def split_sum(value, axes):
    sizes = [lax.axis_size(axis) for axis in axes]
    total = math.prod(sizes)
    if total & (total - 1) or sizes[0] % 2:
        return lax.psum(value, axes)
    half = value.shape[0] // 2
    side = lax.axis_index(axes[0]) % 2
    keep = lax.dynamic_slice_in_dim(value, side * half, half)
    send = lax.dynamic_slice_in_dim(value, (1 - side) * half, half)
    index_axes = tuple(reversed(axes))
    partner = [(i, i ^ 1) for i in range(total)]
    keep = keep + lax.ppermute(send, index_axes, partner)
    bits = [1 << b for b in range(1, total.bit_length() - 1)]
    while len(bits) >= 2:
        near, far, both = (
            lax.ppermute(keep, index_axes, [(i, i ^ mask) for i in range(total)])
            for mask in (bits[0], bits[1], bits[0] | bits[1])
        )
        keep = (keep + near) + (far + both)
        bits = bits[2:]
    for bit in bits:
        keep = keep + lax.ppermute(keep, index_axes, [(i, i ^ bit) for i in range(total)])
    other = lax.ppermute(keep, index_axes, partner)
    return lax.dynamic_update_slice_in_dim(
        jnp.concatenate((other, other)), keep, side * half, axis=0
    )


def row_count(shape):
    return -(-math.prod(shape) // 128)


def pack_rows(parts):
    blocks = []
    for part in parts:
        size = math.prod(part.shape)
        rows = row_count(part.shape)
        flat = part.reshape(-1)
        if rows * 128 != size:
            flat = jnp.pad(flat, (0, rows * 128 - size))
        blocks.append(flat.reshape(rows, 128))
    total = sum(block.shape[0] for block in blocks)
    blocks.append(jnp.zeros((-(-total // 16) * 16 - total, 128), jnp.float32))
    return jnp.concatenate(blocks)


def unpack_rows(packed, shapes):
    parts = []
    start = 0
    for shape in shapes:
        size = math.prod(shape)
        rows = row_count(shape)
        block = packed[start : start + rows]
        if rows * 128 != size:
            block = block.reshape(-1)[:size]
        parts.append(block.reshape(shape))
        start += rows
    return parts


def silu_slope(value):
    sigma = jax.nn.sigmoid(value)
    return sigma * (1.0 + value * (1.0 - sigma))


def wrap_columns(field):
    return jnp.concatenate((field[..., -1:], field, field[..., :1]), axis=-1)


def spread_local(weight, extended_field, shape):
    windows = jnp.stack(
        [
            extended_field[:, 2 - tap_x : 2 - tap_x + shape[1], 2 - tap_z : 2 - tap_z + shape[2]]
            for tap_x in range(3)
            for tap_z in range(3)
        ]
    )
    per_shift = jnp.einsum(
        "toxzy,tsoi->sixzy",
        windows,
        weight.reshape(9, 3, shape[0], shape[0]),
        preferred_element_type=jnp.float32,
    )
    return sum(jnp.roll(per_shift[tap_y], tap_y - 1, axis=3) for tap_y in range(3))


def taps_from_halo(extended_grad, inputs):
    shape = inputs.shape
    windows = jnp.stack(
        [
            extended_grad[:, 2 - tap_x : 2 - tap_x + shape[1], 2 - tap_z : 2 - tap_z + shape[2]]
            for tap_x in range(3)
            for tap_z in range(3)
        ]
    )
    rolled = jnp.stack([jnp.roll(inputs, 1 - tap_y, axis=3) for tap_y in range(3)])
    taps = jnp.einsum(
        "toxzy,sixzy->tsoi", windows, rolled, preferred_element_type=jnp.float32
    )
    return taps.reshape(3, 3, 3, extended_grad.shape[0], shape[0])


def per_device(
    features, pre_first, pre_second, w_first, w_second, w_out, b_out, y_target, k_target
):
    count_sky = lax.axis_size("sky")
    count_los = lax.axis_size("los")
    depth_all = pre_first.shape[2] * count_los
    norm_factor = 1.0 / math.sqrt(features.shape[1] * count_sky * features.shape[3] * depth_all)
    shape = features.shape
    first_wide = pre_first.astype(jnp.float32)
    second_wide = pre_second.astype(jnp.float32)
    hidden_second = jax.nn.silu(second_wide).astype(jnp.bfloat16)
    heads_raw = jnp.einsum(
        "oi,ixzy->oxzy", w_out, hidden_second, preferred_element_type=jnp.float32
    )
    heads_raw = heads_raw + b_out[:, None, None, None]
    pressure = jax.nn.softplus(heads_raw[0])
    density = jax.nn.softplus(heads_raw[1])
    velocity = heads_raw[2]
    y_part = jnp.sum(pressure, axis=1) / depth_all
    k_part = -jnp.sum(density * velocity, axis=1) / depth_all
    y_map, k_map = quad_sum(jnp.stack((y_part, k_part)), "los")
    y_resid = y_map - y_target
    k_resid = k_map - k_target
    y_resid = y_resid[:, None, :]
    k_resid = k_resid[:, None, :]
    head_grad = jnp.stack(
        (
            y_resid * jax.nn.sigmoid(heads_raw[0]),
            -k_resid * velocity * jax.nn.sigmoid(heads_raw[1]),
            -k_resid * density,
        )
    ).astype(jnp.bfloat16)
    grad_out = (
        jnp.einsum("oxzy,ixzy->oi", head_grad, hidden_second, preferred_element_type=jnp.float32)
        * norm_factor
    )
    grad_bias = jnp.sum(head_grad.astype(jnp.float32), axis=(1, 2, 3)) * norm_factor
    back_second = jnp.einsum("oi,oxzy->ixzy", w_out, head_grad, preferred_element_type=jnp.float32)
    grad_second_pre = (back_second * silu_slope(second_wide)).astype(jnp.bfloat16)
    second_padded = extended(grad_second_pre, (("sky", 1), ("los", 2)), 1)
    back_first = spread_local(w_second, second_padded, shape)
    grad_first_pre = (back_first * silu_slope(first_wide)).astype(jnp.bfloat16)
    first_padded = extended(grad_first_pre, (("sky", 1), ("los", 2)), 1)
    grad_features = spread_local(w_first, first_padded, shape).astype(jnp.bfloat16)
    hidden_first = jax.nn.silu(first_wide).astype(jnp.bfloat16)
    grad_second = taps_from_halo(second_padded, hidden_first)
    grad_first = taps_from_halo(first_padded, features)
    reduced = (grad_first * norm_factor, grad_second * norm_factor, grad_out, grad_bias)
    reduced_shapes = [part.shape for part in reduced]
    grad_first, grad_second, grad_out, grad_bias = unpack_rows(
        split_sum(pack_rows(reduced), ("los", "sky")), reduced_shapes
    )
    return (grad_features, grad_first, grad_second, grad_out, grad_bias)


def solution(mesh):
    in_specs = (
        P(None, "sky", "los", None),
        P(None, "sky", "los", None),
        P(None, "sky", "los", None),
        P(),
        P(),
        P(),
        P(),
        P("sky", None),
        P("sky", None),
    )
    out_specs = (P(None, "sky", "los", None), P(), P(), P(), P())
    return jax.shard_map(
        per_device, mesh=mesh, in_specs=in_specs, out_specs=out_specs, check_vma=False
    )
```

```python
import math

import jax
import jax.numpy as jnp
from jax import lax
from jax.sharding import PartitionSpec as P


def extended(block, sides, width):
    for axis, dim in sides:
        count = lax.axis_size(axis)
        forward = [(i, i + 1) for i in range(count - 1)]
        forward.append((count - 1, 0))
        backward = [(target, source) for source, target in forward]
        low = lax.ppermute(
            lax.slice_in_dim(block, block.shape[dim] - width, None, axis=dim), axis, forward
        )
        high = lax.ppermute(lax.slice_in_dim(block, 0, width, axis=dim), axis, backward)
        block = jnp.concatenate([low, block, high], axis=dim)
    return block


def butterfly_sum(value, axes, skip=0):
    for axis in axes:
        count = lax.axis_size(axis)
        if count & (count - 1):
            value = lax.psum(value, axis)
            continue
        step = 2 if skip and axis == axes[0] else 1
        while step < count:
            pairs = [(i, i ^ step) for i in range(count)]
            value = value + lax.ppermute(value, axis, pairs)
            step *= 2
    return value


def quad_sum(value, axis):
    count = lax.axis_size(axis)
    if count & (count - 1):
        return lax.psum(value, axis)
    step = 1
    while step < count:
        if step * 2 >= count:
            value = value + lax.ppermute(value, axis, [(i, i ^ step) for i in range(count)])
            break
        near, far, both = (
            lax.ppermute(value, axis, [(i, i ^ mask) for i in range(count)])
            for mask in (step, step * 2, step * 3)
        )
        value = (value + near) + (far + both)
        step *= 4
    return value


def split_sum(value, axes):
    sizes = [lax.axis_size(axis) for axis in axes]
    total = math.prod(sizes)
    if total & (total - 1) or sizes[0] % 2:
        return lax.psum(value, axes)
    half = value.shape[0] // 2
    side = lax.axis_index(axes[0]) % 2
    keep = lax.dynamic_slice_in_dim(value, side * half, half)
    send = lax.dynamic_slice_in_dim(value, (1 - side) * half, half)
    index_axes = tuple(reversed(axes))
    partner = [(i, i ^ 1) for i in range(total)]
    keep = keep + lax.ppermute(send, index_axes, partner)
    bits = [1 << b for b in range(1, total.bit_length() - 1)]
    if len(bits) >= 8:
        near, far, both = (
            lax.ppermute(keep, index_axes, [(i, i ^ mask) for i in range(total)])
            for mask in (bits[0], bits[1], bits[0] | bits[1])
        )
        keep = (keep + near) + (far + both)
        bits = bits[2:]
    for bit in bits:
        keep = keep + lax.ppermute(keep, index_axes, [(i, i ^ bit) for i in range(total)])
    other = lax.ppermute(keep, index_axes, partner)
    return lax.dynamic_update_slice_in_dim(
        jnp.concatenate((other, other)), keep, side * half, axis=0
    )


def row_count(shape):
    return -(-math.prod(shape) // 128)


def pack_rows(parts):
    blocks = []
    for part in parts:
        size = math.prod(part.shape)
        rows = row_count(part.shape)
        flat = part.reshape(-1)
        if rows * 128 != size:
            flat = jnp.pad(flat, (0, rows * 128 - size))
        blocks.append(flat.reshape(rows, 128))
    total = sum(block.shape[0] for block in blocks)
    blocks.append(jnp.zeros((-(-total // 16) * 16 - total, 128), jnp.float32))
    return jnp.concatenate(blocks)


def unpack_rows(packed, shapes):
    parts = []
    start = 0
    for shape in shapes:
        size = math.prod(shape)
        rows = row_count(shape)
        block = packed[start : start + rows]
        if rows * 128 != size:
            block = block.reshape(-1)[:size]
        parts.append(block.reshape(shape))
        start += rows
    return parts


def silu_slope(value):
    sigma = jax.nn.sigmoid(value)
    return sigma * (1.0 + value * (1.0 - sigma))


def wrap_columns(field):
    return jnp.concatenate((field[..., -1:], field, field[..., :1]), axis=-1)


def spread_local(weight, extended_field, shape):
    windows = jnp.stack(
        [
            extended_field[:, 2 - tap_x : 2 - tap_x + shape[1], 2 - tap_z : 2 - tap_z + shape[2]]
            for tap_x in range(3)
            for tap_z in range(3)
        ]
    )
    per_shift = jnp.einsum(
        "toxzy,tsoi->sixzy",
        windows,
        weight.reshape(9, 3, shape[0], shape[0]),
        preferred_element_type=jnp.float32,
    )
    return sum(jnp.roll(per_shift[tap_y], tap_y - 1, axis=3) for tap_y in range(3))


def taps_from_halo(extended_grad, inputs):
    shape = inputs.shape
    windows = jnp.stack(
        [
            extended_grad[:, 2 - tap_x : 2 - tap_x + shape[1], 2 - tap_z : 2 - tap_z + shape[2]]
            for tap_x in range(3)
            for tap_z in range(3)
        ]
    )
    rolled = jnp.stack([jnp.roll(inputs, 1 - tap_y, axis=3) for tap_y in range(3)])
    taps = jnp.einsum(
        "toxzy,sixzy->tsoi", windows, rolled, preferred_element_type=jnp.float32
    )
    return taps.reshape(3, 3, 3, extended_grad.shape[0], shape[0])


def per_device(
    features, pre_first, pre_second, w_first, w_second, w_out, b_out, y_target, k_target
):
    count_sky = lax.axis_size("sky")
    count_los = lax.axis_size("los")
    depth_all = pre_first.shape[2] * count_los
    norm_factor = 1.0 / math.sqrt(features.shape[1] * count_sky * features.shape[3] * depth_all)
    shape = features.shape
    first_wide = pre_first.astype(jnp.float32)
    second_wide = pre_second.astype(jnp.float32)
    hidden_second = jax.nn.silu(second_wide).astype(jnp.bfloat16)
    heads_raw = jnp.einsum(
        "oi,ixzy->oxzy", w_out, hidden_second, preferred_element_type=jnp.float32
    )
    heads_raw = heads_raw + b_out[:, None, None, None]
    pressure = jax.nn.softplus(heads_raw[0])
    density = jax.nn.softplus(heads_raw[1])
    velocity = heads_raw[2]
    y_part = jnp.sum(pressure, axis=1) / depth_all
    k_part = -jnp.sum(density * velocity, axis=1) / depth_all
    y_map, k_map = quad_sum(jnp.stack((y_part, k_part)), "los")
    y_resid = y_map - y_target
    k_resid = k_map - k_target
    y_resid = y_resid[:, None, :]
    k_resid = k_resid[:, None, :]
    head_grad = jnp.stack(
        (
            y_resid * jax.nn.sigmoid(heads_raw[0]),
            -k_resid * velocity * jax.nn.sigmoid(heads_raw[1]),
            -k_resid * density,
        )
    ).astype(jnp.bfloat16)
    grad_out = (
        jnp.einsum("oxzy,ixzy->oi", head_grad, hidden_second, preferred_element_type=jnp.float32)
        * norm_factor
    )
    grad_bias = jnp.sum(head_grad.astype(jnp.float32), axis=(1, 2, 3)) * norm_factor
    back_second = jnp.einsum("oi,oxzy->ixzy", w_out, head_grad, preferred_element_type=jnp.float32)
    grad_second_pre = (back_second * silu_slope(second_wide)).astype(jnp.bfloat16)
    second_padded = extended(grad_second_pre, (("sky", 1), ("los", 2)), 1)
    back_first = spread_local(w_second, second_padded, shape)
    grad_first_pre = (back_first * silu_slope(first_wide)).astype(jnp.bfloat16)
    first_padded = extended(grad_first_pre, (("sky", 1), ("los", 2)), 1)
    grad_features = spread_local(w_first, first_padded, shape).astype(jnp.bfloat16)
    hidden_first = jax.nn.silu(first_wide).astype(jnp.bfloat16)
    grad_second = taps_from_halo(second_padded, hidden_first)
    grad_first = taps_from_halo(first_padded, features)
    reduced = (grad_first * norm_factor, grad_second * norm_factor, grad_out, grad_bias)
    reduced_shapes = [part.shape for part in reduced]
    grad_first, grad_second, grad_out, grad_bias = unpack_rows(
        split_sum(pack_rows(reduced), ("los", "sky")), reduced_shapes
    )
    return (grad_features, grad_first, grad_second, grad_out, grad_bias)


def solution(mesh):
    in_specs = (
        P(None, "sky", "los", None),
        P(None, "sky", "los", None),
        P(None, "sky", "los", None),
        P(),
        P(),
        P(),
        P(),
        P("sky", None),
        P("sky", None),
    )
    out_specs = (P(None, "sky", "los", None), P(), P(), P(), P())
    return jax.shard_map(
        per_device, mesh=mesh, in_specs=in_specs, out_specs=out_specs, check_vma=False
    )
```

```python
import math

import jax
import jax.numpy as jnp
from jax import lax
from jax.sharding import PartitionSpec as P


def extended(block, sides, width):
    for axis, dim in sides:
        count = lax.axis_size(axis)
        forward = [(i, i + 1) for i in range(count - 1)]
        forward.append((count - 1, 0))
        backward = [(target, source) for source, target in forward]
        low = lax.ppermute(
            lax.slice_in_dim(block, block.shape[dim] - width, None, axis=dim), axis, forward
        )
        high = lax.ppermute(lax.slice_in_dim(block, 0, width, axis=dim), axis, backward)
        block = jnp.concatenate([low, block, high], axis=dim)
    return block


def butterfly_sum(value, axes, skip=0):
    for axis in axes:
        count = lax.axis_size(axis)
        if count & (count - 1):
            value = lax.psum(value, axis)
            continue
        step = 2 if skip and axis == axes[0] else 1
        while step < count:
            pairs = [(i, i ^ step) for i in range(count)]
            value = value + lax.ppermute(value, axis, pairs)
            step *= 2
    return value


def quad_sum(value, axis):
    count = lax.axis_size(axis)
    if count & (count - 1):
        return lax.psum(value, axis)
    step = 1
    while step < count:
        if step * 2 >= count:
            value = value + lax.ppermute(value, axis, [(i, i ^ step) for i in range(count)])
            break
        near, far, both = (
            lax.ppermute(value, axis, [(i, i ^ mask) for i in range(count)])
            for mask in (step, step * 2, step * 3)
        )
        value = (value + near) + (far + both)
        step *= 4
    return value


def split_sum(value, axes):
    sizes = [lax.axis_size(axis) for axis in axes]
    total = math.prod(sizes)
    if total & (total - 1) or sizes[0] % 2:
        return lax.psum(value, axes)
    half = value.shape[0] // 2
    side = lax.axis_index(axes[0]) % 2
    keep = lax.dynamic_slice_in_dim(value, side * half, half)
    send = lax.dynamic_slice_in_dim(value, (1 - side) * half, half)
    index_axes = tuple(reversed(axes))
    partner = [(i, i ^ 1) for i in range(total)]
    keep = keep + lax.ppermute(send, index_axes, partner)
    bits = [1 << b for b in range(1, total.bit_length() - 1)]
    if len(bits) >= 2:
        near, far, both = (
            lax.ppermute(keep, index_axes, [(i, i ^ mask) for i in range(total)])
            for mask in (bits[0], bits[1], bits[0] | bits[1])
        )
        keep = (keep + near) + (far + both)
        bits = bits[2:]
    for bit in bits:
        keep = keep + lax.ppermute(keep, index_axes, [(i, i ^ bit) for i in range(total)])
    other = lax.ppermute(keep, index_axes, partner)
    return lax.dynamic_update_slice_in_dim(
        jnp.concatenate((other, other)), keep, side * half, axis=0
    )


def row_count(shape):
    return -(-math.prod(shape) // 128)


def pack_rows(parts):
    blocks = []
    for part in parts:
        size = math.prod(part.shape)
        rows = row_count(part.shape)
        flat = part.reshape(-1)
        if rows * 128 != size:
            flat = jnp.pad(flat, (0, rows * 128 - size))
        blocks.append(flat.reshape(rows, 128))
    total = sum(block.shape[0] for block in blocks)
    blocks.append(jnp.zeros((-(-total // 16) * 16 - total, 128), jnp.float32))
    return jnp.concatenate(blocks)


def unpack_rows(packed, shapes):
    parts = []
    start = 0
    for shape in shapes:
        size = math.prod(shape)
        rows = row_count(shape)
        block = packed[start : start + rows]
        if rows * 128 != size:
            block = block.reshape(-1)[:size]
        parts.append(block.reshape(shape))
        start += rows
    return parts


def silu_slope(value):
    sigma = jax.nn.sigmoid(value)
    return sigma * (1.0 + value * (1.0 - sigma))


def wrap_columns(field):
    return jnp.concatenate((field[..., -1:], field, field[..., :1]), axis=-1)


def spread_local(weight, extended_field, shape):
    windows = jnp.stack(
        [
            extended_field[:, 2 - tap_x : 2 - tap_x + shape[1], 2 - tap_z : 2 - tap_z + shape[2]]
            for tap_x in range(3)
            for tap_z in range(3)
        ]
    )
    per_shift = jnp.einsum(
        "toxzy,tsoi->sixzy",
        windows,
        weight.reshape(9, 3, shape[0], shape[0]),
        preferred_element_type=jnp.float32,
    )
    return sum(jnp.roll(per_shift[tap_y], tap_y - 1, axis=3) for tap_y in range(3))


def taps_from_halo(extended_grad, inputs):
    shape = inputs.shape
    windows = jnp.stack(
        [
            extended_grad[:, 2 - tap_x : 2 - tap_x + shape[1], 2 - tap_z : 2 - tap_z + shape[2]]
            for tap_x in range(3)
            for tap_z in range(3)
        ]
    )
    rolled = jnp.stack([jnp.roll(inputs, 1 - tap_y, axis=3) for tap_y in range(3)])
    taps = jnp.einsum(
        "toxzy,sixzy->tsoi", windows, rolled, preferred_element_type=jnp.float32
    )
    return taps.reshape(3, 3, 3, extended_grad.shape[0], shape[0])


def per_device(
    features, pre_first, pre_second, w_first, w_second, w_out, b_out, y_target, k_target
):
    count_sky = lax.axis_size("sky")
    count_los = lax.axis_size("los")
    depth_all = pre_first.shape[2] * count_los
    norm_factor = 1.0 / math.sqrt(features.shape[1] * count_sky * features.shape[3] * depth_all)
    shape = features.shape
    first_wide = pre_first.astype(jnp.float32)
    second_wide = pre_second.astype(jnp.float32)
    hidden_second = jax.nn.silu(second_wide).astype(jnp.bfloat16)
    heads_raw = jnp.einsum(
        "oi,ixzy->oxzy", w_out, hidden_second, preferred_element_type=jnp.float32
    )
    heads_raw = heads_raw + b_out[:, None, None, None]
    pressure = jax.nn.softplus(heads_raw[0])
    density = jax.nn.softplus(heads_raw[1])
    velocity = heads_raw[2]
    y_part = jnp.sum(pressure, axis=1) / depth_all
    k_part = -jnp.sum(density * velocity, axis=1) / depth_all
    y_map, k_map = quad_sum(jnp.stack((y_part, k_part)), "los")
    y_resid = y_map - y_target
    k_resid = k_map - k_target
    y_resid = y_resid[:, None, :]
    k_resid = k_resid[:, None, :]
    head_grad = jnp.stack(
        (
            y_resid * jax.nn.sigmoid(heads_raw[0]),
            -k_resid * velocity * jax.nn.sigmoid(heads_raw[1]),
            -k_resid * density,
        )
    ).astype(jnp.bfloat16)
    grad_out = (
        jnp.einsum("oxzy,ixzy->oi", head_grad, hidden_second, preferred_element_type=jnp.float32)
        * norm_factor
    )
    grad_bias = jnp.sum(head_grad.astype(jnp.float32), axis=(1, 2, 3)) * norm_factor
    back_second = jnp.einsum("oi,oxzy->ixzy", w_out, head_grad, preferred_element_type=jnp.float32)
    grad_second_pre = (back_second * silu_slope(second_wide)).astype(jnp.bfloat16)
    second_padded = extended(grad_second_pre, (("los", 2), ("sky", 1)), 1)
    back_first = spread_local(w_second, second_padded, shape)
    grad_first_pre = (back_first * silu_slope(first_wide)).astype(jnp.bfloat16)
    first_padded = extended(grad_first_pre, (("sky", 1), ("los", 2)), 1)
    grad_features = spread_local(w_first, first_padded, shape).astype(jnp.bfloat16)
    hidden_first = jax.nn.silu(first_wide).astype(jnp.bfloat16)
    grad_second = taps_from_halo(second_padded, hidden_first)
    grad_first = taps_from_halo(first_padded, features)
    reduced = (grad_first * norm_factor, grad_second * norm_factor, grad_out, grad_bias)
    reduced_shapes = [part.shape for part in reduced]
    grad_first, grad_second, grad_out, grad_bias = unpack_rows(
        split_sum(pack_rows(reduced), ("los", "sky")), reduced_shapes
    )
    return (grad_features, grad_first, grad_second, grad_out, grad_bias)


def solution(mesh):
    in_specs = (
        P(None, "sky", "los", None),
        P(None, "sky", "los", None),
        P(None, "sky", "los", None),
        P(),
        P(),
        P(),
        P(),
        P("sky", None),
        P("sky", None),
    )
    out_specs = (P(None, "sky", "los", None), P(), P(), P(), P())
    return jax.shard_map(
        per_device, mesh=mesh, in_specs=in_specs, out_specs=out_specs, check_vma=False
    )
```
